32 devices in a mesh: groups: 2 (over y), lon: 4 (over z), tm: 2 (over x), branch: 2 (over core).
Axes of the slice: x: 2, y: 2, z: 4, core: 2. Of those that a mesh axis runs over, the one named last changes fastest.
Arguments:
- queries: bfloat16 [4, 2, 32, 32, 1536], P(('groups', 'branch'), 'tm', None, 'lon'), parts along dimension 0
- keys: bfloat16 [4, 2, 32, 32, 1536], P(('groups', 'branch'), 'tm', None, 'lon'), parts along dimension 0
- values: bfloat16 [4, 2, 32, 32, 1536], P(('groups', 'branch'), 'tm', None, 'lon'), parts along dimension 0, may hold values from -6 to 6
- window_map: int32 [32, 15], P(('groups', 'lon')), parts along dimension 0, may hold values from 0 to 1, as said below
- frame_valid: int32 [4, 32], P('groups', 'lon'), parts along dimension 0, may hold values 0 or 1
Outputs:
- guided: bfloat16 [4, 32, 32, 1536], P(('groups', 'tm'), None, 'lon', 'branch'), parts along dimension 0
The draws below stay inside these ranges and needn't reach their ends.
There are 2 independent parts, one for each index of `groups`. The reference program is written for one: setup_inputs(seed, part) draws one part's arguments, and reference() takes and returns one part's arrays. A program takes and returns all parts, laid end to end along the dimension named above; each array names one. Nothing has to cross between parts.
Inputs may be any that keep to these rules, and one draw needn't show every extreme that they name: `window_map`: entries are 0 or 1; entry 7 of every row, the query block itself, is 1.
All inputs are finite; a program needn't handle non-finite values. No bound on the sum of `frame_valid` on one device may be relied on, other than what follows from the above.
Results may differ from the reference program's by a relative error of at most 0.008.
Values may be sent and summed in bfloat16 or wider, within the bound.
No kernel may reach another device: no remote copies, remote signals or barrier semaphores. Data moves between devices by JAX's collectives and lax.ppermute only.
A program may use at most 64 MiB of HBM per device.

```python
import jax
import jax.numpy as jnp
from jax import lax

HEADS = 12
DH = 128
D = 1536
F = 2
LAT = 32
W = 32
BLK = 2
REACH = 7
WIN = 15
NBLK = 16


def draw_queries(key, part):
    base = jax.random.normal(jax.random.fold_in(key, 1), (2, F, LAT, W, HEADS * DH), jnp.float32)
    return base.astype(jnp.bfloat16)


def draw_keys(key, part):
    base = jax.random.normal(jax.random.fold_in(key, 2), (2, F, LAT, W, HEADS * DH), jnp.float32)
    return base.astype(jnp.bfloat16)


def draw_window_map(key, part):
    levels = jax.random.randint(jax.random.fold_in(key, 11), (NBLK, 1), 1, 10)
    rolls = jax.random.randint(jax.random.fold_in(key, 12), (NBLK, WIN), 0, 10)
    entries = (rolls < levels).astype(jnp.int32)
    center = (jnp.arange(WIN) == REACH)[None, :]
    return jnp.where(center, 1, entries).astype(jnp.int32)


def touch_ends(values, key, low, high):
    spot = [jax.random.randint(jax.random.fold_in(key, axis), (), 0, length) for axis, length in enumerate(values.shape)]
    widest = values.shape.index(max(values.shape))
    neighbour = spot[:widest] + [(spot[widest] + 1) % values.shape[widest]] + spot[widest + 1:]
    return values.at[tuple(spot)].set(low).at[tuple(neighbour)].set(high)


def steps_of(rng, extent, shards, least, largest):
    def one(dim, shards_of):
        draws = jax.random.uniform(jax.random.fold_in(jax.random.fold_in(rng, 6), dim), (shards_of,), jnp.float32, least / len(shards), largest / len(shards))
        return jnp.repeat(jnp.exp(draws), extent[dim] // shards_of).reshape((-1,) + (1,) * (len(extent) - dim - 1))

    factor_of = one(*shards[0])
    for cut in shards[1:]:
        factor_of = factor_of * one(*cut)
    return factor_of


def noise(rng, shape, width, limit, pieces=(), kind=jnp.bfloat16):
    values = width * jax.random.normal(rng, shape, jnp.float32)
    if pieces:
        values = values * steps_of(rng, shape, pieces, -0.22, 0.18)
    return jnp.clip(values, -limit, limit).astype(kind)


def setup_inputs(seed: int = 0, part: int = 0) -> dict:
    seeds = jax.random.split(jax.random.key(seed), 6)
    part_splits = jax.random.split(jax.random.fold_in(seeds[5], part), 6)
    queries = draw_queries(jax.random.fold_in(jax.random.fold_in(seeds[5], part), 71), part)
    keys = draw_keys(jax.random.fold_in(jax.random.fold_in(seeds[5], part), 71), part)
    values = noise(part_splits[2], (2, F, LAT, W, D), 1.0, 6.0, ((0, 2), (1, 2), (3, 4)))
    window_map = draw_window_map(jax.random.fold_in(jax.random.fold_in(seeds[5], part), 71), part)
    frame_valid = touch_ends((jax.random.randint(part_splits[4], (F, W), 0, 3) < 2).astype(jnp.int32), jax.random.fold_in(part_splits[4], 1), 0, 1)
    return dict(queries=queries, keys=keys, values=values, window_map=window_map, frame_valid=frame_valid)


guidance_weight = 5.0
masked_score = -1e30


def softmax_terms(scores, allowed):
    limited = jnp.where(allowed, scores, masked_score)
    maxima = jnp.max(limited, axis=-1, keepdims=True)
    weights = jnp.exp(limited - maxima)
    totals = jnp.sum(weights, axis=-1)
    rounded = lax.optimization_barrier(weights.astype(jnp.bfloat16)).astype(jnp.float32)
    return rounded, totals


def reference(queries, keys, values, window_map, frame_valid):
    scale = DH ** -0.5
    span = WIN * BLK
    offsets = jnp.arange(span, dtype=jnp.int32) - REACH * BLK
    slot_of = jnp.arange(span, dtype=jnp.int32) // BLK
    shaped_q = queries.reshape(2, F, LAT, W, HEADS, DH)
    shaped_k = keys.reshape(2, F, LAT, W, HEADS, DH)
    shaped_v = values.reshape(2, F, LAT, W, HEADS, DH)

    def spatial_block(block):
        start = (block * BLK).astype(jnp.int32)
        query_block = lax.dynamic_slice_in_dim(shaped_q, start, BLK, 3).astype(jnp.float32)
        query_block = query_block.reshape(2, F, LAT * BLK, HEADS, DH)
        columns = ((start + offsets) % W).astype(jnp.int32)
        key_block = jnp.take(shaped_k, columns, axis=3).astype(jnp.float32).reshape(2, F, LAT * span, HEADS, DH)
        value_block = jnp.take(shaped_v, columns, axis=3).astype(jnp.float32).reshape(2, F, LAT * span, HEADS, DH)
        active = jnp.tile(window_map[block][slot_of] > 0, LAT)
        scores = jnp.einsum('bfqhd,bfkhd->bfhqk', query_block, key_block) * scale
        weights, totals = softmax_terms(scores, active)
        result = jnp.einsum('bfhqk,bfkhd->bfqhd', weights, value_block)
        result = result / jnp.transpose(totals, (0, 1, 3, 2))[..., None]
        return result.reshape(2, F, LAT, BLK, D)

    blocks = lax.map(spatial_block, jnp.arange(NBLK, dtype=jnp.int32))
    spatial = jnp.transpose(blocks, (1, 2, 3, 0, 4, 5)).reshape(2, F, LAT, W, D)

    frame_ids = jnp.arange(F, dtype=jnp.int32)
    same_frame = frame_ids[:, None] == frame_ids[None, :]
    valid_tokens = jnp.tile(frame_valid, (1, LAT))
    allowed = (jnp.transpose(valid_tokens)[:, None, :] > 0) | same_frame[None]

    def temporal_branch(branch_index):
        query_rows = queries[branch_index].reshape(F, LAT * W, HEADS, DH).astype(jnp.float32)
        key_rows = keys[branch_index].reshape(F, LAT * W, HEADS, DH).astype(jnp.float32)
        value_rows = values[branch_index].reshape(F, LAT * W, HEADS, DH).astype(jnp.float32)
        scores = jnp.einsum('fthd,gthd->thfg', query_rows, key_rows) * scale
        weights, totals = softmax_terms(scores, allowed[:, None])
        result = jnp.einsum('thfg,gthd->fthd', weights, value_rows)
        result = result / jnp.transpose(totals, (2, 0, 1))[..., None]
        return result.reshape(F, LAT, W, D)

    temporal = lax.map(temporal_branch, jnp.arange(2, dtype=jnp.int32))
    temporal = lax.optimization_barrier(temporal.astype(jnp.bfloat16)).astype(jnp.float32)
    mixed = lax.optimization_barrier((spatial + temporal).astype(jnp.bfloat16)).astype(jnp.float32)
    conditional = mixed[0]
    unconditional = mixed[1]
    return (unconditional + guidance_weight * (conditional - unconditional)).astype(jnp.bfloat16)
```

```python
import functools

import jax
import jax.numpy as jnp
from jax import lax
from jax.experimental import pallas as pl
from jax.sharding import PartitionSpec as P

DH = 128
BLK = 2
REACH = 7
WIN = 15


guidance_weight = 5.0
masked_score = -1e30


def shifted(value, axis, by):
    count = lax.axis_size(axis)
    return lax.ppermute(value, axis, [(i, (i + by) % count) for i in range(count)])


def from_partner(value, axis, bit):
    return lax.ppermute(value, axis, [(i, i ^ 1 << bit) for i in range(lax.axis_size(axis))])


def spatial_kernel(q_ref, k_ref, v_ref, m_ref, o_ref, *, scale):
    scores = (
        lax.dot_general(
            q_ref[...], k_ref[...], (((1,), (1,)), ((), ())), preferred_element_type=jnp.float32
        )
        * scale
    )
    limited = jnp.where(m_ref[...] > 0, scores, masked_score)
    maxima = jnp.max(limited, axis=-1, keepdims=True)
    weights = jnp.exp(limited - maxima)
    totals = jnp.sum(weights, axis=-1, keepdims=True)
    result = jnp.dot(
        weights.astype(jnp.bfloat16), v_ref[...], preferred_element_type=jnp.float32
    )
    o_ref[...] = result / totals


def spatial_attention(query_flat, key_value_flat, mask, scale):
    frames, query_count, model_width = query_flat.shape
    key_count = key_value_flat.shape[2]
    head_count = model_width // DH
    return pl.pallas_call(
        functools.partial(spatial_kernel, scale=scale),
        grid=(frames, head_count),
        in_specs=[
            pl.BlockSpec((None, query_count, DH), lambda f, h: (f, 0, h)),
            pl.BlockSpec((None, None, key_count, DH), lambda f, h: (0, f, 0, h)),
            pl.BlockSpec((None, None, key_count, DH), lambda f, h: (1, f, 0, h)),
            pl.BlockSpec((query_count, key_count), lambda f, h: (0, 0)),
        ],
        out_specs=pl.BlockSpec((None, query_count, DH), lambda f, h: (f, 0, h)),
        out_shape=jax.ShapeDtypeStruct((frames, query_count, model_width), jnp.float32),
        cost_estimate=pl.CostEstimate(
            flops=4 * frames * query_count * key_count * model_width,
            transcendentals=frames * head_count * query_count * key_count,
            bytes_accessed=2 * model_width * frames * (query_count + 2 * key_count)
            + 4 * frames * query_count * model_width,
        ),
    )(query_flat, key_value_flat, key_value_flat, mask)


def temporal_attention(own_q, all_k, all_v, valid, own_ids, all_ids, scale):
    q32 = own_q.astype(jnp.float32)
    k32 = all_k.astype(jnp.float32)
    scores = jnp.sum(q32[:, None] * k32[None], axis=-1) * scale
    same = own_ids[:, None] == all_ids[None, :]
    allowed = (valid[None, :, :] > 0) | same[:, :, None]
    limited = jnp.where(allowed[..., None], scores, masked_score)
    maxima = jnp.max(limited, axis=1, keepdims=True)
    weights = jnp.exp(limited - maxima)
    totals = jnp.sum(weights, axis=1)
    rounded = weights.astype(jnp.bfloat16).astype(jnp.float32)
    result = jnp.sum(rounded[..., None] * all_v.astype(jnp.float32)[None], axis=1)
    return (result / totals[..., None]).astype(jnp.bfloat16)


def local(queries, keys, values, window_map, frame_valid):
    own_q = queries[0]
    own_k = keys[0]
    own_v = values[0]
    frames, lat_rows, columns, model_width = own_q.shape
    head_count = model_width // DH
    scale = DH ** (-0.5)
    reach_cols = REACH * BLK
    lon_count = lax.axis_size("lon")
    total_cols = lon_count * columns
    ext_count = columns + 2 * reach_cols
    key_value = jnp.stack([own_k, own_v])
    column_ids = jnp.arange(columns, dtype=jnp.int32)
    per_column_map = jnp.repeat(window_map, BLK, axis=0)
    if ext_count >= total_cols and WIN * BLK <= total_cols:
        extended = lax.all_gather(key_value, "lon", axis=3, tiled=True)
        key_cols = total_cols
        block_count = total_cols // BLK
        query_blocks = (lax.axis_index("lon") * columns + column_ids) // BLK
        key_blocks = jnp.arange(total_cols, dtype=jnp.int32) // BLK
        slots = (key_blocks[None, :] - query_blocks[:, None] + REACH) % block_count
    else:
        reach_devices = -(-reach_cols // columns)
        left_parts, right_parts = [], []
        for step_by in range(1, reach_devices + 1):
            need = min(columns, reach_cols - (step_by - 1) * columns)
            left_parts.insert(0, shifted(key_value[:, :, :, columns - need :, :], "lon", step_by))
            right_parts.append(shifted(key_value[:, :, :, :need, :], "lon", -step_by))
        extended = jnp.concatenate(left_parts + [key_value] + right_parts, axis=3)
        key_cols = ext_count
        ext_ids = jnp.arange(ext_count, dtype=jnp.int32)
        slots = ext_ids[None, :] // BLK - column_ids[:, None] // BLK
    picks = slots[:, :, None] == jnp.arange(WIN, dtype=jnp.int32)[None, None, :]
    active = jnp.any(picks & (per_column_map[:, None, :] > 0), axis=-1)
    mask = jnp.broadcast_to(
        active[None, :, None, :].astype(jnp.float32), (lat_rows, columns, lat_rows, key_cols)
    ).reshape(lat_rows * columns, lat_rows * key_cols)
    query_flat = own_q.reshape(frames, lat_rows * columns, model_width)
    key_value_flat = extended.reshape(2, frames, lat_rows * key_cols, model_width)
    spatial = spatial_attention(query_flat, key_value_flat, mask, scale)

    token_count = lat_rows * columns
    tm_count = lax.axis_size("tm")
    tm_index = lax.axis_index("tm")
    key_value_rows = key_value.reshape(2, frames, token_count, head_count, DH)
    pieces = [key_value_rows]
    for step_by in range(1, tm_count):
        pieces.append(shifted(key_value_rows, "tm", step_by))
    gathered = jnp.concatenate(pieces, axis=1)
    piece_ids = jnp.arange(tm_count * frames, dtype=jnp.int32)
    frame_ids = ((tm_index - piece_ids // frames) % tm_count) * frames + piece_ids % frames
    valid_tokens = jnp.take(jnp.tile(frame_valid, (1, lat_rows)), frame_ids, axis=0)
    temporal = temporal_attention(
        own_q.reshape(frames, token_count, head_count, DH),
        gathered[0],
        gathered[1],
        valid_tokens,
        frame_ids[:frames],
        frame_ids,
        scale,
    )
    temporal = temporal.reshape(frames, token_count, model_width).astype(jnp.float32)
    mixed = (
        (spatial + temporal).astype(jnp.bfloat16).reshape(frames, lat_rows, columns, model_width)
    )
    half_width = model_width // 2
    branch_index = lax.axis_index("branch")
    own_half = lax.dynamic_slice_in_dim(mixed, branch_index * half_width, half_width, 3)
    other_half = lax.dynamic_slice_in_dim(mixed, (1 - branch_index) * half_width, half_width, 3)
    partner = from_partner(other_half, "branch", 0)
    is_conditional = branch_index == 0
    conditional = jnp.where(is_conditional, own_half, partner).astype(jnp.float32)
    unconditional = jnp.where(is_conditional, partner, own_half).astype(jnp.float32)
    return (unconditional + guidance_weight * (conditional - unconditional)).astype(jnp.bfloat16)


def solution(mesh):
    in_specs = (
        P(("groups", "branch"), "tm", None, "lon", None),
        P(("groups", "branch"), "tm", None, "lon", None),
        P(("groups", "branch"), "tm", None, "lon", None),
        P(("groups", "lon"), None),
        P("groups", "lon"),
    )
    out_specs = P(("groups", "tm"), None, "lon", "branch")
    return jax.shard_map(local, mesh=mesh, in_specs=in_specs, out_specs=out_specs, check_vma=False)
```

```python
import functools

import jax
import jax.numpy as jnp
from jax import lax
from jax.experimental import pallas as pl
from jax.sharding import PartitionSpec as P

DH = 128
BLK = 2
REACH = 7
WIN = 15


guidance_weight = 5.0
masked_score = -1e30


def shifted(value, axis, by):
    count = lax.axis_size(axis)
    return lax.ppermute(value, axis, [(i, (i + by) % count) for i in range(count)])


def from_partner(value, axis, bit):
    return lax.ppermute(value, axis, [(i, i ^ 1 << bit) for i in range(lax.axis_size(axis))])


def spatial_kernel(q_ref, k_ref, v_ref, m_ref, o_ref, *, scale):
    scores = (
        lax.dot_general(
            q_ref[...], k_ref[...], (((1,), (1,)), ((), ())), preferred_element_type=jnp.float32
        )
        * scale
    )
    limited = jnp.where(m_ref[...] > 0, scores, masked_score)
    maxima = jnp.max(limited, axis=-1, keepdims=True)
    weights = jnp.exp(limited - maxima)
    totals = jnp.sum(weights, axis=-1, keepdims=True)
    result = jnp.dot(
        weights.astype(jnp.bfloat16), v_ref[...], preferred_element_type=jnp.float32
    )
    o_ref[...] = result / totals


def spatial_attention(query_flat, key_value_flat, mask, scale):
    frames, query_count, model_width = query_flat.shape
    key_count = key_value_flat.shape[2]
    head_count = model_width // DH
    return pl.pallas_call(
        functools.partial(spatial_kernel, scale=scale),
        grid=(frames, head_count),
        in_specs=[
            pl.BlockSpec((None, query_count, DH), lambda f, h: (f, 0, h)),
            pl.BlockSpec((None, None, key_count, DH), lambda f, h: (0, f, 0, h)),
            pl.BlockSpec((None, None, key_count, DH), lambda f, h: (1, f, 0, h)),
            pl.BlockSpec((query_count, key_count), lambda f, h: (0, 0)),
        ],
        out_specs=pl.BlockSpec((None, query_count, DH), lambda f, h: (f, 0, h)),
        out_shape=jax.ShapeDtypeStruct((frames, query_count, model_width), jnp.float32),
        cost_estimate=pl.CostEstimate(
            flops=4 * frames * query_count * key_count * model_width,
            transcendentals=frames * head_count * query_count * key_count,
            bytes_accessed=2 * model_width * frames * (query_count + 2 * key_count)
            + 4 * frames * query_count * model_width,
        ),
    )(query_flat, key_value_flat, key_value_flat, mask)


def temporal_attention(own_q, all_k, all_v, valid, own_ids, all_ids, scale):
    q32 = own_q.astype(jnp.float32)
    k32 = all_k.astype(jnp.float32)
    scores = jnp.sum(q32[:, None] * k32[None], axis=-1) * scale
    same = own_ids[:, None] == all_ids[None, :]
    allowed = (valid[None, :, :] > 0) | same[:, :, None]
    limited = jnp.where(allowed[..., None], scores, masked_score)
    maxima = jnp.max(limited, axis=1, keepdims=True)
    weights = jnp.exp(limited - maxima)
    totals = jnp.sum(weights, axis=1)
    rounded = lax.reduce_precision(weights, exponent_bits=8, mantissa_bits=7)
    result = jnp.sum(rounded[..., None] * all_v.astype(jnp.float32)[None], axis=1)
    result = lax.reduce_precision(result / totals[..., None], exponent_bits=8, mantissa_bits=7)
    return result.astype(jnp.bfloat16)


def line_gather(block, axis):
    count = lax.axis_size(axis)
    index = lax.axis_index(axis)
    left, right = {}, {}
    from_left = from_right = block
    for step in range(1, count):
        from_left = lax.ppermute(from_left, axis, [(s, s + 1) for s in range(step - 1, count - 1)])
        from_right = lax.ppermute(
            from_right, axis, [(s, s - 1) for s in range(1, count - step + 1)]
        )
        left[step], right[step] = from_left, from_right
    relative = [block]
    for d in range(1, count):
        relative.append(jnp.where(index + d < count, right[d], left[count - d]))
    return relative


def local(queries, keys, values, window_map, frame_valid):
    own_q = queries[0]
    own_k = keys[0]
    own_v = values[0]
    frames, lat_rows, columns, model_width = own_q.shape
    head_count = model_width // DH
    scale = DH ** (-0.5)
    reach_cols = REACH * BLK
    lon_count = lax.axis_size("lon")
    total_cols = lon_count * columns
    ext_count = columns + 2 * reach_cols
    key_value = jnp.stack([own_k, own_v])
    column_ids = jnp.arange(columns, dtype=jnp.int32)
    per_column_map = jnp.repeat(window_map, BLK, axis=0)
    if ext_count >= total_cols and WIN * BLK <= total_cols:
        extended = jnp.concatenate(line_gather(key_value, "lon"), axis=3)
        key_cols = total_cols
        block_count = total_cols // BLK
        first_col = lax.axis_index("lon") * columns
        query_blocks = (first_col + column_ids) // BLK
        key_blocks = ((first_col + jnp.arange(total_cols, dtype=jnp.int32)) % total_cols) // BLK
        slots = (key_blocks[None, :] - query_blocks[:, None] + REACH) % block_count
    else:
        reach_devices = -(-reach_cols // columns)
        left_parts, right_parts = [], []
        for step_by in range(1, reach_devices + 1):
            need = min(columns, reach_cols - (step_by - 1) * columns)
            left_parts.insert(0, shifted(key_value[:, :, :, columns - need :, :], "lon", step_by))
            right_parts.append(shifted(key_value[:, :, :, :need, :], "lon", -step_by))
        extended = jnp.concatenate(left_parts + [key_value] + right_parts, axis=3)
        key_cols = ext_count
        ext_ids = jnp.arange(ext_count, dtype=jnp.int32)
        slots = ext_ids[None, :] // BLK - column_ids[:, None] // BLK
    picks = slots[:, :, None] == jnp.arange(WIN, dtype=jnp.int32)[None, None, :]
    active = jnp.any(picks & (per_column_map[:, None, :] > 0), axis=-1)
    mask = jnp.broadcast_to(
        active[None, :, None, :].astype(jnp.float32), (lat_rows, columns, lat_rows, key_cols)
    ).reshape(lat_rows * columns, lat_rows * key_cols)
    query_flat = own_q.reshape(frames, lat_rows * columns, model_width)
    key_value_flat = extended.reshape(2, frames, lat_rows * key_cols, model_width)
    spatial = spatial_attention(query_flat, key_value_flat, mask, scale)

    token_count = lat_rows * columns
    tm_count = lax.axis_size("tm")
    tm_index = lax.axis_index("tm")
    key_value_rows = key_value.reshape(2, frames, token_count, head_count, DH)
    pieces = [key_value_rows]
    for step_by in range(1, tm_count):
        pieces.append(shifted(key_value_rows, "tm", step_by))
    gathered = jnp.concatenate(pieces, axis=1)
    piece_ids = jnp.arange(tm_count * frames, dtype=jnp.int32)
    frame_ids = ((tm_index - piece_ids // frames) % tm_count) * frames + piece_ids % frames
    valid_tokens = jnp.take(jnp.tile(frame_valid, (1, lat_rows)), frame_ids, axis=0)
    temporal = temporal_attention(
        own_q.reshape(frames, token_count, head_count, DH),
        gathered[0],
        gathered[1],
        valid_tokens,
        frame_ids[:frames],
        frame_ids,
        scale,
    )
    temporal = temporal.reshape(frames, token_count, model_width).astype(jnp.float32)
    mixed = (
        (spatial + temporal).astype(jnp.bfloat16).reshape(frames, lat_rows, columns, model_width)
    )
    half_width = model_width // 2
    branch_index = lax.axis_index("branch")
    own_half = lax.dynamic_slice_in_dim(mixed, branch_index * half_width, half_width, 3)
    other_half = lax.dynamic_slice_in_dim(mixed, (1 - branch_index) * half_width, half_width, 3)
    partner = from_partner(other_half, "branch", 0)
    is_conditional = branch_index == 0
    conditional = jnp.where(is_conditional, own_half, partner).astype(jnp.float32)
    unconditional = jnp.where(is_conditional, partner, own_half).astype(jnp.float32)
    return (unconditional + guidance_weight * (conditional - unconditional)).astype(jnp.bfloat16)


def solution(mesh):
    in_specs = (
        P(("groups", "branch"), "tm", None, "lon", None),
        P(("groups", "branch"), "tm", None, "lon", None),
        P(("groups", "branch"), "tm", None, "lon", None),
        P(("groups", "lon"), None),
        P("groups", "lon"),
    )
    out_specs = P(("groups", "tm"), None, "lon", "branch")
    return jax.shard_map(local, mesh=mesh, in_specs=in_specs, out_specs=out_specs, check_vma=False)
```

```python
import functools

import jax
import jax.numpy as jnp
from jax import lax
from jax.experimental import pallas as pl
from jax.sharding import PartitionSpec as P

DH = 128
BLK = 2
REACH = 7
WIN = 15


guidance_weight = 5.0
masked_score = -1e30


def shifted(value, axis, by):
    count = lax.axis_size(axis)
    return lax.ppermute(value, axis, [(i, (i + by) % count) for i in range(count)])


def from_partner(value, axis, bit):
    return lax.ppermute(value, axis, [(i, i ^ 1 << bit) for i in range(lax.axis_size(axis))])


def spatial_kernel(q_ref, k_ref, v_ref, m_ref, o_ref, lse_ref, *, scale):
    scores = (
        lax.dot_general(
            q_ref[...], k_ref[...], (((1,), (1,)), ((), ())), preferred_element_type=jnp.float32
        )
        * scale
    )
    limited = jnp.where(m_ref[...] > 0, scores, masked_score)
    maxima = jnp.max(limited, axis=-1, keepdims=True)
    weights = jnp.exp(limited - maxima)
    totals = jnp.sum(weights, axis=-1, keepdims=True)
    result = jnp.dot(
        weights.astype(jnp.bfloat16), v_ref[...], preferred_element_type=jnp.float32
    )
    o_ref[...] = result / totals
    lse_ref[...] = maxima + jnp.log(totals)


def spatial_attention(query_flat, key_value_flat, mask, scale):
    frames, query_count, model_width = query_flat.shape
    key_count = key_value_flat.shape[2]
    head_count = model_width // DH
    return pl.pallas_call(
        functools.partial(spatial_kernel, scale=scale),
        grid=(frames, head_count),
        in_specs=[
            pl.BlockSpec((None, query_count, DH), lambda f, h: (f, 0, h)),
            pl.BlockSpec((None, None, key_count, DH), lambda f, h: (0, f, 0, h)),
            pl.BlockSpec((None, None, key_count, DH), lambda f, h: (1, f, 0, h)),
            pl.BlockSpec((query_count, key_count), lambda f, h: (0, 0)),
        ],
        out_specs=[
            pl.BlockSpec((None, query_count, DH), lambda f, h: (f, 0, h)),
            pl.BlockSpec((None, None, query_count, 1), lambda f, h: (f, h, 0, 0)),
        ],
        out_shape=[
            jax.ShapeDtypeStruct((frames, query_count, model_width), jnp.float32),
            jax.ShapeDtypeStruct((frames, head_count, query_count, 1), jnp.float32),
        ],
        cost_estimate=pl.CostEstimate(
            flops=4 * frames * query_count * key_count * model_width,
            transcendentals=frames * head_count * query_count * key_count,
            bytes_accessed=2 * model_width * frames * (query_count + 2 * key_count)
            + 4 * frames * query_count * model_width,
        ),
    )(query_flat, key_value_flat, key_value_flat, mask)


def temporal_attention(own_q, all_k, all_v, valid, own_ids, all_ids, scale):
    q32 = own_q.astype(jnp.float32)
    k32 = all_k.astype(jnp.float32)
    scores = jnp.sum(q32[:, None] * k32[None], axis=-1) * scale
    same = own_ids[:, None] == all_ids[None, :]
    allowed = (valid[None, :, :] > 0) | same[:, :, None]
    limited = jnp.where(allowed[..., None], scores, masked_score)
    maxima = jnp.max(limited, axis=1, keepdims=True)
    weights = jnp.exp(limited - maxima)
    totals = jnp.sum(weights, axis=1)
    rounded = lax.reduce_precision(weights, exponent_bits=8, mantissa_bits=7)
    result = jnp.sum(rounded[..., None] * all_v.astype(jnp.float32)[None], axis=1)
    result = lax.reduce_precision(result / totals[..., None], exponent_bits=8, mantissa_bits=7)
    return result.astype(jnp.bfloat16)


def line_gather(block, axis):
    count = lax.axis_size(axis)
    index = lax.axis_index(axis)
    left, right = {}, {}
    from_left = from_right = block
    for step in range(1, count):
        from_left = lax.ppermute(from_left, axis, [(s, s + 1) for s in range(step - 1, count - 1)])
        from_right = lax.ppermute(
            from_right, axis, [(s, s - 1) for s in range(1, count - step + 1)]
        )
        left[step], right[step] = from_left, from_right
    relative = [block]
    for d in range(1, count):
        relative.append(jnp.where(index + d < count, right[d], left[count - d]))
    return relative


def window_mask(query_cols, key_cols, column_map, total_cols, lat_rows):
    block_count = total_cols // BLK
    slots = (key_cols[None, :] // BLK - query_cols[:, None] // BLK + REACH) % block_count
    picks = slots[:, :, None] == jnp.arange(WIN, dtype=jnp.int32)[None, None, :]
    return jnp.any(picks & (column_map[:, None, :] > 0), axis=-1)


def expand_mask(active, lat_rows):
    query_cols, key_cols = active.shape
    return jnp.broadcast_to(
        active[None, :, None, :].astype(jnp.float32), (lat_rows, query_cols, lat_rows, key_cols)
    ).reshape(lat_rows * query_cols, lat_rows * key_cols)


def flat_keys(blocks):
    joined = jnp.concatenate(blocks, axis=3)
    two, frames, lat_rows, cols, model_width = joined.shape
    return joined.reshape(two, frames, lat_rows * cols, model_width)


def spatial_line_of_four(own_q, key_value, window_map, scale):
    frames, lat_rows, columns, model_width = own_q.shape
    head_count = model_width // DH
    count = 4
    total_cols = count * columns
    index = lax.axis_index("lon")
    is_middle = (index >= 1) & (index <= count - 2)
    from_left = lax.ppermute(key_value, "lon", [(0, 1), (1, 2), (2, 3)])
    from_right = lax.ppermute(key_value, "lon", [(3, 2), (2, 1), (1, 0)])
    onward = jnp.where(index == 1, from_left, from_right)
    two_away = lax.ppermute(onward, "lon", [(1, 2), (2, 1)])
    held_q, _ = lax.optimization_barrier((own_q, from_left))
    guest_q = lax.ppermute(held_q, "lon", [(0, 1), (3, 2)])
    guest_map = lax.ppermute(window_map, "lon", [(0, 1), (3, 2)])

    column_ids = jnp.arange(columns, dtype=jnp.int32)
    guest_device = jnp.where(index == 1, 0, count - 1)
    near_block = jnp.where(index == 1, index + 1, index - 1)
    far_block = (index + 2) % count
    guest_key_cols = jnp.concatenate([near_block * columns + column_ids, far_block * columns + column_ids])
    guest_active = window_mask(
        guest_device * columns + column_ids,
        guest_key_cols,
        jnp.repeat(guest_map, BLK, axis=0),
        total_cols,
        lat_rows,
    ) & is_middle
    guest_near = jnp.where(index == 1, from_right, from_left)
    guest_out, guest_lse = spatial_attention(
        guest_q.reshape(frames, lat_rows * columns, model_width),
        flat_keys([guest_near, two_away]),
        expand_mask(guest_active, lat_rows),
        scale,
    )
    returned, returned_lse = lax.ppermute(
        (guest_out.astype(jnp.bfloat16), guest_lse.reshape(frames, head_count, lat_rows * columns)),
        "lon",
        [(1, 0), (2, 3)],
    )

    rel_cols = ((index - 1) * columns + jnp.arange(total_cols, dtype=jnp.int32)) % total_cols
    rel_block = jnp.arange(total_cols, dtype=jnp.int32) // columns
    block_valid = jnp.stack([index >= 1, index >= 0, index <= count - 2, is_middle])
    own_active = window_mask(
        index * columns + column_ids, rel_cols, jnp.repeat(window_map, BLK, axis=0), total_cols, lat_rows
    ) & block_valid[rel_block][None, :]
    own_out, own_lse = spatial_attention(
        own_q.reshape(frames, lat_rows * columns, model_width),
        flat_keys([from_left, key_value, from_right, two_away]),
        expand_mask(own_active, lat_rows),
        scale,
    )
    own_lse = jnp.transpose(own_lse[..., 0], (0, 2, 1))[..., None]
    returned_lse = jnp.transpose(returned_lse, (0, 2, 1))[..., None]
    top = jnp.maximum(own_lse, returned_lse)
    own_weight = jnp.exp(own_lse - top)
    returned_weight = jnp.exp(returned_lse - top)
    shape4 = (frames, lat_rows * columns, head_count, DH)
    joined = (
        own_weight * own_out.reshape(shape4)
        + returned_weight * returned.astype(jnp.float32).reshape(shape4)
    ) / (own_weight + returned_weight)
    spatial = jnp.where(is_middle, own_out, joined.reshape(own_out.shape))
    return spatial


def local(queries, keys, values, window_map, frame_valid):
    own_q = queries[0]
    own_k = keys[0]
    own_v = values[0]
    frames, lat_rows, columns, model_width = own_q.shape
    head_count = model_width // DH
    scale = DH ** (-0.5)
    reach_cols = REACH * BLK
    lon_count = lax.axis_size("lon")
    total_cols = lon_count * columns
    ext_count = columns + 2 * reach_cols
    key_value = jnp.stack([own_k, own_v])
    column_ids = jnp.arange(columns, dtype=jnp.int32)
    per_column_map = jnp.repeat(window_map, BLK, axis=0)
    full_ring = ext_count >= total_cols and WIN * BLK <= total_cols
    if full_ring and lon_count == 4:
        spatial = spatial_line_of_four(own_q, key_value, window_map, scale)
    else:
        if full_ring:
            extended = jnp.concatenate(line_gather(key_value, "lon"), axis=3)
            key_cols = total_cols
            block_count = total_cols // BLK
            first_col = lax.axis_index("lon") * columns
            query_blocks = (first_col + column_ids) // BLK
            key_blocks = ((first_col + jnp.arange(total_cols, dtype=jnp.int32)) % total_cols) // BLK
            slots = (key_blocks[None, :] - query_blocks[:, None] + REACH) % block_count
        else:
            reach_devices = -(-reach_cols // columns)
            left_parts, right_parts = [], []
            for step_by in range(1, reach_devices + 1):
                need = min(columns, reach_cols - (step_by - 1) * columns)
                left_parts.insert(
                    0, shifted(key_value[:, :, :, columns - need :, :], "lon", step_by)
                )
                right_parts.append(shifted(key_value[:, :, :, :need, :], "lon", -step_by))
            extended = jnp.concatenate(left_parts + [key_value] + right_parts, axis=3)
            key_cols = ext_count
            ext_ids = jnp.arange(ext_count, dtype=jnp.int32)
            slots = ext_ids[None, :] // BLK - column_ids[:, None] // BLK
        picks = slots[:, :, None] == jnp.arange(WIN, dtype=jnp.int32)[None, None, :]
        active = jnp.any(picks & (per_column_map[:, None, :] > 0), axis=-1)
        query_flat = own_q.reshape(frames, lat_rows * columns, model_width)
        key_value_flat = extended.reshape(2, frames, lat_rows * key_cols, model_width)
        spatial = spatial_attention(query_flat, key_value_flat, expand_mask(active, lat_rows), scale)[0]

    token_count = lat_rows * columns
    tm_count = lax.axis_size("tm")
    tm_index = lax.axis_index("tm")
    key_value_rows = key_value.reshape(2, frames, token_count, head_count, DH)
    pieces = [key_value_rows]
    for step_by in range(1, tm_count):
        pieces.append(shifted(key_value_rows, "tm", step_by))
    gathered = jnp.concatenate(pieces, axis=1)
    piece_ids = jnp.arange(tm_count * frames, dtype=jnp.int32)
    frame_ids = ((tm_index - piece_ids // frames) % tm_count) * frames + piece_ids % frames
    valid_tokens = jnp.take(jnp.tile(frame_valid, (1, lat_rows)), frame_ids, axis=0)
    temporal = temporal_attention(
        own_q.reshape(frames, token_count, head_count, DH),
        gathered[0],
        gathered[1],
        valid_tokens,
        frame_ids[:frames],
        frame_ids,
        scale,
    )
    temporal = temporal.reshape(frames, token_count, model_width).astype(jnp.float32)
    mixed = (
        (spatial + temporal).astype(jnp.bfloat16).reshape(frames, lat_rows, columns, model_width)
    )
    half_width = model_width // 2
    branch_index = lax.axis_index("branch")
    own_half = lax.dynamic_slice_in_dim(mixed, branch_index * half_width, half_width, 3)
    other_half = lax.dynamic_slice_in_dim(mixed, (1 - branch_index) * half_width, half_width, 3)
    partner = from_partner(other_half, "branch", 0)
    is_conditional = branch_index == 0
    conditional = jnp.where(is_conditional, own_half, partner).astype(jnp.float32)
    unconditional = jnp.where(is_conditional, partner, own_half).astype(jnp.float32)
    return (unconditional + guidance_weight * (conditional - unconditional)).astype(jnp.bfloat16)


def solution(mesh):
    in_specs = (
        P(("groups", "branch"), "tm", None, "lon", None),
        P(("groups", "branch"), "tm", None, "lon", None),
        P(("groups", "branch"), "tm", None, "lon", None),
        P(("groups", "lon"), None),
        P("groups", "lon"),
    )
    out_specs = P(("groups", "tm"), None, "lon", "branch")
    return jax.shard_map(local, mesh=mesh, in_specs=in_specs, out_specs=out_specs, check_vma=False)
```

```python
import functools

import jax
import jax.numpy as jnp
from jax import lax
from jax.experimental import pallas as pl
from jax.sharding import PartitionSpec as P

DH = 128
BLK = 2
REACH = 7
WIN = 15


guidance_weight = 5.0
masked_score = -1e30


def shifted(value, axis, by):
    count = lax.axis_size(axis)
    return lax.ppermute(value, axis, [(i, (i + by) % count) for i in range(count)])


def from_partner(value, axis, bit):
    return lax.ppermute(value, axis, [(i, i ^ 1 << bit) for i in range(lax.axis_size(axis))])


def group_width(model_width):
    for width in (512, 384, 256):
        if model_width % width == 0:
            return width
    return DH


def spatial_kernel(q_ref, k_ref, v_ref, m_ref, o_ref, lse_ref, *, scale):
    allowed = m_ref[...] > 0
    for head in range(q_ref.shape[-1] // DH):
        lanes = slice(head * DH, (head + 1) * DH)
        scores = (
            lax.dot_general(
                q_ref[:, lanes],
                k_ref[:, lanes],
                (((1,), (1,)), ((), ())),
                preferred_element_type=jnp.float32,
            )
            * scale
        )
        limited = jnp.where(allowed, scores, masked_score)
        maxima = jnp.max(limited, axis=-1, keepdims=True)
        weights = jnp.exp(limited - maxima)
        totals = jnp.sum(weights, axis=-1, keepdims=True)
        result = jnp.dot(
            weights.astype(jnp.bfloat16), v_ref[:, lanes], preferred_element_type=jnp.float32
        )
        o_ref[:, lanes] = result / totals
        lse_ref[:, head : head + 1] = maxima + jnp.log(totals)


def spatial_attention(query_flat, key_value_flat, mask, scale):
    frames, query_count, model_width = query_flat.shape
    key_count = key_value_flat.shape[2]
    head_count = model_width // DH
    width = group_width(model_width)
    groups = model_width // width
    return pl.pallas_call(
        functools.partial(spatial_kernel, scale=scale),
        grid=(frames, groups),
        in_specs=[
            pl.BlockSpec((None, query_count, width), lambda f, g: (f, 0, g)),
            pl.BlockSpec((None, None, key_count, width), lambda f, g: (0, f, 0, g)),
            pl.BlockSpec((None, None, key_count, width), lambda f, g: (1, f, 0, g)),
            pl.BlockSpec((query_count, key_count), lambda f, g: (0, 0)),
        ],
        out_specs=[
            pl.BlockSpec((None, query_count, width), lambda f, g: (f, 0, g)),
            pl.BlockSpec((None, None, query_count, width // DH), lambda f, g: (f, g, 0, 0)),
        ],
        out_shape=[
            jax.ShapeDtypeStruct((frames, query_count, model_width), jnp.float32),
            jax.ShapeDtypeStruct((frames, groups, query_count, width // DH), jnp.float32),
        ],
        cost_estimate=pl.CostEstimate(
            flops=4 * frames * query_count * key_count * model_width,
            transcendentals=frames * head_count * query_count * key_count,
            bytes_accessed=2 * model_width * frames * (query_count + 2 * key_count)
            + 4 * frames * query_count * model_width,
        ),
    )(query_flat, key_value_flat, key_value_flat, mask)


def combine_kernel(*refs):
    *parts, temporal_ref, mixed_ref = refs
    outs, lses = parts[0::2], parts[1::2]
    for head in range(mixed_ref.shape[-1] // DH):
        lanes = slice(head * DH, (head + 1) * DH)
        logs = [lse[:, head : head + 1] for lse in lses]
        top = functools.reduce(jnp.maximum, logs)
        weights = [jnp.exp(log - top) for log in logs]
        total = functools.reduce(jnp.add, weights)
        value = functools.reduce(
            jnp.add,
            [w * o[:, lanes].astype(jnp.float32) for w, o in zip(weights, outs)],
        )
        mixed_ref[:, lanes] = (value / total + temporal_ref[:, lanes].astype(jnp.float32)).astype(
            mixed_ref.dtype
        )


def combine_partials(partials, temporal):
    frames, query_count, model_width = temporal.shape
    width = group_width(model_width)
    groups = model_width // width
    big = pl.BlockSpec((None, query_count, width), lambda f, g: (f, 0, g))
    small = pl.BlockSpec((None, None, query_count, width // DH), lambda f, g: (f, g, 0, 0))
    operands = []
    for out, lse in partials:
        operands += [out, lse]
    return pl.pallas_call(
        combine_kernel,
        grid=(frames, groups),
        in_specs=[big, small] * len(partials) + [big],
        out_specs=big,
        out_shape=jax.ShapeDtypeStruct((frames, query_count, model_width), jnp.bfloat16),
    )(*operands, temporal)


def temporal_attention(own_q, all_k, all_v, valid, own_ids, all_ids, scale):
    q32 = own_q.astype(jnp.float32)
    k32 = all_k.astype(jnp.float32)
    scores = jnp.sum(q32[:, None] * k32[None], axis=-1) * scale
    same = own_ids[:, None] == all_ids[None, :]
    allowed = (valid[None, :, :] > 0) | same[:, :, None]
    limited = jnp.where(allowed[..., None], scores, masked_score)
    maxima = jnp.max(limited, axis=1, keepdims=True)
    weights = jnp.exp(limited - maxima)
    totals = jnp.sum(weights, axis=1)
    rounded = lax.reduce_precision(weights, exponent_bits=8, mantissa_bits=7)
    result = jnp.sum(rounded[..., None] * all_v.astype(jnp.float32)[None], axis=1)
    result = lax.reduce_precision(result / totals[..., None], exponent_bits=8, mantissa_bits=7)
    return result.astype(jnp.bfloat16)


def line_gather(block, axis):
    count = lax.axis_size(axis)
    index = lax.axis_index(axis)
    left, right = {}, {}
    from_left = from_right = block
    for step in range(1, count):
        from_left = lax.ppermute(from_left, axis, [(s, s + 1) for s in range(step - 1, count - 1)])
        from_right = lax.ppermute(
            from_right, axis, [(s, s - 1) for s in range(1, count - step + 1)]
        )
        left[step], right[step] = from_left, from_right
    relative = [block]
    for d in range(1, count):
        relative.append(jnp.where(index + d < count, right[d], left[count - d]))
    return relative


def window_mask(query_cols, key_cols, column_map, total_cols, lat_rows):
    block_count = total_cols // BLK
    slots = (key_cols[None, :] // BLK - query_cols[:, None] // BLK + REACH) % block_count
    picks = slots[:, :, None] == jnp.arange(WIN, dtype=jnp.int32)[None, None, :]
    return jnp.any(picks & (column_map[:, None, :] > 0), axis=-1)


def expand_mask(active, lat_rows):
    query_cols, key_cols = active.shape
    return jnp.broadcast_to(
        active[None, :, None, :].astype(jnp.float32), (lat_rows, query_cols, lat_rows, key_cols)
    ).reshape(lat_rows * query_cols, lat_rows * key_cols)


def flat_keys(blocks):
    joined = jnp.concatenate(blocks, axis=3)
    two, frames, lat_rows, cols, model_width = joined.shape
    return joined.reshape(two, frames, lat_rows * cols, model_width)


def spatial_line_of_four(own_q, key_value, window_map, scale):
    frames, lat_rows, columns, model_width = own_q.shape
    count = 4
    total_cols = count * columns
    index = lax.axis_index("lon")
    is_middle = (index >= 1) & (index <= count - 2)
    column_ids = jnp.arange(columns, dtype=jnp.int32)
    own_map = jnp.repeat(window_map, BLK, axis=0)
    own_cols = index * columns + column_ids
    query_flat = own_q.reshape(frames, lat_rows * columns, model_width)

    from_left = lax.ppermute(key_value, "lon", [(0, 1), (1, 2), (2, 3)])
    from_right = lax.ppermute(key_value, "lon", [(3, 2), (2, 1), (1, 0)])
    guest_map = lax.ppermute(window_map, "lon", [(0, 1), (3, 2)])

    near_cols = ((index - 1) * columns + jnp.arange(3 * columns, dtype=jnp.int32)) % total_cols
    near_valid = jnp.stack([index >= 1, index >= 0, index <= count - 2])
    near_active = window_mask(own_cols, near_cols, own_map, total_cols, lat_rows) & jnp.repeat(
        near_valid, columns
    )[None, :]
    near_part = spatial_attention(
        query_flat,
        flat_keys([from_left, key_value, from_right]),
        expand_mask(near_active, lat_rows),
        scale,
    )

    onward = jnp.where(index == 1, from_left, from_right)
    two_away = lax.ppermute(onward, "lon", [(1, 2), (2, 1)])
    held_q, _ = lax.optimization_barrier((own_q, from_left))
    guest_q = lax.ppermute(held_q, "lon", [(0, 1), (3, 2)])
    near_part, two_away, guest_q = lax.optimization_barrier((near_part, two_away, guest_q))

    guest_device = jnp.where(index == 1, 0, count - 1)
    near_block = jnp.where(index == 1, index + 1, index - 1)
    far_block = (index + 2) % count
    guest_key_cols = jnp.concatenate(
        [near_block * columns + column_ids, far_block * columns + column_ids]
    )
    guest_active = window_mask(
        guest_device * columns + column_ids,
        guest_key_cols,
        jnp.repeat(guest_map, BLK, axis=0),
        total_cols,
        lat_rows,
    ) & is_middle
    guest_near = jnp.where(index == 1, from_right, from_left)
    guest_out, guest_lse = spatial_attention(
        guest_q.reshape(frames, lat_rows * columns, model_width),
        flat_keys([guest_near, two_away]),
        expand_mask(guest_active, lat_rows),
        scale,
    )
    lse_shape = guest_lse.shape
    returned, returned_lse = lax.ppermute(
        (guest_out.astype(jnp.bfloat16), jnp.swapaxes(guest_lse, 2, 3)),
        "lon",
        [(1, 0), (2, 3)],
    )
    returned_lse = jnp.where(is_middle, masked_score, jnp.swapaxes(returned_lse, 2, 3))
    assert returned_lse.shape == lse_shape

    far_active = window_mask(
        own_cols, far_block * columns + column_ids, own_map, total_cols, lat_rows
    ) & is_middle
    far_part = spatial_attention(
        query_flat, flat_keys([two_away]), expand_mask(far_active, lat_rows), scale
    )
    return [near_part, far_part, (returned, returned_lse)]


def local(queries, keys, values, window_map, frame_valid):
    own_q = queries[0]
    own_k = keys[0]
    own_v = values[0]
    frames, lat_rows, columns, model_width = own_q.shape
    head_count = model_width // DH
    scale = DH ** (-0.5)
    reach_cols = REACH * BLK
    lon_count = lax.axis_size("lon")
    total_cols = lon_count * columns
    ext_count = columns + 2 * reach_cols
    key_value = jnp.stack([own_k, own_v])
    column_ids = jnp.arange(columns, dtype=jnp.int32)
    per_column_map = jnp.repeat(window_map, BLK, axis=0)
    full_ring = ext_count >= total_cols and WIN * BLK <= total_cols
    if full_ring and lon_count == 4:
        partials = spatial_line_of_four(own_q, key_value, window_map, scale)
    else:
        if full_ring:
            extended = jnp.concatenate(line_gather(key_value, "lon"), axis=3)
            key_cols = total_cols
            block_count = total_cols // BLK
            first_col = lax.axis_index("lon") * columns
            query_blocks = (first_col + column_ids) // BLK
            key_blocks = ((first_col + jnp.arange(total_cols, dtype=jnp.int32)) % total_cols) // BLK
            slots = (key_blocks[None, :] - query_blocks[:, None] + REACH) % block_count
        else:
            reach_devices = -(-reach_cols // columns)
            left_parts, right_parts = [], []
            for step_by in range(1, reach_devices + 1):
                need = min(columns, reach_cols - (step_by - 1) * columns)
                left_parts.insert(
                    0, shifted(key_value[:, :, :, columns - need :, :], "lon", step_by)
                )
                right_parts.append(shifted(key_value[:, :, :, :need, :], "lon", -step_by))
            extended = jnp.concatenate(left_parts + [key_value] + right_parts, axis=3)
            key_cols = ext_count
            ext_ids = jnp.arange(ext_count, dtype=jnp.int32)
            slots = ext_ids[None, :] // BLK - column_ids[:, None] // BLK
        picks = slots[:, :, None] == jnp.arange(WIN, dtype=jnp.int32)[None, None, :]
        active = jnp.any(picks & (per_column_map[:, None, :] > 0), axis=-1)
        query_flat = own_q.reshape(frames, lat_rows * columns, model_width)
        key_value_flat = extended.reshape(2, frames, lat_rows * key_cols, model_width)
        partials = [
            spatial_attention(query_flat, key_value_flat, expand_mask(active, lat_rows), scale)
        ]

    token_count = lat_rows * columns
    tm_count = lax.axis_size("tm")
    tm_index = lax.axis_index("tm")
    key_value_rows = key_value.reshape(2, frames, token_count, head_count, DH)
    pieces = [key_value_rows]
    for step_by in range(1, tm_count):
        pieces.append(shifted(key_value_rows, "tm", step_by))
    gathered = jnp.concatenate(pieces, axis=1)
    piece_ids = jnp.arange(tm_count * frames, dtype=jnp.int32)
    frame_ids = ((tm_index - piece_ids // frames) % tm_count) * frames + piece_ids % frames
    valid_tokens = jnp.take(jnp.tile(frame_valid, (1, lat_rows)), frame_ids, axis=0)
    temporal = temporal_attention(
        own_q.reshape(frames, token_count, head_count, DH),
        gathered[0],
        gathered[1],
        valid_tokens,
        frame_ids[:frames],
        frame_ids,
        scale,
    )
    temporal = temporal.reshape(frames, token_count, model_width)
    mixed = combine_partials(partials, temporal).reshape(frames, lat_rows, columns, model_width)
    half_width = model_width // 2
    branch_index = lax.axis_index("branch")
    own_half = lax.dynamic_slice_in_dim(mixed, branch_index * half_width, half_width, 3)
    other_half = lax.dynamic_slice_in_dim(mixed, (1 - branch_index) * half_width, half_width, 3)
    partner = from_partner(other_half, "branch", 0)
    is_conditional = branch_index == 0
    conditional = jnp.where(is_conditional, own_half, partner).astype(jnp.float32)
    unconditional = jnp.where(is_conditional, partner, own_half).astype(jnp.float32)
    return (unconditional + guidance_weight * (conditional - unconditional)).astype(jnp.bfloat16)


def solution(mesh):
    in_specs = (
        P(("groups", "branch"), "tm", None, "lon", None),
        P(("groups", "branch"), "tm", None, "lon", None),
        P(("groups", "branch"), "tm", None, "lon", None),
        P(("groups", "lon"), None),
        P("groups", "lon"),
    )
    out_specs = P(("groups", "tm"), None, "lon", "branch")
    return jax.shard_map(local, mesh=mesh, in_specs=in_specs, out_specs=out_specs, check_vma=False)
```

```python
import functools

import jax
import jax.numpy as jnp
from jax import lax
from jax.experimental import pallas as pl
from jax.sharding import PartitionSpec as P

DH = 128
BLK = 2
REACH = 7
WIN = 15


guidance_weight = 5.0
masked_score = -1e30


def shifted(value, axis, by):
    count = lax.axis_size(axis)
    return lax.ppermute(value, axis, [(i, (i + by) % count) for i in range(count)])


def from_partner(value, axis, bit):
    return lax.ppermute(value, axis, [(i, i ^ 1 << bit) for i in range(lax.axis_size(axis))])


def group_width(model_width):
    for width in (512, 384, 256):
        if model_width % width == 0:
            return width
    return DH


def spatial_kernel(q_ref, k_ref, v_ref, m_ref, o_ref, lse_ref, *, scale):
    allowed = m_ref[...] > 0
    for head in range(q_ref.shape[-1] // DH):
        lanes = slice(head * DH, (head + 1) * DH)
        scores = (
            lax.dot_general(
                q_ref[:, lanes],
                k_ref[:, lanes],
                (((1,), (1,)), ((), ())),
                preferred_element_type=jnp.float32,
            )
            * scale
        )
        limited = jnp.where(allowed, scores, masked_score)
        maxima = jnp.max(limited, axis=-1, keepdims=True)
        weights = jnp.exp(limited - maxima)
        totals = jnp.sum(weights, axis=-1, keepdims=True)
        result = jnp.dot(
            weights.astype(jnp.bfloat16), v_ref[:, lanes], preferred_element_type=jnp.float32
        )
        o_ref[:, lanes] = (result / totals).astype(o_ref.dtype)
        lse_ref[:, head : head + 1] = maxima + jnp.log(totals)


def spatial_attention(query_flat, key_value_flat, mask, scale, out_dtype=jnp.float32):
    frames, query_count, model_width = query_flat.shape
    key_count = key_value_flat.shape[2]
    head_count = model_width // DH
    width = group_width(model_width)
    groups = model_width // width
    return pl.pallas_call(
        functools.partial(spatial_kernel, scale=scale),
        grid=(frames, groups),
        in_specs=[
            pl.BlockSpec((None, query_count, width), lambda f, g: (f, 0, g)),
            pl.BlockSpec((None, None, key_count, width), lambda f, g: (0, f, 0, g)),
            pl.BlockSpec((None, None, key_count, width), lambda f, g: (1, f, 0, g)),
            pl.BlockSpec((query_count, key_count), lambda f, g: (0, 0)),
        ],
        out_specs=[
            pl.BlockSpec((None, query_count, width), lambda f, g: (f, 0, g)),
            pl.BlockSpec((None, None, query_count, width // DH), lambda f, g: (f, g, 0, 0)),
        ],
        out_shape=[
            jax.ShapeDtypeStruct((frames, query_count, model_width), out_dtype),
            jax.ShapeDtypeStruct((frames, groups, query_count, width // DH), jnp.float32),
        ],
        cost_estimate=pl.CostEstimate(
            flops=4 * frames * query_count * key_count * model_width,
            transcendentals=frames * head_count * query_count * key_count,
            bytes_accessed=2 * model_width * frames * (query_count + 2 * key_count)
            + 4 * frames * query_count * model_width,
        ),
    )(query_flat, key_value_flat, key_value_flat, mask)


def combine_kernel(*refs):
    *parts, temporal_ref, mixed_ref = refs
    outs, lses = parts[0::2], parts[1::2]
    for head in range(mixed_ref.shape[-1] // DH):
        lanes = slice(head * DH, (head + 1) * DH)
        logs = [lse[:, head : head + 1] for lse in lses]
        top = functools.reduce(jnp.maximum, logs)
        weights = [jnp.exp(log - top) for log in logs]
        total = functools.reduce(jnp.add, weights)
        value = functools.reduce(
            jnp.add,
            [w * o[:, lanes].astype(jnp.float32) for w, o in zip(weights, outs)],
        )
        mixed_ref[:, lanes] = (value / total + temporal_ref[:, lanes].astype(jnp.float32)).astype(
            mixed_ref.dtype
        )


def combine_partials(partials, temporal):
    frames, query_count, model_width = temporal.shape
    width = group_width(model_width)
    groups = model_width // width
    big = pl.BlockSpec((None, query_count, width), lambda f, g: (f, 0, g))
    small = pl.BlockSpec((None, None, query_count, width // DH), lambda f, g: (f, g, 0, 0))
    operands = []
    for out, lse in partials:
        operands += [out, lse]
    return pl.pallas_call(
        combine_kernel,
        grid=(frames, groups),
        in_specs=[big, small] * len(partials) + [big],
        out_specs=big,
        out_shape=jax.ShapeDtypeStruct((frames, query_count, model_width), jnp.bfloat16),
    )(*operands, temporal)


def temporal_attention(own_q, all_k, all_v, valid, own_ids, all_ids, scale):
    q32 = own_q.astype(jnp.float32)
    k32 = all_k.astype(jnp.float32)
    scores = jnp.sum(q32[:, None] * k32[None], axis=-1) * scale
    same = own_ids[:, None] == all_ids[None, :]
    allowed = (valid[None, :, :] > 0) | same[:, :, None]
    limited = jnp.where(allowed[..., None], scores, masked_score)
    maxima = jnp.max(limited, axis=1, keepdims=True)
    weights = jnp.exp(limited - maxima)
    totals = jnp.sum(weights, axis=1)
    rounded = lax.reduce_precision(weights, exponent_bits=8, mantissa_bits=7)
    result = jnp.sum(rounded[..., None] * all_v.astype(jnp.float32)[None], axis=1)
    result = lax.reduce_precision(result / totals[..., None], exponent_bits=8, mantissa_bits=7)
    return result.astype(jnp.bfloat16)


def line_gather(block, axis):
    count = lax.axis_size(axis)
    index = lax.axis_index(axis)
    left, right = {}, {}
    from_left = from_right = block
    for step in range(1, count):
        from_left = lax.ppermute(from_left, axis, [(s, s + 1) for s in range(step - 1, count - 1)])
        from_right = lax.ppermute(
            from_right, axis, [(s, s - 1) for s in range(1, count - step + 1)]
        )
        left[step], right[step] = from_left, from_right
    relative = [block]
    for d in range(1, count):
        relative.append(jnp.where(index + d < count, right[d], left[count - d]))
    return relative


def window_mask(query_cols, key_cols, column_map, total_cols, lat_rows):
    block_count = total_cols // BLK
    slots = (key_cols[None, :] // BLK - query_cols[:, None] // BLK + REACH) % block_count
    picks = slots[:, :, None] == jnp.arange(WIN, dtype=jnp.int32)[None, None, :]
    return jnp.any(picks & (column_map[:, None, :] > 0), axis=-1)


def expand_mask(active, lat_rows):
    query_cols, key_cols = active.shape
    return jnp.broadcast_to(
        active[None, :, None, :].astype(jnp.float32), (lat_rows, query_cols, lat_rows, key_cols)
    ).reshape(lat_rows * query_cols, lat_rows * key_cols)


def flat_keys(blocks):
    joined = jnp.concatenate(blocks, axis=3)
    two, frames, lat_rows, cols, model_width = joined.shape
    return joined.reshape(two, frames, lat_rows * cols, model_width)


def spatial_line_of_four(own_q, key_value, window_map, scale):
    frames, lat_rows, columns, model_width = own_q.shape
    count = 4
    total_cols = count * columns
    index = lax.axis_index("lon")
    is_middle = (index >= 1) & (index <= count - 2)
    column_ids = jnp.arange(columns, dtype=jnp.int32)
    own_map = jnp.repeat(window_map, BLK, axis=0)
    own_cols = index * columns + column_ids
    query_flat = own_q.reshape(frames, lat_rows * columns, model_width)

    from_left = lax.ppermute(key_value, "lon", [(0, 1), (1, 2), (2, 3)])
    from_right = lax.ppermute(key_value, "lon", [(3, 2), (2, 1), (1, 0)])
    guest_map = lax.ppermute(window_map, "lon", [(0, 1), (3, 2)])

    near_cols = ((index - 1) * columns + jnp.arange(3 * columns, dtype=jnp.int32)) % total_cols
    near_valid = jnp.stack([index >= 1, index >= 0, index <= count - 2])
    near_active = window_mask(own_cols, near_cols, own_map, total_cols, lat_rows) & jnp.repeat(
        near_valid, columns
    )[None, :]
    near_part = spatial_attention(
        query_flat,
        flat_keys([from_left, key_value, from_right]),
        expand_mask(near_active, lat_rows),
        scale,
    )

    two_away = jnp.where(
        index == 1,
        lax.ppermute(from_right, "lon", [(2, 1)]),
        lax.ppermute(from_left, "lon", [(1, 2)]),
    )
    held_q, _ = lax.optimization_barrier((own_q, from_left))
    guest_q = lax.ppermute(held_q, "lon", [(0, 1), (3, 2)])
    near_part, two_away, guest_q = lax.optimization_barrier((near_part, two_away, guest_q))

    guest_device = jnp.where(index == 1, 0, count - 1)
    near_block = jnp.where(index == 1, index + 1, index - 1)
    far_block = (index + 2) % count
    guest_key_cols = jnp.concatenate(
        [near_block * columns + column_ids, far_block * columns + column_ids]
    )
    guest_active = window_mask(
        guest_device * columns + column_ids,
        guest_key_cols,
        jnp.repeat(guest_map, BLK, axis=0),
        total_cols,
        lat_rows,
    ) & is_middle
    guest_near = jnp.where(index == 1, from_right, from_left)
    guest_out, guest_lse = spatial_attention(
        guest_q.reshape(frames, lat_rows * columns, model_width),
        flat_keys([guest_near, two_away]),
        expand_mask(guest_active, lat_rows),
        scale,
        jnp.bfloat16,
    )
    lse_shape = guest_lse.shape
    returned, returned_lse = lax.ppermute(
        (guest_out, jnp.swapaxes(guest_lse, 2, 3)),
        "lon",
        [(1, 0), (2, 3)],
    )
    returned_lse = jnp.where(is_middle, masked_score, jnp.swapaxes(returned_lse, 2, 3))
    assert returned_lse.shape == lse_shape

    far_active = window_mask(
        own_cols, far_block * columns + column_ids, own_map, total_cols, lat_rows
    ) & is_middle
    far_part = spatial_attention(
        query_flat, flat_keys([two_away]), expand_mask(far_active, lat_rows), scale
    )
    return [near_part, far_part, (returned, returned_lse)]


def local(queries, keys, values, window_map, frame_valid):
    own_q = queries[0]
    own_k = keys[0]
    own_v = values[0]
    frames, lat_rows, columns, model_width = own_q.shape
    head_count = model_width // DH
    scale = DH ** (-0.5)
    reach_cols = REACH * BLK
    lon_count = lax.axis_size("lon")
    total_cols = lon_count * columns
    ext_count = columns + 2 * reach_cols
    key_value = jnp.stack([own_k, own_v])
    column_ids = jnp.arange(columns, dtype=jnp.int32)
    per_column_map = jnp.repeat(window_map, BLK, axis=0)
    full_ring = ext_count >= total_cols and WIN * BLK <= total_cols
    if full_ring and lon_count == 4:
        partials = spatial_line_of_four(own_q, key_value, window_map, scale)
    else:
        if full_ring:
            extended = jnp.concatenate(line_gather(key_value, "lon"), axis=3)
            key_cols = total_cols
            block_count = total_cols // BLK
            first_col = lax.axis_index("lon") * columns
            query_blocks = (first_col + column_ids) // BLK
            key_blocks = ((first_col + jnp.arange(total_cols, dtype=jnp.int32)) % total_cols) // BLK
            slots = (key_blocks[None, :] - query_blocks[:, None] + REACH) % block_count
        else:
            reach_devices = -(-reach_cols // columns)
            left_parts, right_parts = [], []
            for step_by in range(1, reach_devices + 1):
                need = min(columns, reach_cols - (step_by - 1) * columns)
                left_parts.insert(
                    0, shifted(key_value[:, :, :, columns - need :, :], "lon", step_by)
                )
                right_parts.append(shifted(key_value[:, :, :, :need, :], "lon", -step_by))
            extended = jnp.concatenate(left_parts + [key_value] + right_parts, axis=3)
            key_cols = ext_count
            ext_ids = jnp.arange(ext_count, dtype=jnp.int32)
            slots = ext_ids[None, :] // BLK - column_ids[:, None] // BLK
        picks = slots[:, :, None] == jnp.arange(WIN, dtype=jnp.int32)[None, None, :]
        active = jnp.any(picks & (per_column_map[:, None, :] > 0), axis=-1)
        query_flat = own_q.reshape(frames, lat_rows * columns, model_width)
        key_value_flat = extended.reshape(2, frames, lat_rows * key_cols, model_width)
        partials = [
            spatial_attention(query_flat, key_value_flat, expand_mask(active, lat_rows), scale)
        ]

    token_count = lat_rows * columns
    tm_count = lax.axis_size("tm")
    tm_index = lax.axis_index("tm")
    key_value_rows = key_value.reshape(2, frames, token_count, head_count, DH)
    pieces = [key_value_rows]
    for step_by in range(1, tm_count):
        pieces.append(shifted(key_value_rows, "tm", step_by))
    gathered = jnp.concatenate(pieces, axis=1)
    piece_ids = jnp.arange(tm_count * frames, dtype=jnp.int32)
    frame_ids = ((tm_index - piece_ids // frames) % tm_count) * frames + piece_ids % frames
    valid_tokens = jnp.take(jnp.tile(frame_valid, (1, lat_rows)), frame_ids, axis=0)
    temporal = temporal_attention(
        own_q.reshape(frames, token_count, head_count, DH),
        gathered[0],
        gathered[1],
        valid_tokens,
        frame_ids[:frames],
        frame_ids,
        scale,
    )
    temporal = temporal.reshape(frames, token_count, model_width)
    mixed = combine_partials(partials, temporal).reshape(frames, lat_rows, columns, model_width)
    half_width = model_width // 2
    branch_index = lax.axis_index("branch")
    own_half = lax.dynamic_slice_in_dim(mixed, branch_index * half_width, half_width, 3)
    other_half = lax.dynamic_slice_in_dim(mixed, (1 - branch_index) * half_width, half_width, 3)
    partner = from_partner(other_half, "branch", 0)
    is_conditional = branch_index == 0
    conditional = jnp.where(is_conditional, own_half, partner).astype(jnp.float32)
    unconditional = jnp.where(is_conditional, partner, own_half).astype(jnp.float32)
    return (unconditional + guidance_weight * (conditional - unconditional)).astype(jnp.bfloat16)


def solution(mesh):
    in_specs = (
        P(("groups", "branch"), "tm", None, "lon", None),
        P(("groups", "branch"), "tm", None, "lon", None),
        P(("groups", "branch"), "tm", None, "lon", None),
        P(("groups", "lon"), None),
        P("groups", "lon"),
    )
    out_specs = P(("groups", "tm"), None, "lon", "branch")
    return jax.shard_map(local, mesh=mesh, in_specs=in_specs, out_specs=out_specs, check_vma=False)
```

```python
import functools

import jax
import jax.numpy as jnp
from jax import lax
from jax.experimental import pallas as pl
from jax.sharding import PartitionSpec as P

DH = 128
BLK = 2
REACH = 7
WIN = 15


guidance_weight = 5.0
masked_score = -1e30


def shifted(value, axis, by):
    count = lax.axis_size(axis)
    return lax.ppermute(value, axis, [(i, (i + by) % count) for i in range(count)])


def from_partner(value, axis, bit):
    return lax.ppermute(value, axis, [(i, i ^ 1 << bit) for i in range(lax.axis_size(axis))])


def group_width(model_width):
    for width in (512, 384, 256):
        if model_width % width == 0:
            return width
    return DH


def spatial_kernel(q_ref, k_ref, v_ref, m_ref, o_ref, lse_ref, *, scale):
    allowed = m_ref[...] > 0
    for head in range(q_ref.shape[-1] // DH):
        lanes = slice(head * DH, (head + 1) * DH)
        scores = (
            lax.dot_general(
                q_ref[:, lanes],
                k_ref[:, lanes],
                (((1,), (1,)), ((), ())),
                preferred_element_type=jnp.float32,
            )
            * scale
        )
        limited = jnp.where(allowed, scores, masked_score)
        maxima = jnp.max(limited, axis=-1, keepdims=True)
        weights = jnp.exp(limited - maxima)
        totals = jnp.sum(weights, axis=-1, keepdims=True)
        result = jnp.dot(
            weights.astype(jnp.bfloat16), v_ref[:, lanes], preferred_element_type=jnp.float32
        )
        o_ref[:, lanes] = (result / totals).astype(o_ref.dtype)
        lse_ref[:, head : head + 1] = maxima + jnp.log(totals)


def spatial_attention(query_flat, key_value_flat, mask, scale, out_dtype=jnp.float32):
    frames, query_count, model_width = query_flat.shape
    key_count = key_value_flat.shape[2]
    head_count = model_width // DH
    width = group_width(model_width)
    groups = model_width // width
    return pl.pallas_call(
        functools.partial(spatial_kernel, scale=scale),
        grid=(frames, groups),
        in_specs=[
            pl.BlockSpec((None, query_count, width), lambda f, g: (f, 0, g)),
            pl.BlockSpec((None, None, key_count, width), lambda f, g: (0, f, 0, g)),
            pl.BlockSpec((None, None, key_count, width), lambda f, g: (1, f, 0, g)),
            pl.BlockSpec((query_count, key_count), lambda f, g: (0, 0)),
        ],
        out_specs=[
            pl.BlockSpec((None, query_count, width), lambda f, g: (f, 0, g)),
            pl.BlockSpec((None, None, query_count, width // DH), lambda f, g: (f, g, 0, 0)),
        ],
        out_shape=[
            jax.ShapeDtypeStruct((frames, query_count, model_width), out_dtype),
            jax.ShapeDtypeStruct((frames, groups, query_count, width // DH), jnp.float32),
        ],
        cost_estimate=pl.CostEstimate(
            flops=4 * frames * query_count * key_count * model_width,
            transcendentals=frames * head_count * query_count * key_count,
            bytes_accessed=2 * model_width * frames * (query_count + 2 * key_count)
            + 4 * frames * query_count * model_width,
        ),
    )(query_flat, key_value_flat, key_value_flat, mask)


def combine_kernel(*refs):
    *parts, temporal_ref, mixed_ref = refs
    outs, lses = parts[0::2], parts[1::2]
    for head in range(mixed_ref.shape[-1] // DH):
        lanes = slice(head * DH, (head + 1) * DH)
        logs = [lse[:, head : head + 1] for lse in lses]
        top = functools.reduce(jnp.maximum, logs)
        weights = [jnp.exp(log - top) for log in logs]
        total = functools.reduce(jnp.add, weights)
        value = functools.reduce(
            jnp.add,
            [w * o[:, lanes].astype(jnp.float32) for w, o in zip(weights, outs)],
        )
        mixed_ref[:, lanes] = (value / total + temporal_ref[:, lanes].astype(jnp.float32)).astype(
            mixed_ref.dtype
        )


def combine_partials(partials, temporal):
    frames, query_count, model_width = temporal.shape
    width = group_width(model_width)
    groups = model_width // width
    big = pl.BlockSpec((None, query_count, width), lambda f, g: (f, 0, g))
    small = pl.BlockSpec((None, None, query_count, width // DH), lambda f, g: (f, g, 0, 0))
    operands = []
    for out, lse in partials:
        operands += [out, lse]
    return pl.pallas_call(
        combine_kernel,
        grid=(frames, groups),
        in_specs=[big, small] * len(partials) + [big],
        out_specs=big,
        out_shape=jax.ShapeDtypeStruct((frames, query_count, model_width), jnp.bfloat16),
    )(*operands, temporal)


def temporal_attention(own_q, all_k, all_v, valid, own_ids, all_ids, scale):
    q32 = own_q.astype(jnp.float32)
    k32 = all_k.astype(jnp.float32)
    scores = jnp.sum(q32[:, None] * k32[None], axis=-1) * scale
    same = own_ids[:, None] == all_ids[None, :]
    allowed = (valid[None, :, :] > 0) | same[:, :, None]
    limited = jnp.where(allowed[..., None], scores, masked_score)
    maxima = jnp.max(limited, axis=1, keepdims=True)
    weights = jnp.exp(limited - maxima)
    totals = jnp.sum(weights, axis=1)
    rounded = lax.reduce_precision(weights, exponent_bits=8, mantissa_bits=7)
    result = jnp.sum(rounded[..., None] * all_v.astype(jnp.float32)[None], axis=1)
    result = lax.reduce_precision(result / totals[..., None], exponent_bits=8, mantissa_bits=7)
    return result.astype(jnp.bfloat16)


def line_gather(block, axis):
    count = lax.axis_size(axis)
    index = lax.axis_index(axis)
    left, right = {}, {}
    from_left = from_right = block
    for step in range(1, count):
        from_left = lax.ppermute(from_left, axis, [(s, s + 1) for s in range(step - 1, count - 1)])
        from_right = lax.ppermute(
            from_right, axis, [(s, s - 1) for s in range(1, count - step + 1)]
        )
        left[step], right[step] = from_left, from_right
    relative = [block]
    for d in range(1, count):
        relative.append(jnp.where(index + d < count, right[d], left[count - d]))
    return relative


def window_mask(query_cols, key_cols, column_map, total_cols, lat_rows):
    block_count = total_cols // BLK
    slots = (key_cols[None, :] // BLK - query_cols[:, None] // BLK + REACH) % block_count
    picks = slots[:, :, None] == jnp.arange(WIN, dtype=jnp.int32)[None, None, :]
    return jnp.any(picks & (column_map[:, None, :] > 0), axis=-1)


def expand_mask(active, lat_rows):
    query_cols, key_cols = active.shape
    return jnp.broadcast_to(
        active[None, :, None, :].astype(jnp.float32), (lat_rows, query_cols, lat_rows, key_cols)
    ).reshape(lat_rows * query_cols, lat_rows * key_cols)


def flat_keys(blocks):
    joined = jnp.concatenate(blocks, axis=3)
    two, frames, lat_rows, cols, model_width = joined.shape
    return joined.reshape(two, frames, lat_rows * cols, model_width)


def spatial_line_of_four(own_q, key_value, window_map, temporal, scale):
    frames, lat_rows, columns, model_width = own_q.shape
    count = 4
    total_cols = count * columns
    half = model_width // 2
    index = lax.axis_index("lon")
    branch_index = lax.axis_index("branch")
    is_middle = (index >= 1) & (index <= count - 2)
    column_ids = jnp.arange(columns, dtype=jnp.int32)
    own_map = jnp.repeat(window_map, BLK, axis=0)
    own_cols = index * columns + column_ids
    guest_map = lax.ppermute(window_map, "lon", [(0, 1), (3, 2)])

    near_cols = ((index - 1) * columns + jnp.arange(3 * columns, dtype=jnp.int32)) % total_cols
    near_valid = jnp.stack([index >= 1, index >= 0, index <= count - 2])
    near_mask = expand_mask(
        window_mask(own_cols, near_cols, own_map, total_cols, lat_rows)
        & jnp.repeat(near_valid, columns)[None, :],
        lat_rows,
    )
    guest_device = jnp.where(index == 1, 0, count - 1)
    near_block = jnp.where(index == 1, index + 1, index - 1)
    far_block = (index + 2) % count
    guest_key_cols = jnp.concatenate(
        [near_block * columns + column_ids, far_block * columns + column_ids]
    )
    guest_mask = expand_mask(
        window_mask(
            guest_device * columns + column_ids,
            guest_key_cols,
            jnp.repeat(guest_map, BLK, axis=0),
            total_cols,
            lat_rows,
        )
        & is_middle,
        lat_rows,
    )
    far_mask = expand_mask(
        window_mask(own_cols, far_block * columns + column_ids, own_map, total_cols, lat_rows)
        & is_middle,
        lat_rows,
    )

    mixed = []
    previous = None
    for chunk in range(2):
        start = jnp.where(chunk == 0, 1 - branch_index, branch_index) * half
        chunk_q = lax.dynamic_slice_in_dim(own_q, start, half, 3)
        chunk_kv = lax.dynamic_slice_in_dim(key_value, start, half, 4)
        if previous is not None:
            chunk_kv, _ = lax.optimization_barrier((chunk_kv, previous))
        query_flat = chunk_q.reshape(frames, lat_rows * columns, half)
        from_left = lax.ppermute(chunk_kv, "lon", [(0, 1), (1, 2), (2, 3)])
        from_right = lax.ppermute(chunk_kv, "lon", [(3, 2), (2, 1), (1, 0)])
        previous = (from_left, from_right)
        near_part = spatial_attention(
            query_flat, flat_keys([from_left, chunk_kv, from_right]), near_mask, scale
        )
        two_away = jnp.where(
            index == 1,
            lax.ppermute(from_right, "lon", [(2, 1)]),
            lax.ppermute(from_left, "lon", [(1, 2)]),
        )
        held_q, _ = lax.optimization_barrier((chunk_q, from_left))
        guest_q = lax.ppermute(held_q, "lon", [(0, 1), (3, 2)])
        near_part, two_away, guest_q = lax.optimization_barrier((near_part, two_away, guest_q))
        guest_near = jnp.where(index == 1, from_right, from_left)
        guest_out, guest_lse = spatial_attention(
            guest_q.reshape(frames, lat_rows * columns, half),
            flat_keys([guest_near, two_away]),
            guest_mask,
            scale,
            jnp.bfloat16,
        )
        returned, returned_lse = lax.ppermute(
            (guest_out, jnp.swapaxes(guest_lse, 2, 3)), "lon", [(1, 0), (2, 3)]
        )
        returned_lse = jnp.where(is_middle, masked_score, jnp.swapaxes(returned_lse, 2, 3))
        far_part = spatial_attention(query_flat, flat_keys([two_away]), far_mask, scale)
        chunk_temporal = lax.dynamic_slice_in_dim(temporal, start, half, 2)
        mixed.append(
            combine_partials(
                [near_part, far_part, (returned, returned_lse)], chunk_temporal
            ).reshape(frames, lat_rows, columns, half)
        )
    return mixed


def local(queries, keys, values, window_map, frame_valid):
    own_q = queries[0]
    own_k = keys[0]
    own_v = values[0]
    frames, lat_rows, columns, model_width = own_q.shape
    head_count = model_width // DH
    scale = DH ** (-0.5)
    reach_cols = REACH * BLK
    lon_count = lax.axis_size("lon")
    total_cols = lon_count * columns
    ext_count = columns + 2 * reach_cols
    key_value = jnp.stack([own_k, own_v])
    column_ids = jnp.arange(columns, dtype=jnp.int32)
    per_column_map = jnp.repeat(window_map, BLK, axis=0)
    token_count = lat_rows * columns
    tm_count = lax.axis_size("tm")
    tm_index = lax.axis_index("tm")
    key_value_rows = key_value.reshape(2, frames, token_count, head_count, DH)
    pieces = [key_value_rows]
    for step_by in range(1, tm_count):
        pieces.append(shifted(key_value_rows, "tm", step_by))
    gathered = jnp.concatenate(pieces, axis=1)
    piece_ids = jnp.arange(tm_count * frames, dtype=jnp.int32)
    frame_ids = ((tm_index - piece_ids // frames) % tm_count) * frames + piece_ids % frames
    valid_tokens = jnp.take(jnp.tile(frame_valid, (1, lat_rows)), frame_ids, axis=0)
    temporal = temporal_attention(
        own_q.reshape(frames, token_count, head_count, DH),
        gathered[0],
        gathered[1],
        valid_tokens,
        frame_ids[:frames],
        frame_ids,
        scale,
    )
    temporal = temporal.reshape(frames, token_count, model_width)
    full_ring = ext_count >= total_cols and WIN * BLK <= total_cols
    if not (full_ring and lon_count == 4):
        if full_ring:
            extended = jnp.concatenate(line_gather(key_value, "lon"), axis=3)
            key_cols = total_cols
            block_count = total_cols // BLK
            first_col = lax.axis_index("lon") * columns
            query_blocks = (first_col + column_ids) // BLK
            key_blocks = ((first_col + jnp.arange(total_cols, dtype=jnp.int32)) % total_cols) // BLK
            slots = (key_blocks[None, :] - query_blocks[:, None] + REACH) % block_count
        else:
            reach_devices = -(-reach_cols // columns)
            left_parts, right_parts = [], []
            for step_by in range(1, reach_devices + 1):
                need = min(columns, reach_cols - (step_by - 1) * columns)
                left_parts.insert(
                    0, shifted(key_value[:, :, :, columns - need :, :], "lon", step_by)
                )
                right_parts.append(shifted(key_value[:, :, :, :need, :], "lon", -step_by))
            extended = jnp.concatenate(left_parts + [key_value] + right_parts, axis=3)
            key_cols = ext_count
            ext_ids = jnp.arange(ext_count, dtype=jnp.int32)
            slots = ext_ids[None, :] // BLK - column_ids[:, None] // BLK
        picks = slots[:, :, None] == jnp.arange(WIN, dtype=jnp.int32)[None, None, :]
        active = jnp.any(picks & (per_column_map[:, None, :] > 0), axis=-1)
        query_flat = own_q.reshape(frames, lat_rows * columns, model_width)
        key_value_flat = extended.reshape(2, frames, lat_rows * key_cols, model_width)
        partials = [
            spatial_attention(query_flat, key_value_flat, expand_mask(active, lat_rows), scale)
        ]

    half_width = model_width // 2
    branch_index = lax.axis_index("branch")
    if full_ring and lon_count == 4:
        other_half, own_half = spatial_line_of_four(own_q, key_value, window_map, temporal, scale)
    else:
        mixed = combine_partials(partials, temporal).reshape(
            frames, lat_rows, columns, model_width
        )
        own_half = lax.dynamic_slice_in_dim(mixed, branch_index * half_width, half_width, 3)
        other_half = lax.dynamic_slice_in_dim(
            mixed, (1 - branch_index) * half_width, half_width, 3
        )
    partner = from_partner(other_half, "branch", 0)
    is_conditional = branch_index == 0
    conditional = jnp.where(is_conditional, own_half, partner).astype(jnp.float32)
    unconditional = jnp.where(is_conditional, partner, own_half).astype(jnp.float32)
    return (unconditional + guidance_weight * (conditional - unconditional)).astype(jnp.bfloat16)


def solution(mesh):
    in_specs = (
        P(("groups", "branch"), "tm", None, "lon", None),
        P(("groups", "branch"), "tm", None, "lon", None),
        P(("groups", "branch"), "tm", None, "lon", None),
        P(("groups", "lon"), None),
        P("groups", "lon"),
    )
    out_specs = P(("groups", "tm"), None, "lon", "branch")
    return jax.shard_map(local, mesh=mesh, in_specs=in_specs, out_specs=out_specs, check_vma=False)
```

```python
import functools

import jax
import jax.numpy as jnp
from jax import lax
from jax.experimental import pallas as pl
from jax.sharding import PartitionSpec as P

DH = 128
BLK = 2
REACH = 7
WIN = 15


guidance_weight = 5.0
masked_score = -1e30


def shifted(value, axis, by):
    count = lax.axis_size(axis)
    return lax.ppermute(value, axis, [(i, (i + by) % count) for i in range(count)])


def from_partner(value, axis, bit):
    return lax.ppermute(value, axis, [(i, i ^ 1 << bit) for i in range(lax.axis_size(axis))])


def group_width(model_width):
    for width in (512, 384, 256):
        if model_width % width == 0:
            return width
    return DH


def spatial_kernel(q_ref, k_ref, v_ref, m_ref, o_ref, lse_ref, *, scale):
    allowed = m_ref[...] > 0
    for head in range(q_ref.shape[-1] // DH):
        lanes = slice(head * DH, (head + 1) * DH)
        scores = (
            lax.dot_general(
                q_ref[:, lanes],
                k_ref[:, lanes],
                (((1,), (1,)), ((), ())),
                preferred_element_type=jnp.float32,
            )
            * scale
        )
        limited = jnp.where(allowed, scores, masked_score)
        maxima = jnp.max(limited, axis=-1, keepdims=True)
        weights = jnp.exp(limited - maxima)
        totals = jnp.sum(weights, axis=-1, keepdims=True)
        result = jnp.dot(
            weights.astype(jnp.bfloat16), v_ref[:, lanes], preferred_element_type=jnp.float32
        )
        o_ref[:, lanes] = result / totals
        lse_ref[:, head : head + 1] = maxima + jnp.log(totals)


def spatial_attention(query_flat, key_value_flat, mask, scale):
    frames, query_count, model_width = query_flat.shape
    key_count = key_value_flat.shape[2]
    head_count = model_width // DH
    width = group_width(model_width)
    groups = model_width // width
    return pl.pallas_call(
        functools.partial(spatial_kernel, scale=scale),
        grid=(frames, groups),
        in_specs=[
            pl.BlockSpec((None, query_count, width), lambda f, g: (f, 0, g)),
            pl.BlockSpec((None, None, key_count, width), lambda f, g: (0, f, 0, g)),
            pl.BlockSpec((None, None, key_count, width), lambda f, g: (1, f, 0, g)),
            pl.BlockSpec((query_count, key_count), lambda f, g: (0, 0)),
        ],
        out_specs=[
            pl.BlockSpec((None, query_count, width), lambda f, g: (f, 0, g)),
            pl.BlockSpec((None, None, query_count, width // DH), lambda f, g: (f, g, 0, 0)),
        ],
        out_shape=[
            jax.ShapeDtypeStruct((frames, query_count, model_width), jnp.float32),
            jax.ShapeDtypeStruct((frames, groups, query_count, width // DH), jnp.float32),
        ],
        cost_estimate=pl.CostEstimate(
            flops=4 * frames * query_count * key_count * model_width,
            transcendentals=frames * head_count * query_count * key_count,
            bytes_accessed=2 * model_width * frames * (query_count + 2 * key_count)
            + 4 * frames * query_count * model_width,
        ),
    )(query_flat, key_value_flat, key_value_flat, mask)


def combine_kernel(*refs):
    *parts, temporal_ref, mixed_ref = refs
    outs, lses = parts[0::2], parts[1::2]
    for head in range(mixed_ref.shape[-1] // DH):
        lanes = slice(head * DH, (head + 1) * DH)
        logs = [lse[:, head : head + 1] for lse in lses]
        top = functools.reduce(jnp.maximum, logs)
        weights = [jnp.exp(log - top) for log in logs]
        total = functools.reduce(jnp.add, weights)
        value = functools.reduce(
            jnp.add,
            [w * o[:, lanes].astype(jnp.float32) for w, o in zip(weights, outs)],
        )
        mixed_ref[:, lanes] = (value / total + temporal_ref[:, lanes].astype(jnp.float32)).astype(
            mixed_ref.dtype
        )


def combine_partials(partials, temporal):
    frames, query_count, model_width = temporal.shape
    width = group_width(model_width)
    groups = model_width // width
    big = pl.BlockSpec((None, query_count, width), lambda f, g: (f, 0, g))
    small = pl.BlockSpec((None, None, query_count, width // DH), lambda f, g: (f, g, 0, 0))
    operands = []
    for out, lse in partials:
        operands += [out, lse]
    return pl.pallas_call(
        combine_kernel,
        grid=(frames, groups),
        in_specs=[big, small] * len(partials) + [big],
        out_specs=big,
        out_shape=jax.ShapeDtypeStruct((frames, query_count, model_width), jnp.bfloat16),
    )(*operands, temporal)


def temporal_attention(own_q, all_k, all_v, valid, own_ids, all_ids, scale):
    q32 = own_q.astype(jnp.float32)
    k32 = all_k.astype(jnp.float32)
    scores = jnp.sum(q32[:, None] * k32[None], axis=-1) * scale
    same = own_ids[:, None] == all_ids[None, :]
    allowed = (valid[None, :, :] > 0) | same[:, :, None]
    limited = jnp.where(allowed[..., None], scores, masked_score)
    maxima = jnp.max(limited, axis=1, keepdims=True)
    weights = jnp.exp(limited - maxima)
    totals = jnp.sum(weights, axis=1)
    rounded = lax.reduce_precision(weights, exponent_bits=8, mantissa_bits=7)
    result = jnp.sum(rounded[..., None] * all_v.astype(jnp.float32)[None], axis=1)
    result = lax.reduce_precision(result / totals[..., None], exponent_bits=8, mantissa_bits=7)
    return result.astype(jnp.bfloat16)


def line_gather(block, axis):
    count = lax.axis_size(axis)
    index = lax.axis_index(axis)
    left, right = {}, {}
    from_left = from_right = block
    for step in range(1, count):
        from_left = lax.ppermute(from_left, axis, [(s, s + 1) for s in range(step - 1, count - 1)])
        from_right = lax.ppermute(
            from_right, axis, [(s, s - 1) for s in range(1, count - step + 1)]
        )
        left[step], right[step] = from_left, from_right
    relative = [block]
    for d in range(1, count):
        relative.append(jnp.where(index + d < count, right[d], left[count - d]))
    return relative


def window_mask(query_cols, key_cols, column_map, total_cols, lat_rows):
    block_count = total_cols // BLK
    slots = (key_cols[None, :] // BLK - query_cols[:, None] // BLK + REACH) % block_count
    picks = slots[:, :, None] == jnp.arange(WIN, dtype=jnp.int32)[None, None, :]
    return jnp.any(picks & (column_map[:, None, :] > 0), axis=-1)


def expand_mask(active, lat_rows):
    query_cols, key_cols = active.shape
    return jnp.broadcast_to(
        active[None, :, None, :].astype(jnp.float32), (lat_rows, query_cols, lat_rows, key_cols)
    ).reshape(lat_rows * query_cols, lat_rows * key_cols)


def flat_keys(blocks):
    joined = jnp.concatenate(blocks, axis=3)
    two, frames, lat_rows, cols, model_width = joined.shape
    return joined.reshape(two, frames, lat_rows * cols, model_width)


def spatial_line_of_four(own_q, key_value, window_map, scale):
    frames, lat_rows, columns, model_width = own_q.shape
    count = 4
    total_cols = count * columns
    index = lax.axis_index("lon")
    is_middle = (index >= 1) & (index <= count - 2)
    column_ids = jnp.arange(columns, dtype=jnp.int32)
    own_map = jnp.repeat(window_map, BLK, axis=0)
    own_cols = index * columns + column_ids
    query_flat = own_q.reshape(frames, lat_rows * columns, model_width)

    from_left = lax.ppermute(key_value, "lon", [(0, 1), (1, 2), (2, 3)])
    from_right = lax.ppermute(key_value, "lon", [(3, 2), (2, 1), (1, 0)])
    guest_map = lax.ppermute(window_map, "lon", [(0, 1), (3, 2)])

    near_cols = ((index - 1) * columns + jnp.arange(3 * columns, dtype=jnp.int32)) % total_cols
    near_valid = jnp.stack([index >= 1, index >= 0, index <= count - 2])
    near_active = window_mask(own_cols, near_cols, own_map, total_cols, lat_rows) & jnp.repeat(
        near_valid, columns
    )[None, :]
    near_part = spatial_attention(
        query_flat,
        flat_keys([from_left, key_value, from_right]),
        expand_mask(near_active, lat_rows),
        scale,
    )

    two_away = jnp.where(
        index <= 1,
        lax.ppermute(from_right, "lon", [(2, 1), (1, 0)]),
        lax.ppermute(from_left, "lon", [(1, 2), (2, 3)]),
    )
    held_q, _ = lax.optimization_barrier((own_q, from_left))
    guest_q = lax.ppermute(held_q, "lon", [(0, 1), (3, 2)])
    near_part, two_away, guest_q = lax.optimization_barrier((near_part, two_away, guest_q))

    guest_device = jnp.where(index == 1, 0, count - 1)
    far_block = (index + 2) % count
    far_cols = far_block * columns + column_ids
    guest_active = window_mask(
        guest_device * columns + column_ids,
        far_cols,
        jnp.repeat(guest_map, BLK, axis=0),
        total_cols,
        lat_rows,
    ) & is_middle
    far_keys = flat_keys([two_away])
    guest_out, guest_lse = spatial_attention(
        guest_q.reshape(frames, lat_rows * columns, model_width),
        far_keys,
        expand_mask(guest_active, lat_rows),
        scale,
    )
    lse_shape = guest_lse.shape
    returned, returned_lse = lax.ppermute(
        (guest_out.astype(jnp.bfloat16), jnp.swapaxes(guest_lse, 2, 3)),
        "lon",
        [(1, 0), (2, 3)],
    )
    returned_lse = jnp.where(is_middle, masked_score, jnp.swapaxes(returned_lse, 2, 3))
    assert returned_lse.shape == lse_shape

    far_active = window_mask(own_cols, far_cols, own_map, total_cols, lat_rows)
    far_part = spatial_attention(query_flat, far_keys, expand_mask(far_active, lat_rows), scale)
    return [near_part, far_part, (returned, returned_lse)]


def local(queries, keys, values, window_map, frame_valid):
    own_q = queries[0]
    own_k = keys[0]
    own_v = values[0]
    frames, lat_rows, columns, model_width = own_q.shape
    head_count = model_width // DH
    scale = DH ** (-0.5)
    reach_cols = REACH * BLK
    lon_count = lax.axis_size("lon")
    total_cols = lon_count * columns
    ext_count = columns + 2 * reach_cols
    key_value = jnp.stack([own_k, own_v])
    column_ids = jnp.arange(columns, dtype=jnp.int32)
    per_column_map = jnp.repeat(window_map, BLK, axis=0)
    full_ring = ext_count >= total_cols and WIN * BLK <= total_cols
    if full_ring and lon_count == 4:
        partials = spatial_line_of_four(own_q, key_value, window_map, scale)
    else:
        if full_ring:
            extended = jnp.concatenate(line_gather(key_value, "lon"), axis=3)
            key_cols = total_cols
            block_count = total_cols // BLK
            first_col = lax.axis_index("lon") * columns
            query_blocks = (first_col + column_ids) // BLK
            key_blocks = ((first_col + jnp.arange(total_cols, dtype=jnp.int32)) % total_cols) // BLK
            slots = (key_blocks[None, :] - query_blocks[:, None] + REACH) % block_count
        else:
            reach_devices = -(-reach_cols // columns)
            left_parts, right_parts = [], []
            for step_by in range(1, reach_devices + 1):
                need = min(columns, reach_cols - (step_by - 1) * columns)
                left_parts.insert(
                    0, shifted(key_value[:, :, :, columns - need :, :], "lon", step_by)
                )
                right_parts.append(shifted(key_value[:, :, :, :need, :], "lon", -step_by))
            extended = jnp.concatenate(left_parts + [key_value] + right_parts, axis=3)
            key_cols = ext_count
            ext_ids = jnp.arange(ext_count, dtype=jnp.int32)
            slots = ext_ids[None, :] // BLK - column_ids[:, None] // BLK
        picks = slots[:, :, None] == jnp.arange(WIN, dtype=jnp.int32)[None, None, :]
        active = jnp.any(picks & (per_column_map[:, None, :] > 0), axis=-1)
        query_flat = own_q.reshape(frames, lat_rows * columns, model_width)
        key_value_flat = extended.reshape(2, frames, lat_rows * key_cols, model_width)
        partials = [
            spatial_attention(query_flat, key_value_flat, expand_mask(active, lat_rows), scale)
        ]

    token_count = lat_rows * columns
    tm_count = lax.axis_size("tm")
    tm_index = lax.axis_index("tm")
    key_value_rows = key_value.reshape(2, frames, token_count, head_count, DH)
    pieces = [key_value_rows]
    for step_by in range(1, tm_count):
        pieces.append(shifted(key_value_rows, "tm", step_by))
    gathered = jnp.concatenate(pieces, axis=1)
    piece_ids = jnp.arange(tm_count * frames, dtype=jnp.int32)
    frame_ids = ((tm_index - piece_ids // frames) % tm_count) * frames + piece_ids % frames
    valid_tokens = jnp.take(jnp.tile(frame_valid, (1, lat_rows)), frame_ids, axis=0)
    temporal = temporal_attention(
        own_q.reshape(frames, token_count, head_count, DH),
        gathered[0],
        gathered[1],
        valid_tokens,
        frame_ids[:frames],
        frame_ids,
        scale,
    )
    temporal = temporal.reshape(frames, token_count, model_width)
    mixed = combine_partials(partials, temporal).reshape(frames, lat_rows, columns, model_width)
    half_width = model_width // 2
    branch_index = lax.axis_index("branch")
    own_half = lax.dynamic_slice_in_dim(mixed, branch_index * half_width, half_width, 3)
    other_half = lax.dynamic_slice_in_dim(mixed, (1 - branch_index) * half_width, half_width, 3)
    partner = from_partner(other_half, "branch", 0)
    is_conditional = branch_index == 0
    conditional = jnp.where(is_conditional, own_half, partner).astype(jnp.float32)
    unconditional = jnp.where(is_conditional, partner, own_half).astype(jnp.float32)
    return (unconditional + guidance_weight * (conditional - unconditional)).astype(jnp.bfloat16)


def solution(mesh):
    in_specs = (
        P(("groups", "branch"), "tm", None, "lon", None),
        P(("groups", "branch"), "tm", None, "lon", None),
        P(("groups", "branch"), "tm", None, "lon", None),
        P(("groups", "lon"), None),
        P("groups", "lon"),
    )
    out_specs = P(("groups", "tm"), None, "lon", "branch")
    return jax.shard_map(local, mesh=mesh, in_specs=in_specs, out_specs=out_specs, check_vma=False)
```

```python
import functools

import jax
import jax.numpy as jnp
from jax import lax
from jax.experimental import pallas as pl
from jax.experimental.pallas import tpu as pltpu
from jax.sharding import PartitionSpec as P

DH = 128
BLK = 2
REACH = 7
WIN = 15


guidance_weight = 5.0
masked_score = -1e30


def shifted(value, axis, by):
    count = lax.axis_size(axis)
    return lax.ppermute(value, axis, [(i, (i + by) % count) for i in range(count)])


def from_partner(value, axis, bit):
    return lax.ppermute(value, axis, [(i, i ^ 1 << bit) for i in range(lax.axis_size(axis))])


def group_width(model_width):
    for width in (512, 384, 256):
        if model_width % width == 0:
            return width
    return DH


def spatial_kernel(first_ref, q_ref, k_ref, v_ref, m_ref, o_ref, lse_ref, *, scale):
    del first_ref
    allowed = m_ref[...] > 0
    for head in range(q_ref.shape[-1] // DH):
        lanes = slice(head * DH, (head + 1) * DH)
        scores = (
            lax.dot_general(
                q_ref[:, lanes],
                k_ref[:, lanes],
                (((1,), (1,)), ((), ())),
                preferred_element_type=jnp.float32,
            )
            * scale
        )
        limited = jnp.where(allowed, scores, masked_score)
        maxima = jnp.max(limited, axis=-1, keepdims=True)
        weights = jnp.exp(limited - maxima)
        totals = jnp.sum(weights, axis=-1, keepdims=True)
        result = jnp.dot(
            weights.astype(jnp.bfloat16), v_ref[:, lanes], preferred_element_type=jnp.float32
        )
        o_ref[:, lanes] = (result / totals).astype(o_ref.dtype)
        lse_ref[:, head : head + 1] = maxima + jnp.log(totals)


def spatial_attention(
    query_flat, key_value_flat, mask, scale, out_dtype=jnp.float32, first=None, count=None
):
    frames, query_count, model_width = query_flat.shape
    key_count = key_value_flat.shape[2]
    width = group_width(model_width // 2)
    groups = model_width // width
    if first is None:
        first, count = jnp.zeros((1,), jnp.int32), groups
    grid_spec = pltpu.PrefetchScalarGridSpec(
        num_scalar_prefetch=1,
        grid=(frames, count),
        in_specs=[
            pl.BlockSpec((None, query_count, width), lambda f, g, s: (f, 0, s[0] + g)),
            pl.BlockSpec((None, None, key_count, width), lambda f, g, s: (0, f, 0, s[0] + g)),
            pl.BlockSpec((None, None, key_count, width), lambda f, g, s: (1, f, 0, s[0] + g)),
            pl.BlockSpec((query_count, key_count), lambda f, g, s: (0, 0)),
        ],
        out_specs=[
            pl.BlockSpec((None, query_count, width), lambda f, g, s: (f, 0, g)),
            pl.BlockSpec((None, None, query_count, width // DH), lambda f, g, s: (f, g, 0, 0)),
        ],
    )
    used = count * width
    return pl.pallas_call(
        functools.partial(spatial_kernel, scale=scale),
        grid_spec=grid_spec,
        out_shape=[
            jax.ShapeDtypeStruct((frames, query_count, used), out_dtype),
            jax.ShapeDtypeStruct((frames, count, query_count, width // DH), jnp.float32),
        ],
        cost_estimate=pl.CostEstimate(
            flops=4 * frames * query_count * key_count * used,
            transcendentals=frames * (used // DH) * query_count * key_count,
            bytes_accessed=2 * used * frames * (query_count + 2 * key_count)
            + 4 * frames * query_count * used,
        ),
    )(first, query_flat, key_value_flat, key_value_flat, mask)


def combine_kernel(first_ref, *refs):
    del first_ref
    *parts, temporal_ref, mixed_ref = refs
    outs, lses = parts[0::2], parts[1::2]
    for head in range(mixed_ref.shape[-1] // DH):
        lanes = slice(head * DH, (head + 1) * DH)
        logs = [lse[:, head : head + 1] for lse in lses]
        top = functools.reduce(jnp.maximum, logs)
        weights = [jnp.exp(log - top) for log in logs]
        total = functools.reduce(jnp.add, weights)
        value = functools.reduce(
            jnp.add,
            [w * o[:, lanes].astype(jnp.float32) for w, o in zip(weights, outs)],
        )
        mixed_ref[:, lanes] = (value / total + temporal_ref[:, lanes].astype(jnp.float32)).astype(
            mixed_ref.dtype
        )


def combine_partials(partials, temporal, first=None, count=None):
    frames, query_count, model_width = temporal.shape
    width = group_width(model_width // 2)
    groups = model_width // width
    if first is None:
        first, count = jnp.zeros((1,), jnp.int32), groups
    heads = width // DH
    in_specs, operands = [], []
    for out, lse, whole in partials:
        if whole:
            in_specs += [
                pl.BlockSpec((None, query_count, width), lambda f, g, s: (f, 0, s[0] + g)),
                pl.BlockSpec((None, None, query_count, heads), lambda f, g, s: (f, s[0] + g, 0, 0)),
            ]
        else:
            in_specs += [
                pl.BlockSpec((None, query_count, width), lambda f, g, s: (f, 0, g)),
                pl.BlockSpec((None, None, query_count, heads), lambda f, g, s: (f, g, 0, 0)),
            ]
        operands += [out, lse]
    in_specs.append(pl.BlockSpec((None, query_count, width), lambda f, g, s: (f, 0, s[0] + g)))
    grid_spec = pltpu.PrefetchScalarGridSpec(
        num_scalar_prefetch=1,
        grid=(frames, count),
        in_specs=in_specs,
        out_specs=pl.BlockSpec((None, query_count, width), lambda f, g, s: (f, 0, g)),
    )
    return pl.pallas_call(
        combine_kernel,
        grid_spec=grid_spec,
        out_shape=jax.ShapeDtypeStruct((frames, query_count, count * width), jnp.bfloat16),
    )(first, *operands, temporal)


def temporal_attention(own_q, all_k, all_v, valid, own_ids, all_ids, scale):
    q32 = own_q.astype(jnp.float32)
    k32 = all_k.astype(jnp.float32)
    scores = jnp.sum(q32[:, None] * k32[None], axis=-1) * scale
    same = own_ids[:, None] == all_ids[None, :]
    allowed = (valid[None, :, :] > 0) | same[:, :, None]
    limited = jnp.where(allowed[..., None], scores, masked_score)
    maxima = jnp.max(limited, axis=1, keepdims=True)
    weights = jnp.exp(limited - maxima)
    totals = jnp.sum(weights, axis=1)
    rounded = lax.reduce_precision(weights, exponent_bits=8, mantissa_bits=7)
    result = jnp.sum(rounded[..., None] * all_v.astype(jnp.float32)[None], axis=1)
    result = lax.reduce_precision(result / totals[..., None], exponent_bits=8, mantissa_bits=7)
    return result.astype(jnp.bfloat16)


def line_gather(block, axis):
    count = lax.axis_size(axis)
    index = lax.axis_index(axis)
    left, right = {}, {}
    from_left = from_right = block
    for step in range(1, count):
        from_left = lax.ppermute(from_left, axis, [(s, s + 1) for s in range(step - 1, count - 1)])
        from_right = lax.ppermute(
            from_right, axis, [(s, s - 1) for s in range(1, count - step + 1)]
        )
        left[step], right[step] = from_left, from_right
    relative = [block]
    for d in range(1, count):
        relative.append(jnp.where(index + d < count, right[d], left[count - d]))
    return relative


def window_mask(query_cols, key_cols, column_map, total_cols, lat_rows):
    block_count = total_cols // BLK
    slots = (key_cols[None, :] // BLK - query_cols[:, None] // BLK + REACH) % block_count
    picks = slots[:, :, None] == jnp.arange(WIN, dtype=jnp.int32)[None, None, :]
    return jnp.any(picks & (column_map[:, None, :] > 0), axis=-1)


def expand_mask(active, lat_rows):
    query_cols, key_cols = active.shape
    return jnp.broadcast_to(
        active[None, :, None, :].astype(jnp.float32), (lat_rows, query_cols, lat_rows, key_cols)
    ).reshape(lat_rows * query_cols, lat_rows * key_cols)


def flat_keys(blocks):
    joined = jnp.concatenate(blocks, axis=3)
    two, frames, lat_rows, cols, model_width = joined.shape
    return joined.reshape(two, frames, lat_rows * cols, model_width)


def spatial_line_of_four(own_q, key_value, window_map, temporal, scale):
    frames, lat_rows, columns, model_width = own_q.shape
    count = 4
    total_cols = count * columns
    index = lax.axis_index("lon")
    is_middle = (index >= 1) & (index <= count - 2)
    column_ids = jnp.arange(columns, dtype=jnp.int32)
    own_map = jnp.repeat(window_map, BLK, axis=0)
    own_cols = index * columns + column_ids
    query_flat = own_q.reshape(frames, lat_rows * columns, model_width)

    from_left = lax.ppermute(key_value, "lon", [(0, 1), (1, 2), (2, 3)])
    from_right = lax.ppermute(key_value, "lon", [(3, 2), (2, 1), (1, 0)])
    guest_map = lax.ppermute(window_map, "lon", [(0, 1), (3, 2)])

    near_cols = ((index - 1) * columns + jnp.arange(3 * columns, dtype=jnp.int32)) % total_cols
    near_valid = jnp.stack([index >= 1, index >= 0, index <= count - 2])
    near_active = window_mask(own_cols, near_cols, own_map, total_cols, lat_rows) & jnp.repeat(
        near_valid, columns
    )[None, :]
    near_part = spatial_attention(
        query_flat,
        flat_keys([from_left, key_value, from_right]),
        expand_mask(near_active, lat_rows),
        scale,
    )

    two_away = jnp.where(
        index <= 1,
        lax.ppermute(from_right, "lon", [(2, 1), (1, 0)]),
        lax.ppermute(from_left, "lon", [(1, 2), (2, 3)]),
    )
    held_q, _ = lax.optimization_barrier((own_q, from_left))
    guest_q = lax.ppermute(held_q, "lon", [(0, 1), (3, 2)])
    near_part, two_away, guest_q = lax.optimization_barrier((near_part, two_away, guest_q))

    guest_device = jnp.where(index == 1, 0, count - 1)
    far_block = (index + 2) % count
    far_cols = far_block * columns + column_ids
    guest_active = window_mask(
        guest_device * columns + column_ids,
        far_cols,
        jnp.repeat(guest_map, BLK, axis=0),
        total_cols,
        lat_rows,
    ) & is_middle
    far_keys = flat_keys([two_away])
    far_active = window_mask(own_cols, far_cols, own_map, total_cols, lat_rows)
    guest_flat = guest_q.reshape(frames, lat_rows * columns, model_width)
    guest_mask = expand_mask(guest_active, lat_rows)
    branch_index = lax.axis_index("branch")
    half_groups = (model_width // group_width(model_width // 2)) // 2
    sends = []
    for half_index in (1 - branch_index, branch_index):
        first = jnp.reshape(half_index * half_groups, (1,)).astype(jnp.int32)
        guest_out, guest_lse = spatial_attention(
            guest_flat, far_keys, guest_mask, scale, jnp.bfloat16, first, half_groups
        )
        returned, returned_lse = lax.ppermute(
            (guest_out, jnp.swapaxes(guest_lse, 2, 3)), "lon", [(1, 0), (2, 3)]
        )
        returned_lse = jnp.where(is_middle, masked_score, jnp.swapaxes(returned_lse, 2, 3))
        sends.append((returned, returned_lse, first, guest_out))
    far_query, _ = lax.optimization_barrier((query_flat, sends[-1][3]))
    far_part = spatial_attention(far_query, far_keys, expand_mask(far_active, lat_rows), scale)
    halves = []
    for returned, returned_lse, first, _ in sends:
        halves.append(
            combine_partials(
                [near_part + (True,), far_part + (True,), (returned, returned_lse, False)],
                temporal,
                first,
                half_groups,
            ).reshape(frames, lat_rows, columns, model_width // 2)
        )
    return halves


def local(queries, keys, values, window_map, frame_valid):
    own_q = queries[0]
    own_k = keys[0]
    own_v = values[0]
    frames, lat_rows, columns, model_width = own_q.shape
    head_count = model_width // DH
    scale = DH ** (-0.5)
    reach_cols = REACH * BLK
    lon_count = lax.axis_size("lon")
    total_cols = lon_count * columns
    ext_count = columns + 2 * reach_cols
    key_value = jnp.stack([own_k, own_v])
    column_ids = jnp.arange(columns, dtype=jnp.int32)
    per_column_map = jnp.repeat(window_map, BLK, axis=0)
    token_count = lat_rows * columns
    tm_count = lax.axis_size("tm")
    tm_index = lax.axis_index("tm")
    key_value_rows = key_value.reshape(2, frames, token_count, head_count, DH)
    pieces = [key_value_rows]
    for step_by in range(1, tm_count):
        pieces.append(shifted(key_value_rows, "tm", step_by))
    gathered = jnp.concatenate(pieces, axis=1)
    piece_ids = jnp.arange(tm_count * frames, dtype=jnp.int32)
    frame_ids = ((tm_index - piece_ids // frames) % tm_count) * frames + piece_ids % frames
    valid_tokens = jnp.take(jnp.tile(frame_valid, (1, lat_rows)), frame_ids, axis=0)
    temporal = temporal_attention(
        own_q.reshape(frames, token_count, head_count, DH),
        gathered[0],
        gathered[1],
        valid_tokens,
        frame_ids[:frames],
        frame_ids,
        scale,
    )
    temporal = temporal.reshape(frames, token_count, model_width)
    full_ring = ext_count >= total_cols and WIN * BLK <= total_cols
    if not (full_ring and lon_count == 4):
        if full_ring:
            extended = jnp.concatenate(line_gather(key_value, "lon"), axis=3)
            key_cols = total_cols
            block_count = total_cols // BLK
            first_col = lax.axis_index("lon") * columns
            query_blocks = (first_col + column_ids) // BLK
            key_blocks = ((first_col + jnp.arange(total_cols, dtype=jnp.int32)) % total_cols) // BLK
            slots = (key_blocks[None, :] - query_blocks[:, None] + REACH) % block_count
        else:
            reach_devices = -(-reach_cols // columns)
            left_parts, right_parts = [], []
            for step_by in range(1, reach_devices + 1):
                need = min(columns, reach_cols - (step_by - 1) * columns)
                left_parts.insert(
                    0, shifted(key_value[:, :, :, columns - need :, :], "lon", step_by)
                )
                right_parts.append(shifted(key_value[:, :, :, :need, :], "lon", -step_by))
            extended = jnp.concatenate(left_parts + [key_value] + right_parts, axis=3)
            key_cols = ext_count
            ext_ids = jnp.arange(ext_count, dtype=jnp.int32)
            slots = ext_ids[None, :] // BLK - column_ids[:, None] // BLK
        picks = slots[:, :, None] == jnp.arange(WIN, dtype=jnp.int32)[None, None, :]
        active = jnp.any(picks & (per_column_map[:, None, :] > 0), axis=-1)
        query_flat = own_q.reshape(frames, lat_rows * columns, model_width)
        key_value_flat = extended.reshape(2, frames, lat_rows * key_cols, model_width)
        partials = [
            spatial_attention(query_flat, key_value_flat, expand_mask(active, lat_rows), scale)
        ]

    half_width = model_width // 2
    branch_index = lax.axis_index("branch")
    if full_ring and lon_count == 4:
        other_half, own_half = spatial_line_of_four(own_q, key_value, window_map, temporal, scale)
    else:
        mixed = combine_partials([partial + (True,) for partial in partials], temporal)
        mixed = mixed.reshape(frames, lat_rows, columns, model_width)
        own_half = lax.dynamic_slice_in_dim(mixed, branch_index * half_width, half_width, 3)
        other_half = lax.dynamic_slice_in_dim(
            mixed, (1 - branch_index) * half_width, half_width, 3
        )
    partner = from_partner(other_half, "branch", 0)
    is_conditional = branch_index == 0
    conditional = jnp.where(is_conditional, own_half, partner).astype(jnp.float32)
    unconditional = jnp.where(is_conditional, partner, own_half).astype(jnp.float32)
    return (unconditional + guidance_weight * (conditional - unconditional)).astype(jnp.bfloat16)


def solution(mesh):
    in_specs = (
        P(("groups", "branch"), "tm", None, "lon", None),
        P(("groups", "branch"), "tm", None, "lon", None),
        P(("groups", "branch"), "tm", None, "lon", None),
        P(("groups", "lon"), None),
        P("groups", "lon"),
    )
    out_specs = P(("groups", "tm"), None, "lon", "branch")
    return jax.shard_map(local, mesh=mesh, in_specs=in_specs, out_specs=out_specs, check_vma=False)
```

```python
import functools

import jax
import jax.numpy as jnp
from jax import lax
from jax.experimental import pallas as pl
from jax.sharding import PartitionSpec as P

DH = 128
BLK = 2
REACH = 7
WIN = 15


guidance_weight = 5.0
masked_score = -1e30


def shifted(value, axis, by):
    count = lax.axis_size(axis)
    return lax.ppermute(value, axis, [(i, (i + by) % count) for i in range(count)])


def from_partner(value, axis, bit):
    return lax.ppermute(value, axis, [(i, i ^ 1 << bit) for i in range(lax.axis_size(axis))])


def group_width(model_width):
    for width in (512, 384, 256):
        if model_width % width == 0:
            return width
    return DH


def spatial_kernel(q_ref, k_ref, v_ref, m_ref, o_ref, lse_ref, *, scale):
    allowed = m_ref[...] > 0
    for head in range(q_ref.shape[-1] // DH):
        lanes = slice(head * DH, (head + 1) * DH)
        scores = (
            lax.dot_general(
                q_ref[:, lanes],
                k_ref[:, lanes],
                (((1,), (1,)), ((), ())),
                preferred_element_type=jnp.float32,
            )
            * scale
        )
        limited = jnp.where(allowed, scores, masked_score)
        maxima = jnp.max(limited, axis=-1, keepdims=True)
        weights = jnp.exp(limited - maxima)
        totals = jnp.sum(weights, axis=-1, keepdims=True)
        result = jnp.dot(
            weights.astype(jnp.bfloat16), v_ref[:, lanes], preferred_element_type=jnp.float32
        )
        o_ref[:, lanes] = (result / totals).astype(o_ref.dtype)
        lse_ref[:, head : head + 1] = maxima + jnp.log(totals)


def spatial_attention(query_flat, key_value_flat, mask, scale, out_dtype=jnp.float32):
    frames, query_count, model_width = query_flat.shape
    key_count = key_value_flat.shape[2]
    head_count = model_width // DH
    width = group_width(model_width)
    groups = model_width // width
    return pl.pallas_call(
        functools.partial(spatial_kernel, scale=scale),
        grid=(frames, groups),
        in_specs=[
            pl.BlockSpec((None, query_count, width), lambda f, g: (f, 0, g)),
            pl.BlockSpec((None, None, key_count, width), lambda f, g: (0, f, 0, g)),
            pl.BlockSpec((None, None, key_count, width), lambda f, g: (1, f, 0, g)),
            pl.BlockSpec((query_count, key_count), lambda f, g: (0, 0)),
        ],
        out_specs=[
            pl.BlockSpec((None, query_count, width), lambda f, g: (f, 0, g)),
            pl.BlockSpec((None, None, query_count, width // DH), lambda f, g: (f, g, 0, 0)),
        ],
        out_shape=[
            jax.ShapeDtypeStruct((frames, query_count, model_width), out_dtype),
            jax.ShapeDtypeStruct((frames, groups, query_count, width // DH), jnp.float32),
        ],
        cost_estimate=pl.CostEstimate(
            flops=4 * frames * query_count * key_count * model_width,
            transcendentals=frames * head_count * query_count * key_count,
            bytes_accessed=2 * model_width * frames * (query_count + 2 * key_count)
            + 4 * frames * query_count * model_width,
        ),
    )(query_flat, key_value_flat, key_value_flat, mask)


def combine_kernel(*refs):
    *parts, temporal_ref, mixed_ref = refs
    outs, lses = parts[0::2], parts[1::2]
    for head in range(mixed_ref.shape[-1] // DH):
        lanes = slice(head * DH, (head + 1) * DH)
        logs = [lse[:, head : head + 1] for lse in lses]
        top = functools.reduce(jnp.maximum, logs)
        weights = [jnp.exp(log - top) for log in logs]
        total = functools.reduce(jnp.add, weights)
        value = functools.reduce(
            jnp.add,
            [w * o[:, lanes].astype(jnp.float32) for w, o in zip(weights, outs)],
        )
        mixed_ref[:, lanes] = (value / total + temporal_ref[:, lanes].astype(jnp.float32)).astype(
            mixed_ref.dtype
        )


def merge_kernel(*refs):
    *parts, out_ref, lse_ref = refs
    outs, lses = parts[0::2], parts[1::2]
    for head in range(out_ref.shape[-1] // DH):
        lanes = slice(head * DH, (head + 1) * DH)
        logs = [lse[:, head : head + 1] for lse in lses]
        top = functools.reduce(jnp.maximum, logs)
        weights = [jnp.exp(log - top) for log in logs]
        total = functools.reduce(jnp.add, weights)
        value = functools.reduce(jnp.add, [w * o[:, lanes] for w, o in zip(weights, outs)])
        out_ref[:, lanes] = value / total
        lse_ref[:, head : head + 1] = top + jnp.log(total)


def merge_partials(partials):
    out, lse = partials[0]
    frames, query_count, model_width = out.shape
    width = group_width(model_width)
    groups = model_width // width
    big = pl.BlockSpec((None, query_count, width), lambda f, g: (f, 0, g))
    small = pl.BlockSpec((None, None, query_count, width // DH), lambda f, g: (f, g, 0, 0))
    operands = []
    for out, lse in partials:
        operands += [out, lse]
    return pl.pallas_call(
        merge_kernel,
        grid=(frames, groups),
        in_specs=[big, small] * len(partials),
        out_specs=[big, small],
        out_shape=[
            jax.ShapeDtypeStruct(out.shape, jnp.float32),
            jax.ShapeDtypeStruct(lse.shape, jnp.float32),
        ],
    )(*operands)


def combine_partials(partials, temporal):
    frames, query_count, model_width = temporal.shape
    width = group_width(model_width)
    groups = model_width // width
    big = pl.BlockSpec((None, query_count, width), lambda f, g: (f, 0, g))
    small = pl.BlockSpec((None, None, query_count, width // DH), lambda f, g: (f, g, 0, 0))
    operands = []
    for out, lse in partials:
        operands += [out, lse]
    return pl.pallas_call(
        combine_kernel,
        grid=(frames, groups),
        in_specs=[big, small] * len(partials) + [big],
        out_specs=big,
        out_shape=jax.ShapeDtypeStruct((frames, query_count, model_width), jnp.bfloat16),
    )(*operands, temporal)


def temporal_attention(own_q, all_k, all_v, valid, own_ids, all_ids, scale):
    q32 = own_q.astype(jnp.float32)
    k32 = all_k.astype(jnp.float32)
    scores = jnp.sum(q32[:, None] * k32[None], axis=-1) * scale
    same = own_ids[:, None] == all_ids[None, :]
    allowed = (valid[None, :, :] > 0) | same[:, :, None]
    limited = jnp.where(allowed[..., None], scores, masked_score)
    maxima = jnp.max(limited, axis=1, keepdims=True)
    weights = jnp.exp(limited - maxima)
    totals = jnp.sum(weights, axis=1)
    rounded = lax.reduce_precision(weights, exponent_bits=8, mantissa_bits=7)
    result = jnp.sum(rounded[..., None] * all_v.astype(jnp.float32)[None], axis=1)
    result = lax.reduce_precision(result / totals[..., None], exponent_bits=8, mantissa_bits=7)
    return result.astype(jnp.bfloat16)


def line_gather(block, axis):
    count = lax.axis_size(axis)
    index = lax.axis_index(axis)
    left, right = {}, {}
    from_left = from_right = block
    for step in range(1, count):
        from_left = lax.ppermute(from_left, axis, [(s, s + 1) for s in range(step - 1, count - 1)])
        from_right = lax.ppermute(
            from_right, axis, [(s, s - 1) for s in range(1, count - step + 1)]
        )
        left[step], right[step] = from_left, from_right
    relative = [block]
    for d in range(1, count):
        relative.append(jnp.where(index + d < count, right[d], left[count - d]))
    return relative


def window_mask(query_cols, key_cols, column_map, total_cols, lat_rows):
    block_count = total_cols // BLK
    slots = (key_cols[None, :] // BLK - query_cols[:, None] // BLK + REACH) % block_count
    picks = slots[:, :, None] == jnp.arange(WIN, dtype=jnp.int32)[None, None, :]
    return jnp.any(picks & (column_map[:, None, :] > 0), axis=-1)


def expand_mask(active, lat_rows):
    query_cols, key_cols = active.shape
    return jnp.broadcast_to(
        active[None, :, None, :].astype(jnp.float32), (lat_rows, query_cols, lat_rows, key_cols)
    ).reshape(lat_rows * query_cols, lat_rows * key_cols)


def flat_keys(blocks):
    joined = jnp.concatenate(blocks, axis=3)
    two, frames, lat_rows, cols, model_width = joined.shape
    return joined.reshape(two, frames, lat_rows * cols, model_width)


def spatial_line_of_four(own_q, key_value, window_map, scale):
    frames, lat_rows, columns, model_width = own_q.shape
    count = 4
    total_cols = count * columns
    index = lax.axis_index("lon")
    is_middle = (index >= 1) & (index <= count - 2)
    column_ids = jnp.arange(columns, dtype=jnp.int32)
    own_map = jnp.repeat(window_map, BLK, axis=0)
    own_cols = index * columns + column_ids
    query_flat = own_q.reshape(frames, lat_rows * columns, model_width)

    from_left = lax.ppermute(key_value, "lon", [(0, 1), (1, 2), (2, 3)])
    from_right = lax.ppermute(key_value, "lon", [(3, 2), (2, 1), (1, 0)])
    guest_map = lax.ppermute(window_map, "lon", [(0, 1), (3, 2)])

    near_cols = ((index - 1) * columns + jnp.arange(3 * columns, dtype=jnp.int32)) % total_cols
    near_valid = jnp.stack([index >= 1, index >= 0, index <= count - 2])
    near_active = window_mask(own_cols, near_cols, own_map, total_cols, lat_rows) & jnp.repeat(
        near_valid, columns
    )[None, :]
    near_part = spatial_attention(
        query_flat,
        flat_keys([from_left, key_value, from_right]),
        expand_mask(near_active, lat_rows),
        scale,
    )

    two_away = jnp.where(
        index <= 1,
        lax.ppermute(from_right, "lon", [(2, 1), (1, 0)]),
        lax.ppermute(from_left, "lon", [(1, 2), (2, 3)]),
    )
    held_q, _ = lax.optimization_barrier((own_q, from_left))
    guest_q = lax.ppermute(held_q, "lon", [(0, 1), (3, 2)])
    near_part, two_away, guest_q = lax.optimization_barrier((near_part, two_away, guest_q))

    guest_device = jnp.where(index == 1, 0, count - 1)
    far_block = (index + 2) % count
    far_cols = far_block * columns + column_ids
    guest_active = window_mask(
        guest_device * columns + column_ids,
        far_cols,
        jnp.repeat(guest_map, BLK, axis=0),
        total_cols,
        lat_rows,
    ) & is_middle
    far_keys = flat_keys([two_away])
    guest_out, guest_lse = spatial_attention(
        guest_q.reshape(frames, lat_rows * columns, model_width),
        far_keys,
        expand_mask(guest_active, lat_rows),
        scale,
        jnp.bfloat16,
    )
    lse_shape = guest_lse.shape
    returned, returned_lse = lax.ppermute(
        (guest_out, jnp.swapaxes(guest_lse, 2, 3)),
        "lon",
        [(1, 0), (2, 3)],
    )
    returned_lse = jnp.where(is_middle, masked_score, jnp.swapaxes(returned_lse, 2, 3))
    assert returned_lse.shape == lse_shape

    far_active = window_mask(own_cols, far_cols, own_map, total_cols, lat_rows)
    far_part = spatial_attention(query_flat, far_keys, expand_mask(far_active, lat_rows), scale)
    return [merge_partials([near_part, far_part]), (returned, returned_lse)]


def local(queries, keys, values, window_map, frame_valid):
    own_q = queries[0]
    own_k = keys[0]
    own_v = values[0]
    frames, lat_rows, columns, model_width = own_q.shape
    head_count = model_width // DH
    scale = DH ** (-0.5)
    reach_cols = REACH * BLK
    lon_count = lax.axis_size("lon")
    total_cols = lon_count * columns
    ext_count = columns + 2 * reach_cols
    key_value = jnp.stack([own_k, own_v])
    column_ids = jnp.arange(columns, dtype=jnp.int32)
    per_column_map = jnp.repeat(window_map, BLK, axis=0)
    full_ring = ext_count >= total_cols and WIN * BLK <= total_cols
    if full_ring and lon_count == 4:
        partials = spatial_line_of_four(own_q, key_value, window_map, scale)
    else:
        if full_ring:
            extended = jnp.concatenate(line_gather(key_value, "lon"), axis=3)
            key_cols = total_cols
            block_count = total_cols // BLK
            first_col = lax.axis_index("lon") * columns
            query_blocks = (first_col + column_ids) // BLK
            key_blocks = ((first_col + jnp.arange(total_cols, dtype=jnp.int32)) % total_cols) // BLK
            slots = (key_blocks[None, :] - query_blocks[:, None] + REACH) % block_count
        else:
            reach_devices = -(-reach_cols // columns)
            left_parts, right_parts = [], []
            for step_by in range(1, reach_devices + 1):
                need = min(columns, reach_cols - (step_by - 1) * columns)
                left_parts.insert(
                    0, shifted(key_value[:, :, :, columns - need :, :], "lon", step_by)
                )
                right_parts.append(shifted(key_value[:, :, :, :need, :], "lon", -step_by))
            extended = jnp.concatenate(left_parts + [key_value] + right_parts, axis=3)
            key_cols = ext_count
            ext_ids = jnp.arange(ext_count, dtype=jnp.int32)
            slots = ext_ids[None, :] // BLK - column_ids[:, None] // BLK
        picks = slots[:, :, None] == jnp.arange(WIN, dtype=jnp.int32)[None, None, :]
        active = jnp.any(picks & (per_column_map[:, None, :] > 0), axis=-1)
        query_flat = own_q.reshape(frames, lat_rows * columns, model_width)
        key_value_flat = extended.reshape(2, frames, lat_rows * key_cols, model_width)
        partials = [
            spatial_attention(query_flat, key_value_flat, expand_mask(active, lat_rows), scale)
        ]

    token_count = lat_rows * columns
    tm_count = lax.axis_size("tm")
    tm_index = lax.axis_index("tm")
    key_value_rows = key_value.reshape(2, frames, token_count, head_count, DH)
    pieces = [key_value_rows]
    for step_by in range(1, tm_count):
        pieces.append(shifted(key_value_rows, "tm", step_by))
    gathered = jnp.concatenate(pieces, axis=1)
    piece_ids = jnp.arange(tm_count * frames, dtype=jnp.int32)
    frame_ids = ((tm_index - piece_ids // frames) % tm_count) * frames + piece_ids % frames
    valid_tokens = jnp.take(jnp.tile(frame_valid, (1, lat_rows)), frame_ids, axis=0)
    temporal = temporal_attention(
        own_q.reshape(frames, token_count, head_count, DH),
        gathered[0],
        gathered[1],
        valid_tokens,
        frame_ids[:frames],
        frame_ids,
        scale,
    )
    temporal = temporal.reshape(frames, token_count, model_width)
    mixed = combine_partials(partials, temporal).reshape(frames, lat_rows, columns, model_width)
    half_width = model_width // 2
    branch_index = lax.axis_index("branch")
    own_half = lax.dynamic_slice_in_dim(mixed, branch_index * half_width, half_width, 3)
    other_half = lax.dynamic_slice_in_dim(mixed, (1 - branch_index) * half_width, half_width, 3)
    partner = from_partner(other_half, "branch", 0)
    is_conditional = branch_index == 0
    conditional = jnp.where(is_conditional, own_half, partner).astype(jnp.float32)
    unconditional = jnp.where(is_conditional, partner, own_half).astype(jnp.float32)
    return (unconditional + guidance_weight * (conditional - unconditional)).astype(jnp.bfloat16)


def solution(mesh):
    in_specs = (
        P(("groups", "branch"), "tm", None, "lon", None),
        P(("groups", "branch"), "tm", None, "lon", None),
        P(("groups", "branch"), "tm", None, "lon", None),
        P(("groups", "lon"), None),
        P("groups", "lon"),
    )
    out_specs = P(("groups", "tm"), None, "lon", "branch")
    return jax.shard_map(local, mesh=mesh, in_specs=in_specs, out_specs=out_specs, check_vma=False)
```

```python
import functools

import jax
import jax.numpy as jnp
from jax import lax
from jax.experimental import pallas as pl
from jax.sharding import PartitionSpec as P

DH = 128
BLK = 2
REACH = 7
WIN = 15


guidance_weight = 5.0
masked_score = -1e30


def shifted(value, axis, by):
    count = lax.axis_size(axis)
    return lax.ppermute(value, axis, [(i, (i + by) % count) for i in range(count)])


def from_partner(value, axis, bit):
    return lax.ppermute(value, axis, [(i, i ^ 1 << bit) for i in range(lax.axis_size(axis))])


def group_width(model_width):
    for width in (512, 384, 256):
        if model_width % width == 0:
            return width
    return DH


def spatial_kernel(q_ref, k_ref, v_ref, m_ref, o_ref, lse_ref, *, scale):
    allowed = m_ref[...] > 0
    for head in range(q_ref.shape[-1] // DH):
        lanes = slice(head * DH, (head + 1) * DH)
        scores = (
            lax.dot_general(
                q_ref[:, lanes],
                k_ref[:, lanes],
                (((1,), (1,)), ((), ())),
                preferred_element_type=jnp.float32,
            )
            * scale
        )
        limited = jnp.where(allowed, scores, masked_score)
        maxima = jnp.max(limited, axis=-1, keepdims=True)
        weights = jnp.exp(limited - maxima)
        totals = jnp.sum(weights, axis=-1, keepdims=True)
        result = jnp.dot(
            weights.astype(jnp.bfloat16), v_ref[:, lanes], preferred_element_type=jnp.float32
        )
        o_ref[:, lanes] = result / totals
        lse_ref[:, head : head + 1] = maxima + jnp.log(totals)


def spatial_attention(query_flat, key_value_flat, mask, scale):
    frames, query_count, model_width = query_flat.shape
    key_count = key_value_flat.shape[2]
    head_count = model_width // DH
    width = group_width(model_width)
    groups = model_width // width
    return pl.pallas_call(
        functools.partial(spatial_kernel, scale=scale),
        grid=(frames, groups),
        in_specs=[
            pl.BlockSpec((None, query_count, width), lambda f, g: (f, 0, g)),
            pl.BlockSpec((None, None, key_count, width), lambda f, g: (0, f, 0, g)),
            pl.BlockSpec((None, None, key_count, width), lambda f, g: (1, f, 0, g)),
            pl.BlockSpec((query_count, key_count), lambda f, g: (0, 0)),
        ],
        out_specs=[
            pl.BlockSpec((None, query_count, width), lambda f, g: (f, 0, g)),
            pl.BlockSpec((None, None, query_count, width // DH), lambda f, g: (f, g, 0, 0)),
        ],
        out_shape=[
            jax.ShapeDtypeStruct((frames, query_count, model_width), jnp.float32),
            jax.ShapeDtypeStruct((frames, groups, query_count, width // DH), jnp.float32),
        ],
        cost_estimate=pl.CostEstimate(
            flops=4 * frames * query_count * key_count * model_width,
            transcendentals=frames * head_count * query_count * key_count,
            bytes_accessed=2 * model_width * frames * (query_count + 2 * key_count)
            + 4 * frames * query_count * model_width,
        ),
    )(query_flat, key_value_flat, key_value_flat, mask)


def combine_kernel(*refs):
    *parts, temporal_ref, mixed_ref = refs
    outs, lses = parts[0::2], parts[1::2]
    for head in range(mixed_ref.shape[-1] // DH):
        lanes = slice(head * DH, (head + 1) * DH)
        logs = [lse[:, head : head + 1] for lse in lses]
        top = functools.reduce(jnp.maximum, logs)
        weights = [jnp.exp(log - top) for log in logs]
        total = functools.reduce(jnp.add, weights)
        value = functools.reduce(
            jnp.add,
            [w * o[:, lanes].astype(jnp.float32) for w, o in zip(weights, outs)],
        )
        mixed_ref[:, lanes] = (value / total + temporal_ref[:, lanes].astype(jnp.float32)).astype(
            mixed_ref.dtype
        )


def combine_partials(partials, temporal):
    frames, query_count, model_width = temporal.shape
    width = group_width(model_width)
    groups = model_width // width
    big = pl.BlockSpec((None, query_count, width), lambda f, g: (f, 0, g))
    small = pl.BlockSpec((None, None, query_count, width // DH), lambda f, g: (f, g, 0, 0))
    operands = []
    for out, lse in partials:
        operands += [out, lse]
    return pl.pallas_call(
        combine_kernel,
        grid=(frames, groups),
        in_specs=[big, small] * len(partials) + [big],
        out_specs=big,
        out_shape=jax.ShapeDtypeStruct((frames, query_count, model_width), jnp.bfloat16),
    )(*operands, temporal)


def temporal_attention(own_q, all_k, all_v, valid, own_ids, all_ids, scale):
    q32 = own_q.astype(jnp.float32)
    k32 = all_k.astype(jnp.float32)
    scores = jnp.sum(q32[:, None] * k32[None], axis=-1) * scale
    same = own_ids[:, None] == all_ids[None, :]
    allowed = (valid[None, :, :] > 0) | same[:, :, None]
    limited = jnp.where(allowed[..., None], scores, masked_score)
    maxima = jnp.max(limited, axis=1, keepdims=True)
    weights = jnp.exp(limited - maxima)
    totals = jnp.sum(weights, axis=1)
    rounded = lax.reduce_precision(weights, exponent_bits=8, mantissa_bits=7)
    result = jnp.sum(rounded[..., None] * all_v.astype(jnp.float32)[None], axis=1)
    result = lax.reduce_precision(result / totals[..., None], exponent_bits=8, mantissa_bits=7)
    return result.astype(jnp.bfloat16)


def line_gather(block, axis):
    count = lax.axis_size(axis)
    index = lax.axis_index(axis)
    left, right = {}, {}
    from_left = from_right = block
    for step in range(1, count):
        from_left = lax.ppermute(from_left, axis, [(s, s + 1) for s in range(step - 1, count - 1)])
        from_right = lax.ppermute(
            from_right, axis, [(s, s - 1) for s in range(1, count - step + 1)]
        )
        left[step], right[step] = from_left, from_right
    relative = [block]
    for d in range(1, count):
        relative.append(jnp.where(index + d < count, right[d], left[count - d]))
    return relative


def window_mask(query_cols, key_cols, column_map, total_cols, lat_rows):
    block_count = total_cols // BLK
    slots = (key_cols[None, :] // BLK - query_cols[:, None] // BLK + REACH) % block_count
    picks = slots[:, :, None] == jnp.arange(WIN, dtype=jnp.int32)[None, None, :]
    return jnp.any(picks & (column_map[:, None, :] > 0), axis=-1)


def expand_mask(active, lat_rows):
    query_cols, key_cols = active.shape
    return jnp.broadcast_to(
        active[None, :, None, :].astype(jnp.float32), (lat_rows, query_cols, lat_rows, key_cols)
    ).reshape(lat_rows * query_cols, lat_rows * key_cols)


def flat_keys(blocks):
    joined = jnp.concatenate(blocks, axis=3)
    two, frames, lat_rows, cols, model_width = joined.shape
    return joined.reshape(two, frames, lat_rows * cols, model_width)


def send_pair(pair, axis, pairs):
    return tuple(lax.ppermute(part, axis, pairs) for part in pair)


def flat_pairs(pairs):
    joined = jnp.stack([jnp.concatenate([pair[i] for pair in pairs], axis=2) for i in (0, 1)])
    two, frames, lat_rows, cols, model_width = joined.shape
    return joined.reshape(two, frames, lat_rows * cols, model_width)


def spatial_line_of_four(own_q, key_value, window_map, scale):
    frames, lat_rows, columns, model_width = own_q.shape
    count = 4
    total_cols = count * columns
    index = lax.axis_index("lon")
    is_middle = (index >= 1) & (index <= count - 2)
    column_ids = jnp.arange(columns, dtype=jnp.int32)
    own_map = jnp.repeat(window_map, BLK, axis=0)
    own_cols = index * columns + column_ids
    query_flat = own_q.reshape(frames, lat_rows * columns, model_width)

    from_left = send_pair(key_value, "lon", [(0, 1), (1, 2), (2, 3)])
    from_right = send_pair(key_value, "lon", [(3, 2), (2, 1), (1, 0)])
    guest_map = lax.ppermute(window_map, "lon", [(0, 1), (3, 2)])

    near_cols = ((index - 1) * columns + jnp.arange(3 * columns, dtype=jnp.int32)) % total_cols
    near_valid = jnp.stack([index >= 1, index >= 0, index <= count - 2])
    near_active = window_mask(own_cols, near_cols, own_map, total_cols, lat_rows) & jnp.repeat(
        near_valid, columns
    )[None, :]
    near_part = spatial_attention(
        query_flat,
        flat_pairs([from_left, key_value, from_right]),
        expand_mask(near_active, lat_rows),
        scale,
    )

    toward_left = send_pair(from_right, "lon", [(2, 1), (1, 0)])
    toward_right = send_pair(from_left, "lon", [(1, 2), (2, 3)])
    two_away = tuple(jnp.where(index <= 1, a, b) for a, b in zip(toward_left, toward_right))
    held_q, _ = lax.optimization_barrier((own_q, from_left[0]))
    guest_q = lax.ppermute(held_q, "lon", [(0, 1), (3, 2)])
    near_part, two_away, guest_q = lax.optimization_barrier((near_part, two_away, guest_q))

    guest_device = jnp.where(index == 1, 0, count - 1)
    far_block = (index + 2) % count
    far_cols = far_block * columns + column_ids
    guest_active = window_mask(
        guest_device * columns + column_ids,
        far_cols,
        jnp.repeat(guest_map, BLK, axis=0),
        total_cols,
        lat_rows,
    ) & is_middle
    far_keys = flat_pairs([two_away])
    guest_out, guest_lse = spatial_attention(
        guest_q.reshape(frames, lat_rows * columns, model_width),
        far_keys,
        expand_mask(guest_active, lat_rows),
        scale,
    )
    lse_shape = guest_lse.shape
    returned, returned_lse = lax.ppermute(
        (guest_out.astype(jnp.bfloat16), jnp.swapaxes(guest_lse, 2, 3)),
        "lon",
        [(1, 0), (2, 3)],
    )
    returned_lse = jnp.where(is_middle, masked_score, jnp.swapaxes(returned_lse, 2, 3))
    assert returned_lse.shape == lse_shape

    far_active = window_mask(own_cols, far_cols, own_map, total_cols, lat_rows)
    far_part = spatial_attention(query_flat, far_keys, expand_mask(far_active, lat_rows), scale)
    return [near_part, far_part, (returned, returned_lse)]


def local(queries, keys, values, window_map, frame_valid):
    own_q = queries[0]
    own_k = keys[0]
    own_v = values[0]
    frames, lat_rows, columns, model_width = own_q.shape
    head_count = model_width // DH
    scale = DH ** (-0.5)
    reach_cols = REACH * BLK
    lon_count = lax.axis_size("lon")
    total_cols = lon_count * columns
    ext_count = columns + 2 * reach_cols
    key_value = jnp.stack([own_k, own_v])
    column_ids = jnp.arange(columns, dtype=jnp.int32)
    per_column_map = jnp.repeat(window_map, BLK, axis=0)
    full_ring = ext_count >= total_cols and WIN * BLK <= total_cols
    if full_ring and lon_count == 4:
        partials = spatial_line_of_four(own_q, (own_k, own_v), window_map, scale)
    else:
        if full_ring:
            extended = jnp.concatenate(line_gather(key_value, "lon"), axis=3)
            key_cols = total_cols
            block_count = total_cols // BLK
            first_col = lax.axis_index("lon") * columns
            query_blocks = (first_col + column_ids) // BLK
            key_blocks = ((first_col + jnp.arange(total_cols, dtype=jnp.int32)) % total_cols) // BLK
            slots = (key_blocks[None, :] - query_blocks[:, None] + REACH) % block_count
        else:
            reach_devices = -(-reach_cols // columns)
            left_parts, right_parts = [], []
            for step_by in range(1, reach_devices + 1):
                need = min(columns, reach_cols - (step_by - 1) * columns)
                left_parts.insert(
                    0, shifted(key_value[:, :, :, columns - need :, :], "lon", step_by)
                )
                right_parts.append(shifted(key_value[:, :, :, :need, :], "lon", -step_by))
            extended = jnp.concatenate(left_parts + [key_value] + right_parts, axis=3)
            key_cols = ext_count
            ext_ids = jnp.arange(ext_count, dtype=jnp.int32)
            slots = ext_ids[None, :] // BLK - column_ids[:, None] // BLK
        picks = slots[:, :, None] == jnp.arange(WIN, dtype=jnp.int32)[None, None, :]
        active = jnp.any(picks & (per_column_map[:, None, :] > 0), axis=-1)
        query_flat = own_q.reshape(frames, lat_rows * columns, model_width)
        key_value_flat = extended.reshape(2, frames, lat_rows * key_cols, model_width)
        partials = [
            spatial_attention(query_flat, key_value_flat, expand_mask(active, lat_rows), scale)
        ]

    token_count = lat_rows * columns
    tm_count = lax.axis_size("tm")
    tm_index = lax.axis_index("tm")
    key_value_rows = key_value.reshape(2, frames, token_count, head_count, DH)
    pieces = [key_value_rows]
    for step_by in range(1, tm_count):
        pieces.append(shifted(key_value_rows, "tm", step_by))
    gathered = jnp.concatenate(pieces, axis=1)
    piece_ids = jnp.arange(tm_count * frames, dtype=jnp.int32)
    frame_ids = ((tm_index - piece_ids // frames) % tm_count) * frames + piece_ids % frames
    valid_tokens = jnp.take(jnp.tile(frame_valid, (1, lat_rows)), frame_ids, axis=0)
    temporal = temporal_attention(
        own_q.reshape(frames, token_count, head_count, DH),
        gathered[0],
        gathered[1],
        valid_tokens,
        frame_ids[:frames],
        frame_ids,
        scale,
    )
    temporal = temporal.reshape(frames, token_count, model_width)
    mixed = combine_partials(partials, temporal).reshape(frames, lat_rows, columns, model_width)
    half_width = model_width // 2
    branch_index = lax.axis_index("branch")
    own_half = lax.dynamic_slice_in_dim(mixed, branch_index * half_width, half_width, 3)
    other_half = lax.dynamic_slice_in_dim(mixed, (1 - branch_index) * half_width, half_width, 3)
    partner = from_partner(other_half, "branch", 0)
    is_conditional = branch_index == 0
    conditional = jnp.where(is_conditional, own_half, partner).astype(jnp.float32)
    unconditional = jnp.where(is_conditional, partner, own_half).astype(jnp.float32)
    return (unconditional + guidance_weight * (conditional - unconditional)).astype(jnp.bfloat16)


def solution(mesh):
    in_specs = (
        P(("groups", "branch"), "tm", None, "lon", None),
        P(("groups", "branch"), "tm", None, "lon", None),
        P(("groups", "branch"), "tm", None, "lon", None),
        P(("groups", "lon"), None),
        P("groups", "lon"),
    )
    out_specs = P(("groups", "tm"), None, "lon", "branch")
    return jax.shard_map(local, mesh=mesh, in_specs=in_specs, out_specs=out_specs, check_vma=False)
```

```python
import functools

import jax
import jax.numpy as jnp
from jax import lax
from jax.experimental import pallas as pl
from jax.sharding import PartitionSpec as P

DH = 128
BLK = 2
REACH = 7
WIN = 15


guidance_weight = 5.0
masked_score = -1e30


def shifted(value, axis, by):
    count = lax.axis_size(axis)
    return lax.ppermute(value, axis, [(i, (i + by) % count) for i in range(count)])


def from_partner(value, axis, bit):
    return lax.ppermute(value, axis, [(i, i ^ 1 << bit) for i in range(lax.axis_size(axis))])


def group_width(model_width):
    for width in (512, 384, 256):
        if model_width % width == 0:
            return width
    return DH


def spatial_kernel(q_ref, k_ref, v_ref, m_ref, o_ref, lse_ref, *, scale):
    allowed = m_ref[...] > 0
    for head in range(q_ref.shape[-1] // DH):
        lanes = slice(head * DH, (head + 1) * DH)
        scores = (
            lax.dot_general(
                q_ref[:, lanes],
                k_ref[:, lanes],
                (((1,), (1,)), ((), ())),
                preferred_element_type=jnp.float32,
            )
            * scale
        )
        limited = jnp.where(allowed, scores, masked_score)
        maxima = jnp.max(limited, axis=-1, keepdims=True)
        weights = jnp.exp(limited - maxima)
        totals = jnp.sum(weights, axis=-1, keepdims=True)
        result = jnp.dot(
            weights.astype(jnp.bfloat16), v_ref[:, lanes], preferred_element_type=jnp.float32
        )
        o_ref[:, lanes] = result / totals
        lse_ref[:, head : head + 1] = maxima + jnp.log(totals)


def spatial_attention(query_flat, key_value_flat, mask, scale):
    frames, query_count, model_width = query_flat.shape
    key_count = key_value_flat.shape[2]
    head_count = model_width // DH
    width = group_width(model_width)
    groups = model_width // width
    return pl.pallas_call(
        functools.partial(spatial_kernel, scale=scale),
        grid=(frames, groups),
        in_specs=[
            pl.BlockSpec((None, query_count, width), lambda f, g: (f, 0, g)),
            pl.BlockSpec((None, None, key_count, width), lambda f, g: (0, f, 0, g)),
            pl.BlockSpec((None, None, key_count, width), lambda f, g: (1, f, 0, g)),
            pl.BlockSpec((query_count, key_count), lambda f, g: (0, 0)),
        ],
        out_specs=[
            pl.BlockSpec((None, query_count, width), lambda f, g: (f, 0, g)),
            pl.BlockSpec((None, None, query_count, width // DH), lambda f, g: (f, g, 0, 0)),
        ],
        out_shape=[
            jax.ShapeDtypeStruct((frames, query_count, model_width), jnp.float32),
            jax.ShapeDtypeStruct((frames, groups, query_count, width // DH), jnp.float32),
        ],
        cost_estimate=pl.CostEstimate(
            flops=4 * frames * query_count * key_count * model_width,
            transcendentals=frames * head_count * query_count * key_count,
            bytes_accessed=2 * model_width * frames * (query_count + 2 * key_count)
            + 4 * frames * query_count * model_width,
        ),
    )(query_flat, key_value_flat, key_value_flat, mask)


def combine_kernel(*refs):
    *parts, temporal_ref, mixed_ref = refs
    outs, lses = parts[0::2], parts[1::2]
    for head in range(mixed_ref.shape[-1] // DH):
        lanes = slice(head * DH, (head + 1) * DH)
        logs = [lse[:, head : head + 1] for lse in lses]
        top = functools.reduce(jnp.maximum, logs)
        weights = [jnp.exp(log - top) for log in logs]
        total = functools.reduce(jnp.add, weights)
        value = functools.reduce(
            jnp.add,
            [w * o[:, lanes].astype(jnp.float32) for w, o in zip(weights, outs)],
        )
        mixed_ref[:, lanes] = (value / total + temporal_ref[:, lanes].astype(jnp.float32)).astype(
            mixed_ref.dtype
        )


def combine_partials(partials, temporal):
    frames, query_count, model_width = temporal.shape
    width = group_width(model_width)
    groups = model_width // width
    big = pl.BlockSpec((None, query_count, width), lambda f, g: (f, 0, g))
    small = pl.BlockSpec((None, None, query_count, width // DH), lambda f, g: (f, g, 0, 0))
    operands = []
    for out, lse in partials:
        operands += [out, lse]
    return pl.pallas_call(
        combine_kernel,
        grid=(frames, groups),
        in_specs=[big, small] * len(partials) + [big],
        out_specs=big,
        out_shape=jax.ShapeDtypeStruct((frames, query_count, model_width), jnp.bfloat16),
    )(*operands, temporal)


def temporal_attention(own_q, all_k, all_v, valid, own_ids, all_ids, scale):
    q32 = own_q.astype(jnp.float32)
    k32 = all_k.astype(jnp.float32)
    scores = jnp.sum(q32[:, None] * k32[None], axis=-1) * scale
    same = own_ids[:, None] == all_ids[None, :]
    allowed = (valid[None, :, :] > 0) | same[:, :, None]
    limited = jnp.where(allowed[..., None], scores, masked_score)
    maxima = jnp.max(limited, axis=1, keepdims=True)
    weights = jnp.exp(limited - maxima)
    totals = jnp.sum(weights, axis=1)
    rounded = lax.reduce_precision(weights, exponent_bits=8, mantissa_bits=7)
    result = jnp.sum(rounded[..., None] * all_v.astype(jnp.float32)[None], axis=1)
    result = lax.reduce_precision(result / totals[..., None], exponent_bits=8, mantissa_bits=7)
    return result.astype(jnp.bfloat16)


def line_gather(block, axis):
    count = lax.axis_size(axis)
    index = lax.axis_index(axis)
    left, right = {}, {}
    from_left = from_right = block
    for step in range(1, count):
        from_left = lax.ppermute(from_left, axis, [(s, s + 1) for s in range(step - 1, count - 1)])
        from_right = lax.ppermute(
            from_right, axis, [(s, s - 1) for s in range(1, count - step + 1)]
        )
        left[step], right[step] = from_left, from_right
    relative = [block]
    for d in range(1, count):
        relative.append(jnp.where(index + d < count, right[d], left[count - d]))
    return relative


def window_mask(query_cols, key_cols, column_map, total_cols, lat_rows):
    block_count = total_cols // BLK
    slots = (key_cols[None, :] // BLK - query_cols[:, None] // BLK + REACH) % block_count
    picks = slots[:, :, None] == jnp.arange(WIN, dtype=jnp.int32)[None, None, :]
    return jnp.any(picks & (column_map[:, None, :] > 0), axis=-1)


def expand_mask(active, lat_rows):
    query_cols, key_cols = active.shape
    return jnp.broadcast_to(
        active[None, :, None, :].astype(jnp.float32), (lat_rows, query_cols, lat_rows, key_cols)
    ).reshape(lat_rows * query_cols, lat_rows * key_cols)


def flat_keys(blocks):
    joined = jnp.concatenate(blocks, axis=3)
    two, frames, lat_rows, cols, model_width = joined.shape
    return joined.reshape(two, frames, lat_rows * cols, model_width)


def spatial_line_of_four(own_q, key_value, window_map, scale):
    frames, lat_rows, columns, model_width = own_q.shape
    count = 4
    total_cols = count * columns
    index = lax.axis_index("lon")
    is_middle = (index >= 1) & (index <= count - 2)
    column_ids = jnp.arange(columns, dtype=jnp.int32)
    own_map = jnp.repeat(window_map, BLK, axis=0)
    own_cols = index * columns + column_ids
    query_flat = own_q.reshape(frames, lat_rows * columns, model_width)

    from_left = lax.ppermute(key_value, "lon", [(0, 1), (1, 2), (2, 3)])
    from_right = lax.ppermute(key_value, "lon", [(3, 2), (2, 1), (1, 0)])
    guest_map = lax.ppermute(window_map, "lon", [(0, 1), (3, 2)])

    near_cols = ((index - 1) * columns + jnp.arange(3 * columns, dtype=jnp.int32)) % total_cols
    near_valid = jnp.stack([index >= 1, index >= 0, index <= count - 2])
    near_active = window_mask(own_cols, near_cols, own_map, total_cols, lat_rows) & jnp.repeat(
        near_valid, columns
    )[None, :]
    near_part = spatial_attention(
        query_flat,
        flat_keys([from_left, key_value, from_right]),
        expand_mask(near_active, lat_rows),
        scale,
    )

    own_q_pair = jnp.stack([own_q, own_q])
    toward_left = lax.ppermute(
        jnp.where(index == count - 1, own_q_pair, from_right), "lon", [(2, 1), (1, 0), (3, 2)]
    )
    toward_right = lax.ppermute(
        jnp.where(index == 0, own_q_pair, from_left), "lon", [(1, 2), (2, 3), (0, 1)]
    )
    two_away = jnp.where(index <= 1, toward_left, toward_right)
    guest_q = jnp.where(index == 1, toward_right[0], toward_left[0])
    near_part, two_away, guest_q = lax.optimization_barrier((near_part, two_away, guest_q))

    guest_device = jnp.where(index == 1, 0, count - 1)
    far_block = (index + 2) % count
    far_cols = far_block * columns + column_ids
    guest_active = window_mask(
        guest_device * columns + column_ids,
        far_cols,
        jnp.repeat(guest_map, BLK, axis=0),
        total_cols,
        lat_rows,
    ) & is_middle
    far_keys = flat_keys([two_away])
    guest_out, guest_lse = spatial_attention(
        guest_q.reshape(frames, lat_rows * columns, model_width),
        far_keys,
        expand_mask(guest_active, lat_rows),
        scale,
    )
    lse_shape = guest_lse.shape
    returned, returned_lse = lax.ppermute(
        (guest_out.astype(jnp.bfloat16), jnp.swapaxes(guest_lse, 2, 3)),
        "lon",
        [(1, 0), (2, 3)],
    )
    returned_lse = jnp.where(is_middle, masked_score, jnp.swapaxes(returned_lse, 2, 3))
    assert returned_lse.shape == lse_shape

    far_active = window_mask(own_cols, far_cols, own_map, total_cols, lat_rows)
    far_part = spatial_attention(query_flat, far_keys, expand_mask(far_active, lat_rows), scale)
    return [near_part, far_part, (returned, returned_lse)]


def local(queries, keys, values, window_map, frame_valid):
    own_q = queries[0]
    own_k = keys[0]
    own_v = values[0]
    frames, lat_rows, columns, model_width = own_q.shape
    head_count = model_width // DH
    scale = DH ** (-0.5)
    reach_cols = REACH * BLK
    lon_count = lax.axis_size("lon")
    total_cols = lon_count * columns
    ext_count = columns + 2 * reach_cols
    key_value = jnp.stack([own_k, own_v])
    column_ids = jnp.arange(columns, dtype=jnp.int32)
    per_column_map = jnp.repeat(window_map, BLK, axis=0)
    full_ring = ext_count >= total_cols and WIN * BLK <= total_cols
    if full_ring and lon_count == 4:
        partials = spatial_line_of_four(own_q, key_value, window_map, scale)
    else:
        if full_ring:
            extended = jnp.concatenate(line_gather(key_value, "lon"), axis=3)
            key_cols = total_cols
            block_count = total_cols // BLK
            first_col = lax.axis_index("lon") * columns
            query_blocks = (first_col + column_ids) // BLK
            key_blocks = ((first_col + jnp.arange(total_cols, dtype=jnp.int32)) % total_cols) // BLK
            slots = (key_blocks[None, :] - query_blocks[:, None] + REACH) % block_count
        else:
            reach_devices = -(-reach_cols // columns)
            left_parts, right_parts = [], []
            for step_by in range(1, reach_devices + 1):
                need = min(columns, reach_cols - (step_by - 1) * columns)
                left_parts.insert(
                    0, shifted(key_value[:, :, :, columns - need :, :], "lon", step_by)
                )
                right_parts.append(shifted(key_value[:, :, :, :need, :], "lon", -step_by))
            extended = jnp.concatenate(left_parts + [key_value] + right_parts, axis=3)
            key_cols = ext_count
            ext_ids = jnp.arange(ext_count, dtype=jnp.int32)
            slots = ext_ids[None, :] // BLK - column_ids[:, None] // BLK
        picks = slots[:, :, None] == jnp.arange(WIN, dtype=jnp.int32)[None, None, :]
        active = jnp.any(picks & (per_column_map[:, None, :] > 0), axis=-1)
        query_flat = own_q.reshape(frames, lat_rows * columns, model_width)
        key_value_flat = extended.reshape(2, frames, lat_rows * key_cols, model_width)
        partials = [
            spatial_attention(query_flat, key_value_flat, expand_mask(active, lat_rows), scale)
        ]

    token_count = lat_rows * columns
    tm_count = lax.axis_size("tm")
    tm_index = lax.axis_index("tm")
    key_value_rows = key_value.reshape(2, frames, token_count, head_count, DH)
    pieces = [key_value_rows]
    for step_by in range(1, tm_count):
        pieces.append(shifted(key_value_rows, "tm", step_by))
    gathered = jnp.concatenate(pieces, axis=1)
    piece_ids = jnp.arange(tm_count * frames, dtype=jnp.int32)
    frame_ids = ((tm_index - piece_ids // frames) % tm_count) * frames + piece_ids % frames
    valid_tokens = jnp.take(jnp.tile(frame_valid, (1, lat_rows)), frame_ids, axis=0)
    temporal = temporal_attention(
        own_q.reshape(frames, token_count, head_count, DH),
        gathered[0],
        gathered[1],
        valid_tokens,
        frame_ids[:frames],
        frame_ids,
        scale,
    )
    temporal = temporal.reshape(frames, token_count, model_width)
    mixed = combine_partials(partials, temporal).reshape(frames, lat_rows, columns, model_width)
    half_width = model_width // 2
    branch_index = lax.axis_index("branch")
    own_half = lax.dynamic_slice_in_dim(mixed, branch_index * half_width, half_width, 3)
    other_half = lax.dynamic_slice_in_dim(mixed, (1 - branch_index) * half_width, half_width, 3)
    partner = from_partner(other_half, "branch", 0)
    is_conditional = branch_index == 0
    conditional = jnp.where(is_conditional, own_half, partner).astype(jnp.float32)
    unconditional = jnp.where(is_conditional, partner, own_half).astype(jnp.float32)
    return (unconditional + guidance_weight * (conditional - unconditional)).astype(jnp.bfloat16)


def solution(mesh):
    in_specs = (
        P(("groups", "branch"), "tm", None, "lon", None),
        P(("groups", "branch"), "tm", None, "lon", None),
        P(("groups", "branch"), "tm", None, "lon", None),
        P(("groups", "lon"), None),
        P("groups", "lon"),
    )
    out_specs = P(("groups", "tm"), None, "lon", "branch")
    return jax.shard_map(local, mesh=mesh, in_specs=in_specs, out_specs=out_specs, check_vma=False)
```

```python
import functools

import jax
import jax.numpy as jnp
from jax import lax
from jax.experimental import pallas as pl
from jax.sharding import PartitionSpec as P

DH = 128
BLK = 2
REACH = 7
WIN = 15


guidance_weight = 5.0
masked_score = -1e30


def shifted(value, axis, by):
    count = lax.axis_size(axis)
    return lax.ppermute(value, axis, [(i, (i + by) % count) for i in range(count)])


def from_partner(value, axis, bit):
    return lax.ppermute(value, axis, [(i, i ^ 1 << bit) for i in range(lax.axis_size(axis))])


def group_width(model_width):
    for width in (512, 384, 256):
        if model_width % width == 0:
            return width
    return DH


def spatial_kernel(q_ref, k_ref, v_ref, m_ref, o_ref, lse_ref, *, scale):
    allowed = m_ref[...] > 0
    for head in range(q_ref.shape[-1] // DH):
        lanes = slice(head * DH, (head + 1) * DH)
        scores = (
            lax.dot_general(
                q_ref[:, lanes],
                k_ref[:, lanes],
                (((1,), (1,)), ((), ())),
                preferred_element_type=jnp.float32,
            )
            * scale
        )
        limited = jnp.where(allowed, scores, masked_score)
        maxima = jnp.max(limited, axis=-1, keepdims=True)
        weights = jnp.exp(limited - maxima)
        totals = jnp.sum(weights, axis=-1, keepdims=True)
        result = jnp.dot(
            weights.astype(jnp.bfloat16), v_ref[:, lanes], preferred_element_type=jnp.float32
        )
        o_ref[:, lanes] = (result / totals).astype(o_ref.dtype)
        lse_ref[:, head : head + 1] = maxima + jnp.log(totals)


def spatial_attention(query_flat, key_value_flat, mask, scale, out_dtype=jnp.float32):
    frames, query_count, model_width = query_flat.shape
    key_count = key_value_flat.shape[2]
    head_count = model_width // DH
    width = group_width(model_width)
    groups = model_width // width
    return pl.pallas_call(
        functools.partial(spatial_kernel, scale=scale),
        grid=(frames, groups),
        in_specs=[
            pl.BlockSpec((None, query_count, width), lambda f, g: (f, 0, g)),
            pl.BlockSpec((None, None, key_count, width), lambda f, g: (0, f, 0, g)),
            pl.BlockSpec((None, None, key_count, width), lambda f, g: (1, f, 0, g)),
            pl.BlockSpec((query_count, key_count), lambda f, g: (0, 0)),
        ],
        out_specs=[
            pl.BlockSpec((None, query_count, width), lambda f, g: (f, 0, g)),
            pl.BlockSpec((None, None, query_count, width // DH), lambda f, g: (f, g, 0, 0)),
        ],
        out_shape=[
            jax.ShapeDtypeStruct((frames, query_count, model_width), out_dtype),
            jax.ShapeDtypeStruct((frames, groups, query_count, width // DH), jnp.float32),
        ],
        cost_estimate=pl.CostEstimate(
            flops=4 * frames * query_count * key_count * model_width,
            transcendentals=frames * head_count * query_count * key_count,
            bytes_accessed=2 * model_width * frames * (query_count + 2 * key_count)
            + 4 * frames * query_count * model_width,
        ),
    )(query_flat, key_value_flat, key_value_flat, mask)


def combine_kernel(*refs):
    *parts, temporal_ref, mixed_ref = refs
    outs, lses = parts[0::2], parts[1::2]
    for head in range(mixed_ref.shape[-1] // DH):
        lanes = slice(head * DH, (head + 1) * DH)
        logs = [lse[:, head : head + 1] for lse in lses]
        top = functools.reduce(jnp.maximum, logs)
        weights = [jnp.exp(log - top) for log in logs]
        total = functools.reduce(jnp.add, weights)
        value = functools.reduce(
            jnp.add,
            [w * o[:, lanes].astype(jnp.float32) for w, o in zip(weights, outs)],
        )
        mixed_ref[:, lanes] = (value / total + temporal_ref[:, lanes].astype(jnp.float32)).astype(
            mixed_ref.dtype
        )


def combine_partials(partials, temporal):
    frames, query_count, model_width = temporal.shape
    width = group_width(model_width)
    groups = model_width // width
    big = pl.BlockSpec((None, query_count, width), lambda f, g: (f, 0, g))
    small = pl.BlockSpec((None, None, query_count, width // DH), lambda f, g: (f, g, 0, 0))
    operands = []
    for out, lse in partials:
        operands += [out, lse]
    return pl.pallas_call(
        combine_kernel,
        grid=(frames, groups),
        in_specs=[big, small] * len(partials) + [big],
        out_specs=big,
        out_shape=jax.ShapeDtypeStruct((frames, query_count, model_width), jnp.bfloat16),
    )(*operands, temporal)


def temporal_attention(own_q, all_k, all_v, valid, own_ids, all_ids, scale):
    q32 = own_q.astype(jnp.float32)
    k32 = all_k.astype(jnp.float32)
    scores = jnp.sum(q32[:, None] * k32[None], axis=-1) * scale
    same = own_ids[:, None] == all_ids[None, :]
    allowed = (valid[None, :, :] > 0) | same[:, :, None]
    limited = jnp.where(allowed[..., None], scores, masked_score)
    maxima = jnp.max(limited, axis=1, keepdims=True)
    weights = jnp.exp(limited - maxima)
    totals = jnp.sum(weights, axis=1)
    rounded = lax.reduce_precision(weights, exponent_bits=8, mantissa_bits=7)
    result = jnp.sum(rounded[..., None] * all_v.astype(jnp.float32)[None], axis=1)
    result = lax.reduce_precision(result / totals[..., None], exponent_bits=8, mantissa_bits=7)
    return result.astype(jnp.bfloat16)


def line_gather(block, axis):
    count = lax.axis_size(axis)
    index = lax.axis_index(axis)
    left, right = {}, {}
    from_left = from_right = block
    for step in range(1, count):
        from_left = lax.ppermute(from_left, axis, [(s, s + 1) for s in range(step - 1, count - 1)])
        from_right = lax.ppermute(
            from_right, axis, [(s, s - 1) for s in range(1, count - step + 1)]
        )
        left[step], right[step] = from_left, from_right
    relative = [block]
    for d in range(1, count):
        relative.append(jnp.where(index + d < count, right[d], left[count - d]))
    return relative


def window_mask(query_cols, key_cols, column_map, total_cols, lat_rows):
    block_count = total_cols // BLK
    slots = (key_cols[None, :] // BLK - query_cols[:, None] // BLK + REACH) % block_count
    picks = slots[:, :, None] == jnp.arange(WIN, dtype=jnp.int32)[None, None, :]
    return jnp.any(picks & (column_map[:, None, :] > 0), axis=-1)


def expand_mask(active, lat_rows):
    query_cols, key_cols = active.shape
    return jnp.broadcast_to(
        active[None, :, None, :].astype(jnp.float32), (lat_rows, query_cols, lat_rows, key_cols)
    ).reshape(lat_rows * query_cols, lat_rows * key_cols)


def flat_keys(blocks):
    joined = jnp.concatenate(blocks, axis=3)
    two, frames, lat_rows, cols, model_width = joined.shape
    return joined.reshape(two, frames, lat_rows * cols, model_width)


def spatial_line_of_four(own_q, key_value, window_map, scale):
    frames, lat_rows, columns, model_width = own_q.shape
    count = 4
    total_cols = count * columns
    index = lax.axis_index("lon")
    is_middle = (index >= 1) & (index <= count - 2)
    column_ids = jnp.arange(columns, dtype=jnp.int32)
    own_map = jnp.repeat(window_map, BLK, axis=0)
    own_cols = index * columns + column_ids
    query_flat = own_q.reshape(frames, lat_rows * columns, model_width)

    from_left = lax.ppermute(key_value, "lon", [(0, 1), (1, 2), (2, 3)])
    from_right = lax.ppermute(key_value, "lon", [(3, 2), (2, 1), (1, 0)])
    guest_map = lax.ppermute(window_map, "lon", [(0, 1), (3, 2)])

    near_cols = ((index - 1) * columns + jnp.arange(3 * columns, dtype=jnp.int32)) % total_cols
    near_valid = jnp.stack([index >= 1, index >= 0, index <= count - 2])
    near_active = window_mask(own_cols, near_cols, own_map, total_cols, lat_rows) & jnp.repeat(
        near_valid, columns
    )[None, :]
    near_part = spatial_attention(
        query_flat,
        flat_keys([from_left, key_value, from_right]),
        expand_mask(near_active, lat_rows),
        scale,
    )

    two_away = jnp.where(
        index <= 1,
        lax.ppermute(from_right, "lon", [(2, 1), (1, 0)]),
        lax.ppermute(from_left, "lon", [(1, 2), (2, 3)]),
    )
    held_q, _ = lax.optimization_barrier((own_q, from_left))
    guest_q = lax.ppermute(held_q, "lon", [(0, 1), (3, 2)])
    near_part, two_away, guest_q = lax.optimization_barrier((near_part, two_away, guest_q))

    guest_device = jnp.where(index == 1, 0, count - 1)
    far_block = (index + 2) % count
    far_cols = far_block * columns + column_ids
    guest_active = window_mask(
        guest_device * columns + column_ids,
        far_cols,
        jnp.repeat(guest_map, BLK, axis=0),
        total_cols,
        lat_rows,
    ) & is_middle
    far_keys = flat_keys([two_away])
    guest_out, guest_lse = spatial_attention(
        guest_q.reshape(frames, lat_rows * columns, model_width),
        far_keys,
        expand_mask(guest_active, lat_rows),
        scale,
        jnp.bfloat16,
    )
    lse_shape = guest_lse.shape
    returned, returned_lse = lax.ppermute(
        (guest_out, jnp.swapaxes(guest_lse, 2, 3)),
        "lon",
        [(1, 0), (2, 3)],
    )
    returned_lse = jnp.where(is_middle, masked_score, jnp.swapaxes(returned_lse, 2, 3))
    assert returned_lse.shape == lse_shape

    far_active = window_mask(own_cols, far_cols, own_map, total_cols, lat_rows)
    far_part = spatial_attention(query_flat, far_keys, expand_mask(far_active, lat_rows), scale)
    return [near_part, far_part, (returned, returned_lse)]


def local(queries, keys, values, window_map, frame_valid):
    own_q = queries[0]
    own_k = keys[0]
    own_v = values[0]
    frames, lat_rows, columns, model_width = own_q.shape
    head_count = model_width // DH
    scale = DH ** (-0.5)
    reach_cols = REACH * BLK
    lon_count = lax.axis_size("lon")
    total_cols = lon_count * columns
    ext_count = columns + 2 * reach_cols
    key_value = jnp.stack([own_k, own_v])
    column_ids = jnp.arange(columns, dtype=jnp.int32)
    per_column_map = jnp.repeat(window_map, BLK, axis=0)
    full_ring = ext_count >= total_cols and WIN * BLK <= total_cols
    if full_ring and lon_count == 4:
        partials = spatial_line_of_four(own_q, key_value, window_map, scale)
    else:
        if full_ring:
            extended = jnp.concatenate(line_gather(key_value, "lon"), axis=3)
            key_cols = total_cols
            block_count = total_cols // BLK
            first_col = lax.axis_index("lon") * columns
            query_blocks = (first_col + column_ids) // BLK
            key_blocks = ((first_col + jnp.arange(total_cols, dtype=jnp.int32)) % total_cols) // BLK
            slots = (key_blocks[None, :] - query_blocks[:, None] + REACH) % block_count
        else:
            reach_devices = -(-reach_cols // columns)
            left_parts, right_parts = [], []
            for step_by in range(1, reach_devices + 1):
                need = min(columns, reach_cols - (step_by - 1) * columns)
                left_parts.insert(
                    0, shifted(key_value[:, :, :, columns - need :, :], "lon", step_by)
                )
                right_parts.append(shifted(key_value[:, :, :, :need, :], "lon", -step_by))
            extended = jnp.concatenate(left_parts + [key_value] + right_parts, axis=3)
            key_cols = ext_count
            ext_ids = jnp.arange(ext_count, dtype=jnp.int32)
            slots = ext_ids[None, :] // BLK - column_ids[:, None] // BLK
        picks = slots[:, :, None] == jnp.arange(WIN, dtype=jnp.int32)[None, None, :]
        active = jnp.any(picks & (per_column_map[:, None, :] > 0), axis=-1)
        query_flat = own_q.reshape(frames, lat_rows * columns, model_width)
        key_value_flat = extended.reshape(2, frames, lat_rows * key_cols, model_width)
        partials = [
            spatial_attention(query_flat, key_value_flat, expand_mask(active, lat_rows), scale)
        ]

    token_count = lat_rows * columns
    tm_count = lax.axis_size("tm")
    tm_index = lax.axis_index("tm")
    key_value_rows = key_value.reshape(2, frames, token_count, head_count, DH)
    pieces = [key_value_rows]
    for step_by in range(1, tm_count):
        pieces.append(shifted(key_value_rows, "tm", step_by))
    gathered = jnp.concatenate(pieces, axis=1)
    piece_ids = jnp.arange(tm_count * frames, dtype=jnp.int32)
    frame_ids = ((tm_index - piece_ids // frames) % tm_count) * frames + piece_ids % frames
    valid_tokens = jnp.take(jnp.tile(frame_valid, (1, lat_rows)), frame_ids, axis=0)
    temporal = temporal_attention(
        own_q.reshape(frames, token_count, head_count, DH),
        gathered[0],
        gathered[1],
        valid_tokens,
        frame_ids[:frames],
        frame_ids,
        scale,
    )
    temporal = temporal.reshape(frames, token_count, model_width)
    mixed = combine_partials(partials, temporal).reshape(frames, lat_rows, columns, model_width)
    half_width = model_width // 2
    branch_index = lax.axis_index("branch")
    own_half = lax.dynamic_slice_in_dim(mixed, branch_index * half_width, half_width, 3)
    other_half = lax.dynamic_slice_in_dim(mixed, (1 - branch_index) * half_width, half_width, 3)
    partner = from_partner(other_half, "branch", 0)
    is_conditional = branch_index == 0
    conditional = jnp.where(is_conditional, own_half, partner).astype(jnp.float32)
    unconditional = jnp.where(is_conditional, partner, own_half).astype(jnp.float32)
    return (unconditional + guidance_weight * (conditional - unconditional)).astype(jnp.bfloat16)


def solution(mesh):
    in_specs = (
        P(("groups", "branch"), "tm", None, "lon", None),
        P(("groups", "branch"), "tm", None, "lon", None),
        P(("groups", "branch"), "tm", None, "lon", None),
        P(("groups", "lon"), None),
        P("groups", "lon"),
    )
    out_specs = P(("groups", "tm"), None, "lon", "branch")
    return jax.shard_map(local, mesh=mesh, in_specs=in_specs, out_specs=out_specs, check_vma=False)
```

```python
import functools

import jax
import jax.numpy as jnp
from jax import lax
from jax.experimental import pallas as pl
from jax.sharding import PartitionSpec as P

DH = 128
BLK = 2
REACH = 7
WIN = 15


guidance_weight = 5.0
masked_score = -1e30


def shifted(value, axis, by):
    count = lax.axis_size(axis)
    return lax.ppermute(value, axis, [(i, (i + by) % count) for i in range(count)])


def from_partner(value, axis, bit):
    return lax.ppermute(value, axis, [(i, i ^ 1 << bit) for i in range(lax.axis_size(axis))])


def group_width(model_width):
    for width in (512, 384, 256):
        if model_width % width == 0:
            return width
    return DH


def spatial_kernel(q_ref, k_ref, v_ref, m_ref, o_ref, lse_ref, *, scale):
    allowed = m_ref[...] > 0
    for head in range(q_ref.shape[-1] // DH):
        lanes = slice(head * DH, (head + 1) * DH)
        scores = (
            lax.dot_general(
                q_ref[:, lanes],
                k_ref[:, lanes],
                (((1,), (1,)), ((), ())),
                preferred_element_type=jnp.float32,
            )
            * scale
        )
        limited = jnp.where(allowed, scores, masked_score)
        maxima = jnp.max(limited, axis=-1, keepdims=True)
        weights = jnp.exp(limited - maxima)
        totals = jnp.sum(weights, axis=-1, keepdims=True)
        result = jnp.dot(
            weights.astype(jnp.bfloat16), v_ref[:, lanes], preferred_element_type=jnp.float32
        )
        o_ref[:, lanes] = (result / totals).astype(o_ref.dtype)
        lse_ref[:, head : head + 1] = maxima + jnp.log(totals)


def spatial_attention(query_flat, key_value_flat, mask, scale, out_dtype=jnp.float32):
    frames, query_count, model_width = query_flat.shape
    key_count = key_value_flat.shape[2]
    head_count = model_width // DH
    width = group_width(model_width)
    groups = model_width // width
    return pl.pallas_call(
        functools.partial(spatial_kernel, scale=scale),
        grid=(frames, groups),
        in_specs=[
            pl.BlockSpec((None, query_count, width), lambda f, g: (f, 0, g)),
            pl.BlockSpec((None, None, key_count, width), lambda f, g: (0, f, 0, g)),
            pl.BlockSpec((None, None, key_count, width), lambda f, g: (1, f, 0, g)),
            pl.BlockSpec((query_count, key_count), lambda f, g: (0, 0)),
        ],
        out_specs=[
            pl.BlockSpec((None, query_count, width), lambda f, g: (f, 0, g)),
            pl.BlockSpec((None, None, query_count, width // DH), lambda f, g: (f, g, 0, 0)),
        ],
        out_shape=[
            jax.ShapeDtypeStruct((frames, query_count, model_width), out_dtype),
            jax.ShapeDtypeStruct((frames, groups, query_count, width // DH), jnp.float32),
        ],
        cost_estimate=pl.CostEstimate(
            flops=4 * frames * query_count * key_count * model_width,
            transcendentals=frames * head_count * query_count * key_count,
            bytes_accessed=2 * model_width * frames * (query_count + 2 * key_count)
            + 4 * frames * query_count * model_width,
        ),
    )(query_flat, key_value_flat, key_value_flat, mask)


def combine_kernel(*refs):
    *parts, temporal_ref, mixed_ref = refs
    outs, lses = parts[0::2], parts[1::2]
    for head in range(mixed_ref.shape[-1] // DH):
        lanes = slice(head * DH, (head + 1) * DH)
        logs = [lse[:, head : head + 1] for lse in lses]
        top = functools.reduce(jnp.maximum, logs)
        weights = [jnp.exp(log - top) for log in logs]
        total = functools.reduce(jnp.add, weights)
        value = functools.reduce(
            jnp.add,
            [w * o[:, lanes].astype(jnp.float32) for w, o in zip(weights, outs)],
        )
        mixed_ref[:, lanes] = (value / total + temporal_ref[:, lanes].astype(jnp.float32)).astype(
            mixed_ref.dtype
        )


def combine_partials(partials, temporal):
    frames, query_count, model_width = temporal.shape
    width = group_width(model_width)
    groups = model_width // width
    big = pl.BlockSpec((None, query_count, width), lambda f, g: (f, 0, g))
    small = pl.BlockSpec((None, None, query_count, width // DH), lambda f, g: (f, g, 0, 0))
    operands = []
    for out, lse in partials:
        operands += [out, lse]
    return pl.pallas_call(
        combine_kernel,
        grid=(frames, groups),
        in_specs=[big, small] * len(partials) + [big],
        out_specs=big,
        out_shape=jax.ShapeDtypeStruct((frames, query_count, model_width), jnp.bfloat16),
    )(*operands, temporal)


def temporal_attention(own_q, all_k, all_v, valid, own_ids, all_ids, scale):
    q32 = own_q.astype(jnp.float32)
    k32 = all_k.astype(jnp.float32)
    scores = jnp.sum(q32[:, None] * k32[None], axis=-1) * scale
    same = own_ids[:, None] == all_ids[None, :]
    allowed = (valid[None, :, :] > 0) | same[:, :, None]
    limited = jnp.where(allowed[..., None], scores, masked_score)
    maxima = jnp.max(limited, axis=1, keepdims=True)
    weights = jnp.exp(limited - maxima)
    totals = jnp.sum(weights, axis=1)
    rounded = lax.reduce_precision(weights, exponent_bits=8, mantissa_bits=7)
    result = jnp.sum(rounded[..., None] * all_v.astype(jnp.float32)[None], axis=1)
    result = lax.reduce_precision(result / totals[..., None], exponent_bits=8, mantissa_bits=7)
    return result.astype(jnp.bfloat16)


def line_gather(block, axis):
    count = lax.axis_size(axis)
    index = lax.axis_index(axis)
    left, right = {}, {}
    from_left = from_right = block
    for step in range(1, count):
        from_left = lax.ppermute(from_left, axis, [(s, s + 1) for s in range(step - 1, count - 1)])
        from_right = lax.ppermute(
            from_right, axis, [(s, s - 1) for s in range(1, count - step + 1)]
        )
        left[step], right[step] = from_left, from_right
    relative = [block]
    for d in range(1, count):
        relative.append(jnp.where(index + d < count, right[d], left[count - d]))
    return relative


def window_mask(query_cols, key_cols, column_map, total_cols, lat_rows):
    block_count = total_cols // BLK
    slots = (key_cols[None, :] // BLK - query_cols[:, None] // BLK + REACH) % block_count
    picks = slots[:, :, None] == jnp.arange(WIN, dtype=jnp.int32)[None, None, :]
    return jnp.any(picks & (column_map[:, None, :] > 0), axis=-1)


def expand_mask(active, lat_rows):
    query_cols, key_cols = active.shape
    return jnp.broadcast_to(
        active[None, :, None, :].astype(jnp.float32), (lat_rows, query_cols, lat_rows, key_cols)
    ).reshape(lat_rows * query_cols, lat_rows * key_cols)


def flat_keys(blocks):
    joined = jnp.concatenate(blocks, axis=3)
    two, frames, lat_rows, cols, model_width = joined.shape
    return joined.reshape(two, frames, lat_rows * cols, model_width)


def spatial_line_of_four(own_q, key_value, window_map, scale):
    frames, lat_rows, columns, model_width = own_q.shape
    count = 4
    total_cols = count * columns
    index = lax.axis_index("lon")
    is_middle = (index >= 1) & (index <= count - 2)
    column_ids = jnp.arange(columns, dtype=jnp.int32)
    own_map = jnp.repeat(window_map, BLK, axis=0)
    own_cols = index * columns + column_ids
    query_flat = own_q.reshape(frames, lat_rows * columns, model_width)

    from_left = lax.ppermute(key_value, "lon", [(0, 1), (1, 2), (2, 3)])
    from_right = lax.ppermute(key_value, "lon", [(3, 2), (2, 1), (1, 0)])
    guest_map = lax.ppermute(window_map, "lon", [(0, 1), (3, 2)])

    near_cols = ((index - 1) * columns + jnp.arange(3 * columns, dtype=jnp.int32)) % total_cols
    near_valid = jnp.stack([index >= 1, index >= 0, index <= count - 2])
    near_active = window_mask(own_cols, near_cols, own_map, total_cols, lat_rows) & jnp.repeat(
        near_valid, columns
    )[None, :]
    near_part = spatial_attention(
        query_flat,
        flat_keys([from_left, key_value, from_right]),
        expand_mask(near_active, lat_rows),
        scale,
    )

    two_away = jnp.where(
        index <= 1,
        lax.ppermute(from_right, "lon", [(2, 1), (1, 0)]),
        lax.ppermute(from_left, "lon", [(1, 2), (2, 3)]),
    )
    held_q, _ = lax.optimization_barrier((own_q, from_left))
    guest_q = lax.ppermute(held_q, "lon", [(0, 1), (3, 2)])
    near_part, two_away, guest_q = lax.optimization_barrier((near_part, two_away, guest_q))

    guest_device = jnp.where(index == 1, 0, count - 1)
    far_block = (index + 2) % count
    far_cols = far_block * columns + column_ids
    guest_active = window_mask(
        guest_device * columns + column_ids,
        far_cols,
        jnp.repeat(guest_map, BLK, axis=0),
        total_cols,
        lat_rows,
    ) & is_middle
    far_keys = flat_keys([two_away])
    def attend_guest(operands):
        return tuple(spatial_attention(*operands, scale, jnp.bfloat16))

    guest_operands = (
        guest_q.reshape(frames, lat_rows * columns, model_width),
        far_keys,
        expand_mask(guest_active, lat_rows),
    )
    shapes = jax.eval_shape(attend_guest, guest_operands)
    guest_out, guest_lse = lax.cond(
        is_middle,
        attend_guest,
        lambda operands: tuple(jnp.zeros(shape.shape, shape.dtype) for shape in shapes),
        guest_operands,
    )
    lse_shape = guest_lse.shape
    returned, returned_lse = lax.ppermute(
        (guest_out, jnp.swapaxes(guest_lse, 2, 3)),
        "lon",
        [(1, 0), (2, 3)],
    )
    returned_lse = jnp.where(is_middle, masked_score, jnp.swapaxes(returned_lse, 2, 3))
    assert returned_lse.shape == lse_shape

    far_active = window_mask(own_cols, far_cols, own_map, total_cols, lat_rows)
    far_part = spatial_attention(query_flat, far_keys, expand_mask(far_active, lat_rows), scale)
    return [near_part, far_part, (returned, returned_lse)]


def local(queries, keys, values, window_map, frame_valid):
    own_q = queries[0]
    own_k = keys[0]
    own_v = values[0]
    frames, lat_rows, columns, model_width = own_q.shape
    head_count = model_width // DH
    scale = DH ** (-0.5)
    reach_cols = REACH * BLK
    lon_count = lax.axis_size("lon")
    total_cols = lon_count * columns
    ext_count = columns + 2 * reach_cols
    key_value = jnp.stack([own_k, own_v])
    column_ids = jnp.arange(columns, dtype=jnp.int32)
    per_column_map = jnp.repeat(window_map, BLK, axis=0)
    full_ring = ext_count >= total_cols and WIN * BLK <= total_cols
    if full_ring and lon_count == 4:
        partials = spatial_line_of_four(own_q, key_value, window_map, scale)
    else:
        if full_ring:
            extended = jnp.concatenate(line_gather(key_value, "lon"), axis=3)
            key_cols = total_cols
            block_count = total_cols // BLK
            first_col = lax.axis_index("lon") * columns
            query_blocks = (first_col + column_ids) // BLK
            key_blocks = ((first_col + jnp.arange(total_cols, dtype=jnp.int32)) % total_cols) // BLK
            slots = (key_blocks[None, :] - query_blocks[:, None] + REACH) % block_count
        else:
            reach_devices = -(-reach_cols // columns)
            left_parts, right_parts = [], []
            for step_by in range(1, reach_devices + 1):
                need = min(columns, reach_cols - (step_by - 1) * columns)
                left_parts.insert(
                    0, shifted(key_value[:, :, :, columns - need :, :], "lon", step_by)
                )
                right_parts.append(shifted(key_value[:, :, :, :need, :], "lon", -step_by))
            extended = jnp.concatenate(left_parts + [key_value] + right_parts, axis=3)
            key_cols = ext_count
            ext_ids = jnp.arange(ext_count, dtype=jnp.int32)
            slots = ext_ids[None, :] // BLK - column_ids[:, None] // BLK
        picks = slots[:, :, None] == jnp.arange(WIN, dtype=jnp.int32)[None, None, :]
        active = jnp.any(picks & (per_column_map[:, None, :] > 0), axis=-1)
        query_flat = own_q.reshape(frames, lat_rows * columns, model_width)
        key_value_flat = extended.reshape(2, frames, lat_rows * key_cols, model_width)
        partials = [
            spatial_attention(query_flat, key_value_flat, expand_mask(active, lat_rows), scale)
        ]

    token_count = lat_rows * columns
    tm_count = lax.axis_size("tm")
    tm_index = lax.axis_index("tm")
    key_value_rows = key_value.reshape(2, frames, token_count, head_count, DH)
    pieces = [key_value_rows]
    for step_by in range(1, tm_count):
        pieces.append(shifted(key_value_rows, "tm", step_by))
    gathered = jnp.concatenate(pieces, axis=1)
    piece_ids = jnp.arange(tm_count * frames, dtype=jnp.int32)
    frame_ids = ((tm_index - piece_ids // frames) % tm_count) * frames + piece_ids % frames
    valid_tokens = jnp.take(jnp.tile(frame_valid, (1, lat_rows)), frame_ids, axis=0)
    temporal = temporal_attention(
        own_q.reshape(frames, token_count, head_count, DH),
        gathered[0],
        gathered[1],
        valid_tokens,
        frame_ids[:frames],
        frame_ids,
        scale,
    )
    temporal = temporal.reshape(frames, token_count, model_width)
    mixed = combine_partials(partials, temporal).reshape(frames, lat_rows, columns, model_width)
    half_width = model_width // 2
    branch_index = lax.axis_index("branch")
    own_half = lax.dynamic_slice_in_dim(mixed, branch_index * half_width, half_width, 3)
    other_half = lax.dynamic_slice_in_dim(mixed, (1 - branch_index) * half_width, half_width, 3)
    partner = from_partner(other_half, "branch", 0)
    is_conditional = branch_index == 0
    conditional = jnp.where(is_conditional, own_half, partner).astype(jnp.float32)
    unconditional = jnp.where(is_conditional, partner, own_half).astype(jnp.float32)
    return (unconditional + guidance_weight * (conditional - unconditional)).astype(jnp.bfloat16)


def solution(mesh):
    in_specs = (
        P(("groups", "branch"), "tm", None, "lon", None),
        P(("groups", "branch"), "tm", None, "lon", None),
        P(("groups", "branch"), "tm", None, "lon", None),
        P(("groups", "lon"), None),
        P("groups", "lon"),
    )
    out_specs = P(("groups", "tm"), None, "lon", "branch")
    return jax.shard_map(local, mesh=mesh, in_specs=in_specs, out_specs=out_specs, check_vma=False)
```

```python
import functools

import jax
import jax.numpy as jnp
from jax import lax
from jax.experimental import pallas as pl
from jax.sharding import PartitionSpec as P

DH = 128
BLK = 2
REACH = 7
WIN = 15


guidance_weight = 5.0
masked_score = -1e30


def shifted(value, axis, by):
    count = lax.axis_size(axis)
    return lax.ppermute(value, axis, [(i, (i + by) % count) for i in range(count)])


def from_partner(value, axis, bit):
    return lax.ppermute(value, axis, [(i, i ^ 1 << bit) for i in range(lax.axis_size(axis))])


def group_width(model_width):
    for width in (512, 384, 256):
        if model_width % width == 0:
            return width
    return DH


def spatial_kernel(q_ref, k_ref, v_ref, m_ref, o_ref, lse_ref, *, scale):
    allowed = m_ref[...] > 0
    for head in range(q_ref.shape[-1] // DH):
        lanes = slice(head * DH, (head + 1) * DH)
        scores = (
            lax.dot_general(
                q_ref[:, lanes],
                k_ref[:, lanes],
                (((1,), (1,)), ((), ())),
                preferred_element_type=jnp.float32,
            )
            * scale
        )
        limited = jnp.where(allowed, scores, masked_score)
        maxima = jnp.max(limited, axis=-1, keepdims=True)
        weights = jnp.exp(limited - maxima)
        totals = jnp.sum(weights, axis=-1, keepdims=True)
        result = jnp.dot(
            weights.astype(jnp.bfloat16), v_ref[:, lanes], preferred_element_type=jnp.float32
        )
        o_ref[:, lanes] = (result / totals).astype(o_ref.dtype)
        lse_ref[:, head : head + 1] = maxima + jnp.log(totals)


def spatial_attention(
    query_flat, key_value_flat, mask, scale, out_dtype=jnp.float32, query_first=0, count=None
):
    frames, query_count, model_width = query_flat.shape
    key_count = key_value_flat.shape[2]
    width = group_width(model_width)
    if count is None:
        count = key_value_flat.shape[3] // width
    used = count * width
    return pl.pallas_call(
        functools.partial(spatial_kernel, scale=scale),
        grid=(frames, count),
        in_specs=[
            pl.BlockSpec((None, query_count, width), lambda f, g: (f, 0, g + query_first)),
            pl.BlockSpec((None, None, key_count, width), lambda f, g: (0, f, 0, g)),
            pl.BlockSpec((None, None, key_count, width), lambda f, g: (1, f, 0, g)),
            pl.BlockSpec((query_count, key_count), lambda f, g: (0, 0)),
        ],
        out_specs=[
            pl.BlockSpec((None, query_count, width), lambda f, g: (f, 0, g)),
            pl.BlockSpec((None, None, query_count, width // DH), lambda f, g: (f, g, 0, 0)),
        ],
        out_shape=[
            jax.ShapeDtypeStruct((frames, query_count, used), out_dtype),
            jax.ShapeDtypeStruct((frames, count, query_count, width // DH), jnp.float32),
        ],
        cost_estimate=pl.CostEstimate(
            flops=4 * frames * query_count * key_count * used,
            transcendentals=frames * (used // DH) * query_count * key_count,
            bytes_accessed=2 * used * frames * (query_count + 2 * key_count)
            + 4 * frames * query_count * used,
        ),
    )(query_flat, key_value_flat, key_value_flat, mask)


def combine_kernel(*refs):
    *parts, temporal_ref, mixed_ref = refs
    outs, lses = parts[0::2], parts[1::2]
    for head in range(mixed_ref.shape[-1] // DH):
        lanes = slice(head * DH, (head + 1) * DH)
        logs = [lse[:, head : head + 1] for lse in lses]
        top = functools.reduce(jnp.maximum, logs)
        weights = [jnp.exp(log - top) for log in logs]
        total = functools.reduce(jnp.add, weights)
        value = functools.reduce(
            jnp.add,
            [w * o[:, lanes].astype(jnp.float32) for w, o in zip(weights, outs)],
        )
        mixed_ref[:, lanes] = (value / total + temporal_ref[:, lanes].astype(jnp.float32)).astype(
            mixed_ref.dtype
        )


def combine_partials(partials, temporal, first=0, count=None):
    frames, query_count, model_width = temporal.shape
    width = group_width(model_width)
    if count is None:
        count = model_width // width
    heads = width // DH
    whole_big = pl.BlockSpec((None, query_count, width), lambda f, g: (f, 0, g + first))
    whole_small = pl.BlockSpec((None, None, query_count, heads), lambda f, g: (f, g + first, 0, 0))
    part_big = pl.BlockSpec((None, query_count, width), lambda f, g: (f, 0, g))
    part_small = pl.BlockSpec((None, None, query_count, heads), lambda f, g: (f, g, 0, 0))
    in_specs, operands = [], []
    for partial in partials:
        whole = len(partial) == 2
        in_specs += [whole_big, whole_small] if whole else [part_big, part_small]
        operands += list(partial[:2])
    return pl.pallas_call(
        combine_kernel,
        grid=(frames, count),
        in_specs=in_specs + [whole_big],
        out_specs=part_big,
        out_shape=jax.ShapeDtypeStruct((frames, query_count, count * width), jnp.bfloat16),
    )(*operands, temporal)


def temporal_attention(own_q, all_k, all_v, valid, own_ids, all_ids, scale):
    q32 = own_q.astype(jnp.float32)
    k32 = all_k.astype(jnp.float32)
    scores = jnp.sum(q32[:, None] * k32[None], axis=-1) * scale
    same = own_ids[:, None] == all_ids[None, :]
    allowed = (valid[None, :, :] > 0) | same[:, :, None]
    limited = jnp.where(allowed[..., None], scores, masked_score)
    maxima = jnp.max(limited, axis=1, keepdims=True)
    weights = jnp.exp(limited - maxima)
    totals = jnp.sum(weights, axis=1)
    rounded = lax.reduce_precision(weights, exponent_bits=8, mantissa_bits=7)
    result = jnp.sum(rounded[..., None] * all_v.astype(jnp.float32)[None], axis=1)
    result = lax.reduce_precision(result / totals[..., None], exponent_bits=8, mantissa_bits=7)
    return result.astype(jnp.bfloat16)


def line_gather(block, axis):
    count = lax.axis_size(axis)
    index = lax.axis_index(axis)
    left, right = {}, {}
    from_left = from_right = block
    for step in range(1, count):
        from_left = lax.ppermute(from_left, axis, [(s, s + 1) for s in range(step - 1, count - 1)])
        from_right = lax.ppermute(
            from_right, axis, [(s, s - 1) for s in range(1, count - step + 1)]
        )
        left[step], right[step] = from_left, from_right
    relative = [block]
    for d in range(1, count):
        relative.append(jnp.where(index + d < count, right[d], left[count - d]))
    return relative


def window_mask(query_cols, key_cols, column_map, total_cols, lat_rows):
    block_count = total_cols // BLK
    slots = (key_cols[None, :] // BLK - query_cols[:, None] // BLK + REACH) % block_count
    picks = slots[:, :, None] == jnp.arange(WIN, dtype=jnp.int32)[None, None, :]
    return jnp.any(picks & (column_map[:, None, :] > 0), axis=-1)


def expand_mask(active, lat_rows):
    query_cols, key_cols = active.shape
    return jnp.broadcast_to(
        active[None, :, None, :].astype(jnp.float32), (lat_rows, query_cols, lat_rows, key_cols)
    ).reshape(lat_rows * query_cols, lat_rows * key_cols)


def flat_keys(blocks):
    joined = jnp.concatenate(blocks, axis=3)
    two, frames, lat_rows, cols, model_width = joined.shape
    return joined.reshape(two, frames, lat_rows * cols, model_width)


def spatial_line_of_four(own_q, key_value, window_map, temporal, scale):
    frames, lat_rows, columns, model_width = own_q.shape
    count = 4
    total_cols = count * columns
    index = lax.axis_index("lon")
    is_middle = (index >= 1) & (index <= count - 2)
    column_ids = jnp.arange(columns, dtype=jnp.int32)
    own_map = jnp.repeat(window_map, BLK, axis=0)
    own_cols = index * columns + column_ids
    query_flat = own_q.reshape(frames, lat_rows * columns, model_width)

    from_left = lax.ppermute(key_value, "lon", [(0, 1), (1, 2), (2, 3)])
    from_right = lax.ppermute(key_value, "lon", [(3, 2), (2, 1), (1, 0)])
    guest_map = lax.ppermute(window_map, "lon", [(0, 1), (3, 2)])

    near_cols = ((index - 1) * columns + jnp.arange(3 * columns, dtype=jnp.int32)) % total_cols
    near_valid = jnp.stack([index >= 1, index >= 0, index <= count - 2])
    near_active = window_mask(own_cols, near_cols, own_map, total_cols, lat_rows) & jnp.repeat(
        near_valid, columns
    )[None, :]
    near_part = spatial_attention(
        query_flat,
        flat_keys([from_left, key_value, from_right]),
        expand_mask(near_active, lat_rows),
        scale,
    )

    held_q, _ = lax.optimization_barrier((own_q, from_left))
    guest_q = lax.ppermute(held_q, "lon", [(0, 1), (3, 2)])
    guest_device = jnp.where(index == 1, 0, count - 1)
    far_block = (index + 2) % count
    far_cols = far_block * columns + column_ids
    guest_mask = expand_mask(
        window_mask(
            guest_device * columns + column_ids,
            far_cols,
            jnp.repeat(guest_map, BLK, axis=0),
            total_cols,
            lat_rows,
        )
        & is_middle,
        lat_rows,
    )
    far_mask = expand_mask(window_mask(own_cols, far_cols, own_map, total_cols, lat_rows), lat_rows)
    guest_flat = guest_q.reshape(frames, lat_rows * columns, model_width)

    width = group_width(model_width)
    groups = model_width // width
    chunks = [(0, groups - 1), (groups - 1, 1)] if groups > 1 else [(0, groups)]
    mixed, landed = [], None
    for first, size in chunks:
        lanes = slice(first * width, (first + size) * width)
        chunk_left, chunk_right = from_left[..., lanes], from_right[..., lanes]
        if landed is not None:
            chunk_left, chunk_right, _ = lax.optimization_barrier((chunk_left, chunk_right, landed))
        toward_left = lax.ppermute(chunk_right, "lon", [(2, 1), (1, 0)])
        toward_right = lax.ppermute(chunk_left, "lon", [(1, 2), (2, 3)])
        landed = (toward_left, toward_right)
        if first == 0:
            near_part, toward_left, toward_right, guest_flat = lax.optimization_barrier(
                (near_part, toward_left, toward_right, guest_flat)
            )
        far_keys = flat_keys([jnp.where(index <= 1, toward_left, toward_right)])
        guest_out, guest_lse = spatial_attention(
            guest_flat, far_keys, guest_mask, scale, jnp.bfloat16, first, size
        )
        returned, returned_lse = lax.ppermute(
            (guest_out, jnp.swapaxes(guest_lse, 2, 3)), "lon", [(1, 0), (2, 3)]
        )
        returned_lse = jnp.where(is_middle, masked_score, jnp.swapaxes(returned_lse, 2, 3))
        far_part = spatial_attention(query_flat, far_keys, far_mask, scale, jnp.float32, first, size)
        mixed.append(
            combine_partials(
                [near_part, far_part + (False,), (returned, returned_lse, False)],
                temporal,
                first,
                size,
            )
        )
    return jnp.concatenate(mixed, axis=2)


def local(queries, keys, values, window_map, frame_valid):
    own_q = queries[0]
    own_k = keys[0]
    own_v = values[0]
    frames, lat_rows, columns, model_width = own_q.shape
    head_count = model_width // DH
    scale = DH ** (-0.5)
    reach_cols = REACH * BLK
    lon_count = lax.axis_size("lon")
    total_cols = lon_count * columns
    ext_count = columns + 2 * reach_cols
    key_value = jnp.stack([own_k, own_v])
    column_ids = jnp.arange(columns, dtype=jnp.int32)
    per_column_map = jnp.repeat(window_map, BLK, axis=0)
    token_count = lat_rows * columns
    tm_count = lax.axis_size("tm")
    tm_index = lax.axis_index("tm")
    key_value_rows = key_value.reshape(2, frames, token_count, head_count, DH)
    pieces = [key_value_rows]
    for step_by in range(1, tm_count):
        pieces.append(shifted(key_value_rows, "tm", step_by))
    gathered = jnp.concatenate(pieces, axis=1)
    piece_ids = jnp.arange(tm_count * frames, dtype=jnp.int32)
    frame_ids = ((tm_index - piece_ids // frames) % tm_count) * frames + piece_ids % frames
    valid_tokens = jnp.take(jnp.tile(frame_valid, (1, lat_rows)), frame_ids, axis=0)
    temporal = temporal_attention(
        own_q.reshape(frames, token_count, head_count, DH),
        gathered[0],
        gathered[1],
        valid_tokens,
        frame_ids[:frames],
        frame_ids,
        scale,
    )
    temporal = temporal.reshape(frames, token_count, model_width)
    full_ring = ext_count >= total_cols and WIN * BLK <= total_cols
    if not (full_ring and lon_count == 4):
        if full_ring:
            extended = jnp.concatenate(line_gather(key_value, "lon"), axis=3)
            key_cols = total_cols
            block_count = total_cols // BLK
            first_col = lax.axis_index("lon") * columns
            query_blocks = (first_col + column_ids) // BLK
            key_blocks = ((first_col + jnp.arange(total_cols, dtype=jnp.int32)) % total_cols) // BLK
            slots = (key_blocks[None, :] - query_blocks[:, None] + REACH) % block_count
        else:
            reach_devices = -(-reach_cols // columns)
            left_parts, right_parts = [], []
            for step_by in range(1, reach_devices + 1):
                need = min(columns, reach_cols - (step_by - 1) * columns)
                left_parts.insert(
                    0, shifted(key_value[:, :, :, columns - need :, :], "lon", step_by)
                )
                right_parts.append(shifted(key_value[:, :, :, :need, :], "lon", -step_by))
            extended = jnp.concatenate(left_parts + [key_value] + right_parts, axis=3)
            key_cols = ext_count
            ext_ids = jnp.arange(ext_count, dtype=jnp.int32)
            slots = ext_ids[None, :] // BLK - column_ids[:, None] // BLK
        picks = slots[:, :, None] == jnp.arange(WIN, dtype=jnp.int32)[None, None, :]
        active = jnp.any(picks & (per_column_map[:, None, :] > 0), axis=-1)
        query_flat = own_q.reshape(frames, lat_rows * columns, model_width)
        key_value_flat = extended.reshape(2, frames, lat_rows * key_cols, model_width)
        partials = [
            spatial_attention(query_flat, key_value_flat, expand_mask(active, lat_rows), scale)
        ]

    if full_ring and lon_count == 4:
        mixed = spatial_line_of_four(own_q, key_value, window_map, temporal, scale)
    else:
        mixed = combine_partials(partials, temporal)
    mixed = mixed.reshape(frames, lat_rows, columns, model_width)
    half_width = model_width // 2
    branch_index = lax.axis_index("branch")
    own_half = lax.dynamic_slice_in_dim(mixed, branch_index * half_width, half_width, 3)
    other_half = lax.dynamic_slice_in_dim(mixed, (1 - branch_index) * half_width, half_width, 3)
    partner = from_partner(other_half, "branch", 0)
    is_conditional = branch_index == 0
    conditional = jnp.where(is_conditional, own_half, partner).astype(jnp.float32)
    unconditional = jnp.where(is_conditional, partner, own_half).astype(jnp.float32)
    return (unconditional + guidance_weight * (conditional - unconditional)).astype(jnp.bfloat16)


def solution(mesh):
    in_specs = (
        P(("groups", "branch"), "tm", None, "lon", None),
        P(("groups", "branch"), "tm", None, "lon", None),
        P(("groups", "branch"), "tm", None, "lon", None),
        P(("groups", "lon"), None),
        P("groups", "lon"),
    )
    out_specs = P(("groups", "tm"), None, "lon", "branch")
    return jax.shard_map(local, mesh=mesh, in_specs=in_specs, out_specs=out_specs, check_vma=False)
```

```python
import functools

import jax
import jax.numpy as jnp
from jax import lax
from jax.experimental import pallas as pl
from jax.sharding import PartitionSpec as P

DH = 128
BLK = 2
REACH = 7
WIN = 15


guidance_weight = 5.0
masked_score = -1e30


def shifted(value, axis, by):
    count = lax.axis_size(axis)
    return lax.ppermute(value, axis, [(i, (i + by) % count) for i in range(count)])


def from_partner(value, axis, bit):
    return lax.ppermute(value, axis, [(i, i ^ 1 << bit) for i in range(lax.axis_size(axis))])


def group_width(model_width):
    for width in (512, 384, 256):
        if model_width % width == 0:
            return width
    return DH


def spatial_kernel(q_ref, k_ref, v_ref, *refs, scale):
    if len(refs) == 5:
        k2_ref, v2_ref, m_ref, o_ref, lse_ref = refs
        read_k = lambda lanes: k_ref[:, lanes] + k2_ref[:, lanes]
        read_v = lambda lanes: v_ref[:, lanes] + v2_ref[:, lanes]
    else:
        m_ref, o_ref, lse_ref = refs
        read_k = lambda lanes: k_ref[:, lanes]
        read_v = lambda lanes: v_ref[:, lanes]
    allowed = m_ref[...] > 0
    for head in range(q_ref.shape[-1] // DH):
        lanes = slice(head * DH, (head + 1) * DH)
        scores = (
            lax.dot_general(
                q_ref[:, lanes],
                read_k(lanes),
                (((1,), (1,)), ((), ())),
                preferred_element_type=jnp.float32,
            )
            * scale
        )
        limited = jnp.where(allowed, scores, masked_score)
        maxima = jnp.max(limited, axis=-1, keepdims=True)
        weights = jnp.exp(limited - maxima)
        totals = jnp.sum(weights, axis=-1, keepdims=True)
        result = jnp.dot(
            weights.astype(jnp.bfloat16), read_v(lanes), preferred_element_type=jnp.float32
        )
        o_ref[:, lanes] = (result / totals).astype(o_ref.dtype)
        lse_ref[:, head : head + 1] = maxima + jnp.log(totals)


def spatial_attention(query_flat, key_value_flat, mask, scale, out_dtype=jnp.float32, second=None):
    frames, query_count, model_width = query_flat.shape
    key_count = key_value_flat.shape[2]
    head_count = model_width // DH
    width = group_width(model_width)
    groups = model_width // width
    return pl.pallas_call(
        functools.partial(spatial_kernel, scale=scale),
        grid=(frames, groups),
        in_specs=[
            pl.BlockSpec((None, query_count, width), lambda f, g: (f, 0, g)),
            pl.BlockSpec((None, None, key_count, width), lambda f, g: (0, f, 0, g)),
            pl.BlockSpec((None, None, key_count, width), lambda f, g: (1, f, 0, g)),
        ]
        + [
            pl.BlockSpec((None, None, key_count, width), lambda f, g: (0, f, 0, g)),
            pl.BlockSpec((None, None, key_count, width), lambda f, g: (1, f, 0, g)),
        ]
        * (second is not None)
        + [
            pl.BlockSpec((query_count, key_count), lambda f, g: (0, 0)),
        ],
        out_specs=[
            pl.BlockSpec((None, query_count, width), lambda f, g: (f, 0, g)),
            pl.BlockSpec((None, None, query_count, width // DH), lambda f, g: (f, g, 0, 0)),
        ],
        out_shape=[
            jax.ShapeDtypeStruct((frames, query_count, model_width), out_dtype),
            jax.ShapeDtypeStruct((frames, groups, query_count, width // DH), jnp.float32),
        ],
        cost_estimate=pl.CostEstimate(
            flops=4 * frames * query_count * key_count * model_width,
            transcendentals=frames * head_count * query_count * key_count,
            bytes_accessed=2 * model_width * frames * (query_count + 2 * key_count)
            + 4 * frames * query_count * model_width,
        ),
    )(query_flat, key_value_flat, key_value_flat, *([second, second] if second is not None else []), mask)


def combine_kernel(*refs):
    *parts, temporal_ref, mixed_ref = refs
    outs, lses = parts[0::2], parts[1::2]
    for head in range(mixed_ref.shape[-1] // DH):
        lanes = slice(head * DH, (head + 1) * DH)
        logs = [lse[:, head : head + 1] for lse in lses]
        top = functools.reduce(jnp.maximum, logs)
        weights = [jnp.exp(log - top) for log in logs]
        total = functools.reduce(jnp.add, weights)
        value = functools.reduce(
            jnp.add,
            [w * o[:, lanes].astype(jnp.float32) for w, o in zip(weights, outs)],
        )
        mixed_ref[:, lanes] = (value / total + temporal_ref[:, lanes].astype(jnp.float32)).astype(
            mixed_ref.dtype
        )


def combine_partials(partials, temporal):
    frames, query_count, model_width = temporal.shape
    width = group_width(model_width)
    groups = model_width // width
    big = pl.BlockSpec((None, query_count, width), lambda f, g: (f, 0, g))
    small = pl.BlockSpec((None, None, query_count, width // DH), lambda f, g: (f, g, 0, 0))
    operands = []
    for out, lse in partials:
        operands += [out, lse]
    return pl.pallas_call(
        combine_kernel,
        grid=(frames, groups),
        in_specs=[big, small] * len(partials) + [big],
        out_specs=big,
        out_shape=jax.ShapeDtypeStruct((frames, query_count, model_width), jnp.bfloat16),
    )(*operands, temporal)


def temporal_attention(own_q, all_k, all_v, valid, own_ids, all_ids, scale):
    q32 = own_q.astype(jnp.float32)
    k32 = all_k.astype(jnp.float32)
    scores = jnp.sum(q32[:, None] * k32[None], axis=-1) * scale
    same = own_ids[:, None] == all_ids[None, :]
    allowed = (valid[None, :, :] > 0) | same[:, :, None]
    limited = jnp.where(allowed[..., None], scores, masked_score)
    maxima = jnp.max(limited, axis=1, keepdims=True)
    weights = jnp.exp(limited - maxima)
    totals = jnp.sum(weights, axis=1)
    rounded = lax.reduce_precision(weights, exponent_bits=8, mantissa_bits=7)
    result = jnp.sum(rounded[..., None] * all_v.astype(jnp.float32)[None], axis=1)
    result = lax.reduce_precision(result / totals[..., None], exponent_bits=8, mantissa_bits=7)
    return result.astype(jnp.bfloat16)


def line_gather(block, axis):
    count = lax.axis_size(axis)
    index = lax.axis_index(axis)
    left, right = {}, {}
    from_left = from_right = block
    for step in range(1, count):
        from_left = lax.ppermute(from_left, axis, [(s, s + 1) for s in range(step - 1, count - 1)])
        from_right = lax.ppermute(
            from_right, axis, [(s, s - 1) for s in range(1, count - step + 1)]
        )
        left[step], right[step] = from_left, from_right
    relative = [block]
    for d in range(1, count):
        relative.append(jnp.where(index + d < count, right[d], left[count - d]))
    return relative


def window_mask(query_cols, key_cols, column_map, total_cols, lat_rows):
    block_count = total_cols // BLK
    slots = (key_cols[None, :] // BLK - query_cols[:, None] // BLK + REACH) % block_count
    picks = slots[:, :, None] == jnp.arange(WIN, dtype=jnp.int32)[None, None, :]
    return jnp.any(picks & (column_map[:, None, :] > 0), axis=-1)


def expand_mask(active, lat_rows):
    query_cols, key_cols = active.shape
    return jnp.broadcast_to(
        active[None, :, None, :].astype(jnp.float32), (lat_rows, query_cols, lat_rows, key_cols)
    ).reshape(lat_rows * query_cols, lat_rows * key_cols)


def flat_keys(blocks):
    joined = jnp.concatenate(blocks, axis=3)
    two, frames, lat_rows, cols, model_width = joined.shape
    return joined.reshape(two, frames, lat_rows * cols, model_width)


def spatial_line_of_four(own_q, key_value, window_map, scale):
    frames, lat_rows, columns, model_width = own_q.shape
    count = 4
    total_cols = count * columns
    index = lax.axis_index("lon")
    is_middle = (index >= 1) & (index <= count - 2)
    column_ids = jnp.arange(columns, dtype=jnp.int32)
    own_map = jnp.repeat(window_map, BLK, axis=0)
    own_cols = index * columns + column_ids
    query_flat = own_q.reshape(frames, lat_rows * columns, model_width)

    from_left = lax.ppermute(key_value, "lon", [(0, 1), (1, 2), (2, 3)])
    from_right = lax.ppermute(key_value, "lon", [(3, 2), (2, 1), (1, 0)])
    guest_map = lax.ppermute(window_map, "lon", [(0, 1), (3, 2)])

    near_cols = ((index - 1) * columns + jnp.arange(3 * columns, dtype=jnp.int32)) % total_cols
    near_valid = jnp.stack([index >= 1, index >= 0, index <= count - 2])
    near_active = window_mask(own_cols, near_cols, own_map, total_cols, lat_rows) & jnp.repeat(
        near_valid, columns
    )[None, :]
    near_part = spatial_attention(
        query_flat,
        flat_keys([from_left, key_value, from_right]),
        expand_mask(near_active, lat_rows),
        scale,
    )

    toward_left = lax.ppermute(from_right, "lon", [(2, 1), (1, 0)])
    toward_right = lax.ppermute(from_left, "lon", [(1, 2), (2, 3)])
    held_q, _ = lax.optimization_barrier((own_q, from_left))
    guest_q = lax.ppermute(held_q, "lon", [(0, 1), (3, 2)])
    near_part, toward_left, toward_right, guest_q = lax.optimization_barrier(
        (near_part, toward_left, toward_right, guest_q)
    )
    two_away = jnp.where(index <= 1, toward_left, toward_right)

    guest_device = jnp.where(index == 1, 0, count - 1)
    far_block = (index + 2) % count
    far_cols = far_block * columns + column_ids
    guest_active = window_mask(
        guest_device * columns + column_ids,
        far_cols,
        jnp.repeat(guest_map, BLK, axis=0),
        total_cols,
        lat_rows,
    ) & is_middle
    far_keys = flat_keys([two_away])
    guest_out, guest_lse = spatial_attention(
        guest_q.reshape(frames, lat_rows * columns, model_width),
        flat_keys([toward_left]),
        expand_mask(guest_active, lat_rows),
        scale,
        jnp.bfloat16,
        flat_keys([toward_right]),
    )
    lse_shape = guest_lse.shape
    returned, returned_lse = lax.ppermute(
        (guest_out, jnp.swapaxes(guest_lse, 2, 3)),
        "lon",
        [(1, 0), (2, 3)],
    )
    returned_lse = jnp.where(is_middle, masked_score, jnp.swapaxes(returned_lse, 2, 3))
    assert returned_lse.shape == lse_shape

    far_active = window_mask(own_cols, far_cols, own_map, total_cols, lat_rows)
    far_part = spatial_attention(query_flat, far_keys, expand_mask(far_active, lat_rows), scale)
    return [near_part, far_part, (returned, returned_lse)]


def local(queries, keys, values, window_map, frame_valid):
    own_q = queries[0]
    own_k = keys[0]
    own_v = values[0]
    frames, lat_rows, columns, model_width = own_q.shape
    head_count = model_width // DH
    scale = DH ** (-0.5)
    reach_cols = REACH * BLK
    lon_count = lax.axis_size("lon")
    total_cols = lon_count * columns
    ext_count = columns + 2 * reach_cols
    key_value = jnp.stack([own_k, own_v])
    column_ids = jnp.arange(columns, dtype=jnp.int32)
    per_column_map = jnp.repeat(window_map, BLK, axis=0)
    full_ring = ext_count >= total_cols and WIN * BLK <= total_cols
    if full_ring and lon_count == 4:
        partials = spatial_line_of_four(own_q, key_value, window_map, scale)
    else:
        if full_ring:
            extended = jnp.concatenate(line_gather(key_value, "lon"), axis=3)
            key_cols = total_cols
            block_count = total_cols // BLK
            first_col = lax.axis_index("lon") * columns
            query_blocks = (first_col + column_ids) // BLK
            key_blocks = ((first_col + jnp.arange(total_cols, dtype=jnp.int32)) % total_cols) // BLK
            slots = (key_blocks[None, :] - query_blocks[:, None] + REACH) % block_count
        else:
            reach_devices = -(-reach_cols // columns)
            left_parts, right_parts = [], []
            for step_by in range(1, reach_devices + 1):
                need = min(columns, reach_cols - (step_by - 1) * columns)
                left_parts.insert(
                    0, shifted(key_value[:, :, :, columns - need :, :], "lon", step_by)
                )
                right_parts.append(shifted(key_value[:, :, :, :need, :], "lon", -step_by))
            extended = jnp.concatenate(left_parts + [key_value] + right_parts, axis=3)
            key_cols = ext_count
            ext_ids = jnp.arange(ext_count, dtype=jnp.int32)
            slots = ext_ids[None, :] // BLK - column_ids[:, None] // BLK
        picks = slots[:, :, None] == jnp.arange(WIN, dtype=jnp.int32)[None, None, :]
        active = jnp.any(picks & (per_column_map[:, None, :] > 0), axis=-1)
        query_flat = own_q.reshape(frames, lat_rows * columns, model_width)
        key_value_flat = extended.reshape(2, frames, lat_rows * key_cols, model_width)
        partials = [
            spatial_attention(query_flat, key_value_flat, expand_mask(active, lat_rows), scale)
        ]

    token_count = lat_rows * columns
    tm_count = lax.axis_size("tm")
    tm_index = lax.axis_index("tm")
    key_value_rows = key_value.reshape(2, frames, token_count, head_count, DH)
    pieces = [key_value_rows]
    for step_by in range(1, tm_count):
        pieces.append(shifted(key_value_rows, "tm", step_by))
    gathered = jnp.concatenate(pieces, axis=1)
    piece_ids = jnp.arange(tm_count * frames, dtype=jnp.int32)
    frame_ids = ((tm_index - piece_ids // frames) % tm_count) * frames + piece_ids % frames
    valid_tokens = jnp.take(jnp.tile(frame_valid, (1, lat_rows)), frame_ids, axis=0)
    temporal = temporal_attention(
        own_q.reshape(frames, token_count, head_count, DH),
        gathered[0],
        gathered[1],
        valid_tokens,
        frame_ids[:frames],
        frame_ids,
        scale,
    )
    temporal = temporal.reshape(frames, token_count, model_width)
    mixed = combine_partials(partials, temporal).reshape(frames, lat_rows, columns, model_width)
    half_width = model_width // 2
    branch_index = lax.axis_index("branch")
    own_half = lax.dynamic_slice_in_dim(mixed, branch_index * half_width, half_width, 3)
    other_half = lax.dynamic_slice_in_dim(mixed, (1 - branch_index) * half_width, half_width, 3)
    partner = from_partner(other_half, "branch", 0)
    is_conditional = branch_index == 0
    conditional = jnp.where(is_conditional, own_half, partner).astype(jnp.float32)
    unconditional = jnp.where(is_conditional, partner, own_half).astype(jnp.float32)
    return (unconditional + guidance_weight * (conditional - unconditional)).astype(jnp.bfloat16)


def solution(mesh):
    in_specs = (
        P(("groups", "branch"), "tm", None, "lon", None),
        P(("groups", "branch"), "tm", None, "lon", None),
        P(("groups", "branch"), "tm", None, "lon", None),
        P(("groups", "lon"), None),
        P("groups", "lon"),
    )
    out_specs = P(("groups", "tm"), None, "lon", "branch")
    return jax.shard_map(local, mesh=mesh, in_specs=in_specs, out_specs=out_specs, check_vma=False)
```

```python
import functools

import jax
import jax.numpy as jnp
from jax import lax
from jax.experimental import pallas as pl
from jax.sharding import PartitionSpec as P

DH = 128
BLK = 2
REACH = 7
WIN = 15


guidance_weight = 5.0
masked_score = -1e30


def shifted(value, axis, by):
    count = lax.axis_size(axis)
    return lax.ppermute(value, axis, [(i, (i + by) % count) for i in range(count)])


def from_partner(value, axis, bit):
    return lax.ppermute(value, axis, [(i, i ^ 1 << bit) for i in range(lax.axis_size(axis))])


def group_width(model_width):
    for width in (512, 384, 256):
        if model_width % width == 0:
            return width
    return DH


def spatial_kernel(q_ref, k_ref, v_ref, m_ref, o_ref, lse_ref, *, scale):
    allowed = m_ref[...] > 0
    for head in range(q_ref.shape[-1] // DH):
        lanes = slice(head * DH, (head + 1) * DH)
        scores = (
            lax.dot_general(
                q_ref[:, lanes],
                k_ref[:, lanes],
                (((1,), (1,)), ((), ())),
                preferred_element_type=jnp.float32,
            )
            * scale
        )
        limited = jnp.where(allowed, scores, masked_score)
        maxima = jnp.max(limited, axis=-1, keepdims=True)
        weights = jnp.exp(limited - maxima)
        totals = jnp.sum(weights, axis=-1, keepdims=True)
        result = jnp.dot(
            weights.astype(jnp.bfloat16), v_ref[:, lanes], preferred_element_type=jnp.float32
        )
        o_ref[:, lanes] = (result / totals).astype(o_ref.dtype)
        lse_ref[:, head : head + 1] = maxima + jnp.log(totals)


def spatial_attention(query_flat, key_value_flat, mask, scale, out_dtype=jnp.float32):
    frames, query_count, model_width = query_flat.shape
    key_count = key_value_flat.shape[2]
    head_count = model_width // DH
    width = group_width(model_width)
    groups = model_width // width
    return pl.pallas_call(
        functools.partial(spatial_kernel, scale=scale),
        grid=(frames, groups),
        in_specs=[
            pl.BlockSpec((None, query_count, width), lambda f, g: (f, 0, g)),
            pl.BlockSpec((None, None, key_count, width), lambda f, g: (0, f, 0, g)),
            pl.BlockSpec((None, None, key_count, width), lambda f, g: (1, f, 0, g)),
            pl.BlockSpec((query_count, key_count), lambda f, g: (0, 0)),
        ],
        out_specs=[
            pl.BlockSpec((None, query_count, width), lambda f, g: (f, 0, g)),
            pl.BlockSpec((None, None, query_count, width // DH), lambda f, g: (f, g, 0, 0)),
        ],
        out_shape=[
            jax.ShapeDtypeStruct((frames, query_count, model_width), out_dtype),
            jax.ShapeDtypeStruct((frames, groups, query_count, width // DH), jnp.float32),
        ],
        cost_estimate=pl.CostEstimate(
            flops=4 * frames * query_count * key_count * model_width,
            transcendentals=frames * head_count * query_count * key_count,
            bytes_accessed=2 * model_width * frames * (query_count + 2 * key_count)
            + 4 * frames * query_count * model_width,
        ),
    )(query_flat, key_value_flat, key_value_flat, mask)


def combine_kernel(*refs):
    *parts, temporal_ref, mixed_ref = refs
    outs, lses = parts[0::2], parts[1::2]
    for head in range(mixed_ref.shape[-1] // DH):
        lanes = slice(head * DH, (head + 1) * DH)
        logs = [lse[:, head : head + 1] for lse in lses]
        top = functools.reduce(jnp.maximum, logs)
        weights = [jnp.exp(log - top) for log in logs]
        total = functools.reduce(jnp.add, weights)
        value = functools.reduce(
            jnp.add,
            [w * o[:, lanes].astype(jnp.float32) for w, o in zip(weights, outs)],
        )
        mixed_ref[:, lanes] = (value / total + temporal_ref[:, lanes].astype(jnp.float32)).astype(
            mixed_ref.dtype
        )


def combine_partials(partials, temporal):
    frames, query_count, model_width = temporal.shape
    width = group_width(model_width)
    groups = model_width // width
    big = pl.BlockSpec((None, query_count, width), lambda f, g: (f, 0, g))
    small = pl.BlockSpec((None, None, query_count, width // DH), lambda f, g: (f, g, 0, 0))
    operands = []
    for out, lse in partials:
        operands += [out, lse]
    return pl.pallas_call(
        combine_kernel,
        grid=(frames, groups),
        in_specs=[big, small] * len(partials) + [big],
        out_specs=big,
        out_shape=jax.ShapeDtypeStruct((frames, query_count, model_width), jnp.bfloat16),
    )(*operands, temporal)


def temporal_attention(own_q, all_k, all_v, valid, own_ids, all_ids, scale):
    q32 = own_q.astype(jnp.float32)
    k32 = all_k.astype(jnp.float32)
    scores = jnp.sum(q32[:, None] * k32[None], axis=-1) * scale
    same = own_ids[:, None] == all_ids[None, :]
    allowed = (valid[None, :, :] > 0) | same[:, :, None]
    limited = jnp.where(allowed[..., None], scores, masked_score)
    maxima = jnp.max(limited, axis=1, keepdims=True)
    weights = jnp.exp(limited - maxima)
    totals = jnp.sum(weights, axis=1)
    rounded = lax.reduce_precision(weights, exponent_bits=8, mantissa_bits=7)
    result = jnp.sum(rounded[..., None] * all_v.astype(jnp.float32)[None], axis=1)
    result = lax.reduce_precision(result / totals[..., None], exponent_bits=8, mantissa_bits=7)
    return result.astype(jnp.bfloat16)


def line_gather(block, axis):
    count = lax.axis_size(axis)
    index = lax.axis_index(axis)
    left, right = {}, {}
    from_left = from_right = block
    for step in range(1, count):
        from_left = lax.ppermute(from_left, axis, [(s, s + 1) for s in range(step - 1, count - 1)])
        from_right = lax.ppermute(
            from_right, axis, [(s, s - 1) for s in range(1, count - step + 1)]
        )
        left[step], right[step] = from_left, from_right
    relative = [block]
    for d in range(1, count):
        relative.append(jnp.where(index + d < count, right[d], left[count - d]))
    return relative


def window_mask(query_cols, key_cols, column_map, total_cols, lat_rows):
    block_count = total_cols // BLK
    slots = (key_cols[None, :] // BLK - query_cols[:, None] // BLK + REACH) % block_count
    picks = slots[:, :, None] == jnp.arange(WIN, dtype=jnp.int32)[None, None, :]
    return jnp.any(picks & (column_map[:, None, :] > 0), axis=-1)


def expand_mask(active, lat_rows):
    query_cols, key_cols = active.shape
    return jnp.broadcast_to(
        active[None, :, None, :].astype(jnp.float32), (lat_rows, query_cols, lat_rows, key_cols)
    ).reshape(lat_rows * query_cols, lat_rows * key_cols)


def flat_keys(blocks):
    joined = jnp.concatenate(blocks, axis=3)
    two, frames, lat_rows, cols, model_width = joined.shape
    return joined.reshape(two, frames, lat_rows * cols, model_width)


def spatial_line_of_four(own_q, key_value, window_map, scale):
    frames, lat_rows, columns, model_width = own_q.shape
    count = 4
    total_cols = count * columns
    index = lax.axis_index("lon")
    is_middle = (index >= 1) & (index <= count - 2)
    column_ids = jnp.arange(columns, dtype=jnp.int32)
    own_map = jnp.repeat(window_map, BLK, axis=0)
    own_cols = index * columns + column_ids
    query_flat = own_q.reshape(frames, lat_rows * columns, model_width)

    from_left = lax.ppermute(key_value, "lon", [(0, 1), (1, 2), (2, 3)])
    from_right = lax.ppermute(key_value, "lon", [(3, 2), (2, 1), (1, 0)])
    guest_map = lax.ppermute(window_map, "lon", [(0, 1), (3, 2)])

    near_cols = ((index - 1) * columns + jnp.arange(3 * columns, dtype=jnp.int32)) % total_cols
    near_valid = jnp.stack([index >= 1, index >= 0, index <= count - 2])
    near_active = window_mask(own_cols, near_cols, own_map, total_cols, lat_rows) & jnp.repeat(
        near_valid, columns
    )[None, :]
    near_part = spatial_attention(
        query_flat,
        flat_keys([from_left, key_value, from_right]),
        expand_mask(near_active, lat_rows),
        scale,
    )

    two_away = jnp.where(
        index <= 1,
        lax.ppermute(from_right, "lon", [(2, 1), (1, 0)]),
        lax.ppermute(from_left, "lon", [(1, 2), (2, 3)]),
    )
    held_q, _ = lax.optimization_barrier((own_q, from_left))
    guest_q = lax.ppermute(held_q, "lon", [(0, 1), (3, 2)])
    near_part, two_away, guest_q = lax.optimization_barrier((near_part, two_away, guest_q))

    guest_device = jnp.where(index == 1, 0, count - 1)
    far_block = (index + 2) % count
    far_cols = far_block * columns + column_ids
    guest_active = window_mask(
        guest_device * columns + column_ids,
        far_cols,
        jnp.repeat(guest_map, BLK, axis=0),
        total_cols,
        lat_rows,
    ) & is_middle
    far_keys = flat_keys([two_away])
    guest_out, guest_lse = spatial_attention(
        guest_q.reshape(frames, lat_rows * columns, model_width),
        far_keys,
        expand_mask(guest_active, lat_rows),
        scale,
        jnp.bfloat16,
    )
    lse_shape = guest_lse.shape
    returned, returned_lse = lax.ppermute(
        (guest_out, jnp.swapaxes(guest_lse, 2, 3)),
        "lon",
        [(1, 0), (2, 3)],
    )
    returned_lse = jnp.where(is_middle, masked_score, jnp.swapaxes(returned_lse, 2, 3))
    assert returned_lse.shape == lse_shape

    far_active = window_mask(own_cols, far_cols, own_map, total_cols, lat_rows)
    far_part = spatial_attention(query_flat, far_keys, expand_mask(far_active, lat_rows), scale)
    return [near_part, far_part, (returned, returned_lse)], from_left


def local(queries, keys, values, window_map, frame_valid):
    own_q = queries[0]
    own_k = keys[0]
    own_v = values[0]
    frames, lat_rows, columns, model_width = own_q.shape
    head_count = model_width // DH
    scale = DH ** (-0.5)
    reach_cols = REACH * BLK
    lon_count = lax.axis_size("lon")
    total_cols = lon_count * columns
    ext_count = columns + 2 * reach_cols
    key_value = jnp.stack([own_k, own_v])
    column_ids = jnp.arange(columns, dtype=jnp.int32)
    per_column_map = jnp.repeat(window_map, BLK, axis=0)
    full_ring = ext_count >= total_cols and WIN * BLK <= total_cols
    if full_ring and lon_count == 4:
        partials, first_hop = spatial_line_of_four(own_q, key_value, window_map, scale)
    else:
        if full_ring:
            extended = jnp.concatenate(line_gather(key_value, "lon"), axis=3)
            key_cols = total_cols
            block_count = total_cols // BLK
            first_col = lax.axis_index("lon") * columns
            query_blocks = (first_col + column_ids) // BLK
            key_blocks = ((first_col + jnp.arange(total_cols, dtype=jnp.int32)) % total_cols) // BLK
            slots = (key_blocks[None, :] - query_blocks[:, None] + REACH) % block_count
        else:
            reach_devices = -(-reach_cols // columns)
            left_parts, right_parts = [], []
            for step_by in range(1, reach_devices + 1):
                need = min(columns, reach_cols - (step_by - 1) * columns)
                left_parts.insert(
                    0, shifted(key_value[:, :, :, columns - need :, :], "lon", step_by)
                )
                right_parts.append(shifted(key_value[:, :, :, :need, :], "lon", -step_by))
            extended = jnp.concatenate(left_parts + [key_value] + right_parts, axis=3)
            key_cols = ext_count
            ext_ids = jnp.arange(ext_count, dtype=jnp.int32)
            slots = ext_ids[None, :] // BLK - column_ids[:, None] // BLK
        picks = slots[:, :, None] == jnp.arange(WIN, dtype=jnp.int32)[None, None, :]
        active = jnp.any(picks & (per_column_map[:, None, :] > 0), axis=-1)
        query_flat = own_q.reshape(frames, lat_rows * columns, model_width)
        key_value_flat = extended.reshape(2, frames, lat_rows * key_cols, model_width)
        partials = [
            spatial_attention(query_flat, key_value_flat, expand_mask(active, lat_rows), scale)
        ]

    token_count = lat_rows * columns
    tm_count = lax.axis_size("tm")
    tm_index = lax.axis_index("tm")
    key_value_rows = key_value.reshape(2, frames, token_count, head_count, DH)
    if full_ring and lon_count == 4:
        key_value_rows, _ = lax.optimization_barrier((key_value_rows, first_hop))
    pieces = [key_value_rows]
    for step_by in range(1, tm_count):
        pieces.append(shifted(key_value_rows, "tm", step_by))
    gathered = jnp.concatenate(pieces, axis=1)
    piece_ids = jnp.arange(tm_count * frames, dtype=jnp.int32)
    frame_ids = ((tm_index - piece_ids // frames) % tm_count) * frames + piece_ids % frames
    valid_tokens = jnp.take(jnp.tile(frame_valid, (1, lat_rows)), frame_ids, axis=0)
    temporal = temporal_attention(
        own_q.reshape(frames, token_count, head_count, DH),
        gathered[0],
        gathered[1],
        valid_tokens,
        frame_ids[:frames],
        frame_ids,
        scale,
    )
    temporal = temporal.reshape(frames, token_count, model_width)
    mixed = combine_partials(partials, temporal).reshape(frames, lat_rows, columns, model_width)
    half_width = model_width // 2
    branch_index = lax.axis_index("branch")
    own_half = lax.dynamic_slice_in_dim(mixed, branch_index * half_width, half_width, 3)
    other_half = lax.dynamic_slice_in_dim(mixed, (1 - branch_index) * half_width, half_width, 3)
    partner = from_partner(other_half, "branch", 0)
    is_conditional = branch_index == 0
    conditional = jnp.where(is_conditional, own_half, partner).astype(jnp.float32)
    unconditional = jnp.where(is_conditional, partner, own_half).astype(jnp.float32)
    return (unconditional + guidance_weight * (conditional - unconditional)).astype(jnp.bfloat16)


def solution(mesh):
    in_specs = (
        P(("groups", "branch"), "tm", None, "lon", None),
        P(("groups", "branch"), "tm", None, "lon", None),
        P(("groups", "branch"), "tm", None, "lon", None),
        P(("groups", "lon"), None),
        P("groups", "lon"),
    )
    out_specs = P(("groups", "tm"), None, "lon", "branch")
    return jax.shard_map(local, mesh=mesh, in_specs=in_specs, out_specs=out_specs, check_vma=False)
```

```python
import functools

import jax
import jax.numpy as jnp
from jax import lax
from jax.experimental import pallas as pl
from jax.sharding import PartitionSpec as P

DH = 128
BLK = 2
REACH = 7
WIN = 15


guidance_weight = 5.0
masked_score = -1e30


def shifted(value, axis, by):
    count = lax.axis_size(axis)
    return lax.ppermute(value, axis, [(i, (i + by) % count) for i in range(count)])


def from_partner(value, axis, bit):
    return lax.ppermute(value, axis, [(i, i ^ 1 << bit) for i in range(lax.axis_size(axis))])


def group_width(model_width):
    for width in (768, 512, 384, 256):
        if model_width % width == 0:
            return width
    return DH


def spatial_kernel(q_ref, k_ref, v_ref, m_ref, o_ref, lse_ref, *, scale):
    allowed = m_ref[...] > 0
    for head in range(q_ref.shape[-1] // DH):
        lanes = slice(head * DH, (head + 1) * DH)
        scores = (
            lax.dot_general(
                q_ref[:, lanes],
                k_ref[:, lanes],
                (((1,), (1,)), ((), ())),
                preferred_element_type=jnp.float32,
            )
            * scale
        )
        limited = jnp.where(allowed, scores, masked_score)
        maxima = jnp.max(limited, axis=-1, keepdims=True)
        weights = jnp.exp(limited - maxima)
        totals = jnp.sum(weights, axis=-1, keepdims=True)
        result = jnp.dot(
            weights.astype(jnp.bfloat16), v_ref[:, lanes], preferred_element_type=jnp.float32
        )
        o_ref[:, lanes] = (result / totals).astype(o_ref.dtype)
        lse_ref[:, head : head + 1] = maxima + jnp.log(totals)


def spatial_attention(query_flat, key_value_flat, mask, scale, out_dtype=jnp.float32):
    frames, query_count, model_width = query_flat.shape
    key_count = key_value_flat.shape[2]
    head_count = model_width // DH
    width = group_width(model_width)
    groups = model_width // width
    return pl.pallas_call(
        functools.partial(spatial_kernel, scale=scale),
        grid=(frames, groups),
        in_specs=[
            pl.BlockSpec((None, query_count, width), lambda f, g: (f, 0, g)),
            pl.BlockSpec((None, None, key_count, width), lambda f, g: (0, f, 0, g)),
            pl.BlockSpec((None, None, key_count, width), lambda f, g: (1, f, 0, g)),
            pl.BlockSpec((query_count, key_count), lambda f, g: (0, 0)),
        ],
        out_specs=[
            pl.BlockSpec((None, query_count, width), lambda f, g: (f, 0, g)),
            pl.BlockSpec((None, None, query_count, width // DH), lambda f, g: (f, g, 0, 0)),
        ],
        out_shape=[
            jax.ShapeDtypeStruct((frames, query_count, model_width), out_dtype),
            jax.ShapeDtypeStruct((frames, groups, query_count, width // DH), jnp.float32),
        ],
        cost_estimate=pl.CostEstimate(
            flops=4 * frames * query_count * key_count * model_width,
            transcendentals=frames * head_count * query_count * key_count,
            bytes_accessed=2 * model_width * frames * (query_count + 2 * key_count)
            + 4 * frames * query_count * model_width,
        ),
    )(query_flat, key_value_flat, key_value_flat, mask)


def combine_kernel(*refs):
    *parts, temporal_ref, mixed_ref = refs
    outs, lses = parts[0::2], parts[1::2]
    for head in range(mixed_ref.shape[-1] // DH):
        lanes = slice(head * DH, (head + 1) * DH)
        logs = [lse[:, head : head + 1] for lse in lses]
        top = functools.reduce(jnp.maximum, logs)
        weights = [jnp.exp(log - top) for log in logs]
        total = functools.reduce(jnp.add, weights)
        value = functools.reduce(
            jnp.add,
            [w * o[:, lanes].astype(jnp.float32) for w, o in zip(weights, outs)],
        )
        mixed_ref[:, lanes] = (value / total + temporal_ref[:, lanes].astype(jnp.float32)).astype(
            mixed_ref.dtype
        )


def combine_partials(partials, temporal):
    frames, query_count, model_width = temporal.shape
    width = group_width(model_width)
    groups = model_width // width
    big = pl.BlockSpec((None, query_count, width), lambda f, g: (f, 0, g))
    small = pl.BlockSpec((None, None, query_count, width // DH), lambda f, g: (f, g, 0, 0))
    operands = []
    for out, lse in partials:
        operands += [out, lse]
    return pl.pallas_call(
        combine_kernel,
        grid=(frames, groups),
        in_specs=[big, small] * len(partials) + [big],
        out_specs=big,
        out_shape=jax.ShapeDtypeStruct((frames, query_count, model_width), jnp.bfloat16),
    )(*operands, temporal)


def temporal_attention(own_q, all_k, all_v, valid, own_ids, all_ids, scale):
    q32 = own_q.astype(jnp.float32)
    k32 = all_k.astype(jnp.float32)
    scores = jnp.sum(q32[:, None] * k32[None], axis=-1) * scale
    same = own_ids[:, None] == all_ids[None, :]
    allowed = (valid[None, :, :] > 0) | same[:, :, None]
    limited = jnp.where(allowed[..., None], scores, masked_score)
    maxima = jnp.max(limited, axis=1, keepdims=True)
    weights = jnp.exp(limited - maxima)
    totals = jnp.sum(weights, axis=1)
    rounded = lax.reduce_precision(weights, exponent_bits=8, mantissa_bits=7)
    result = jnp.sum(rounded[..., None] * all_v.astype(jnp.float32)[None], axis=1)
    result = lax.reduce_precision(result / totals[..., None], exponent_bits=8, mantissa_bits=7)
    return result.astype(jnp.bfloat16)


def line_gather(block, axis):
    count = lax.axis_size(axis)
    index = lax.axis_index(axis)
    left, right = {}, {}
    from_left = from_right = block
    for step in range(1, count):
        from_left = lax.ppermute(from_left, axis, [(s, s + 1) for s in range(step - 1, count - 1)])
        from_right = lax.ppermute(
            from_right, axis, [(s, s - 1) for s in range(1, count - step + 1)]
        )
        left[step], right[step] = from_left, from_right
    relative = [block]
    for d in range(1, count):
        relative.append(jnp.where(index + d < count, right[d], left[count - d]))
    return relative


def window_mask(query_cols, key_cols, column_map, total_cols, lat_rows):
    block_count = total_cols // BLK
    slots = (key_cols[None, :] // BLK - query_cols[:, None] // BLK + REACH) % block_count
    picks = slots[:, :, None] == jnp.arange(WIN, dtype=jnp.int32)[None, None, :]
    return jnp.any(picks & (column_map[:, None, :] > 0), axis=-1)


def expand_mask(active, lat_rows):
    query_cols, key_cols = active.shape
    return jnp.broadcast_to(
        active[None, :, None, :].astype(jnp.float32), (lat_rows, query_cols, lat_rows, key_cols)
    ).reshape(lat_rows * query_cols, lat_rows * key_cols)


def flat_keys(blocks):
    joined = jnp.concatenate(blocks, axis=3)
    two, frames, lat_rows, cols, model_width = joined.shape
    return joined.reshape(two, frames, lat_rows * cols, model_width)


def spatial_line_of_four(own_q, key_value, window_map, scale):
    frames, lat_rows, columns, model_width = own_q.shape
    count = 4
    total_cols = count * columns
    index = lax.axis_index("lon")
    is_middle = (index >= 1) & (index <= count - 2)
    column_ids = jnp.arange(columns, dtype=jnp.int32)
    own_map = jnp.repeat(window_map, BLK, axis=0)
    own_cols = index * columns + column_ids
    query_flat = own_q.reshape(frames, lat_rows * columns, model_width)

    from_left = lax.ppermute(key_value, "lon", [(0, 1), (1, 2), (2, 3)])
    from_right = lax.ppermute(key_value, "lon", [(3, 2), (2, 1), (1, 0)])
    guest_map = lax.ppermute(window_map, "lon", [(0, 1), (3, 2)])

    near_cols = ((index - 1) * columns + jnp.arange(3 * columns, dtype=jnp.int32)) % total_cols
    near_valid = jnp.stack([index >= 1, index >= 0, index <= count - 2])
    near_active = window_mask(own_cols, near_cols, own_map, total_cols, lat_rows) & jnp.repeat(
        near_valid, columns
    )[None, :]
    near_part = spatial_attention(
        query_flat,
        flat_keys([from_left, key_value, from_right]),
        expand_mask(near_active, lat_rows),
        scale,
    )

    two_away = jnp.where(
        index <= 1,
        lax.ppermute(from_right, "lon", [(2, 1), (1, 0)]),
        lax.ppermute(from_left, "lon", [(1, 2), (2, 3)]),
    )
    held_q, _ = lax.optimization_barrier((own_q, from_left))
    guest_q = lax.ppermute(held_q, "lon", [(0, 1), (3, 2)])
    near_part, two_away, guest_q = lax.optimization_barrier((near_part, two_away, guest_q))

    guest_device = jnp.where(index == 1, 0, count - 1)
    far_block = (index + 2) % count
    far_cols = far_block * columns + column_ids
    guest_active = window_mask(
        guest_device * columns + column_ids,
        far_cols,
        jnp.repeat(guest_map, BLK, axis=0),
        total_cols,
        lat_rows,
    ) & is_middle
    far_keys = flat_keys([two_away])
    guest_out, guest_lse = spatial_attention(
        guest_q.reshape(frames, lat_rows * columns, model_width),
        far_keys,
        expand_mask(guest_active, lat_rows),
        scale,
        jnp.bfloat16,
    )
    lse_shape = guest_lse.shape
    returned, returned_lse = lax.ppermute(
        (guest_out, jnp.swapaxes(guest_lse, 2, 3)),
        "lon",
        [(1, 0), (2, 3)],
    )
    returned_lse = jnp.where(is_middle, masked_score, jnp.swapaxes(returned_lse, 2, 3))
    assert returned_lse.shape == lse_shape

    far_active = window_mask(own_cols, far_cols, own_map, total_cols, lat_rows)
    far_part = spatial_attention(query_flat, far_keys, expand_mask(far_active, lat_rows), scale)
    return [near_part, far_part, (returned, returned_lse)]


def local(queries, keys, values, window_map, frame_valid):
    own_q = queries[0]
    own_k = keys[0]
    own_v = values[0]
    frames, lat_rows, columns, model_width = own_q.shape
    head_count = model_width // DH
    scale = DH ** (-0.5)
    reach_cols = REACH * BLK
    lon_count = lax.axis_size("lon")
    total_cols = lon_count * columns
    ext_count = columns + 2 * reach_cols
    key_value = jnp.stack([own_k, own_v])
    column_ids = jnp.arange(columns, dtype=jnp.int32)
    per_column_map = jnp.repeat(window_map, BLK, axis=0)
    full_ring = ext_count >= total_cols and WIN * BLK <= total_cols
    if full_ring and lon_count == 4:
        partials = spatial_line_of_four(own_q, key_value, window_map, scale)
    else:
        if full_ring:
            extended = jnp.concatenate(line_gather(key_value, "lon"), axis=3)
            key_cols = total_cols
            block_count = total_cols // BLK
            first_col = lax.axis_index("lon") * columns
            query_blocks = (first_col + column_ids) // BLK
            key_blocks = ((first_col + jnp.arange(total_cols, dtype=jnp.int32)) % total_cols) // BLK
            slots = (key_blocks[None, :] - query_blocks[:, None] + REACH) % block_count
        else:
            reach_devices = -(-reach_cols // columns)
            left_parts, right_parts = [], []
            for step_by in range(1, reach_devices + 1):
                need = min(columns, reach_cols - (step_by - 1) * columns)
                left_parts.insert(
                    0, shifted(key_value[:, :, :, columns - need :, :], "lon", step_by)
                )
                right_parts.append(shifted(key_value[:, :, :, :need, :], "lon", -step_by))
            extended = jnp.concatenate(left_parts + [key_value] + right_parts, axis=3)
            key_cols = ext_count
            ext_ids = jnp.arange(ext_count, dtype=jnp.int32)
            slots = ext_ids[None, :] // BLK - column_ids[:, None] // BLK
        picks = slots[:, :, None] == jnp.arange(WIN, dtype=jnp.int32)[None, None, :]
        active = jnp.any(picks & (per_column_map[:, None, :] > 0), axis=-1)
        query_flat = own_q.reshape(frames, lat_rows * columns, model_width)
        key_value_flat = extended.reshape(2, frames, lat_rows * key_cols, model_width)
        partials = [
            spatial_attention(query_flat, key_value_flat, expand_mask(active, lat_rows), scale)
        ]

    token_count = lat_rows * columns
    tm_count = lax.axis_size("tm")
    tm_index = lax.axis_index("tm")
    key_value_rows = key_value.reshape(2, frames, token_count, head_count, DH)
    pieces = [key_value_rows]
    for step_by in range(1, tm_count):
        pieces.append(shifted(key_value_rows, "tm", step_by))
    gathered = jnp.concatenate(pieces, axis=1)
    piece_ids = jnp.arange(tm_count * frames, dtype=jnp.int32)
    frame_ids = ((tm_index - piece_ids // frames) % tm_count) * frames + piece_ids % frames
    valid_tokens = jnp.take(jnp.tile(frame_valid, (1, lat_rows)), frame_ids, axis=0)
    temporal = temporal_attention(
        own_q.reshape(frames, token_count, head_count, DH),
        gathered[0],
        gathered[1],
        valid_tokens,
        frame_ids[:frames],
        frame_ids,
        scale,
    )
    temporal = temporal.reshape(frames, token_count, model_width)
    mixed = combine_partials(partials, temporal).reshape(frames, lat_rows, columns, model_width)
    half_width = model_width // 2
    branch_index = lax.axis_index("branch")
    own_half = lax.dynamic_slice_in_dim(mixed, branch_index * half_width, half_width, 3)
    other_half = lax.dynamic_slice_in_dim(mixed, (1 - branch_index) * half_width, half_width, 3)
    partner = from_partner(other_half, "branch", 0)
    is_conditional = branch_index == 0
    conditional = jnp.where(is_conditional, own_half, partner).astype(jnp.float32)
    unconditional = jnp.where(is_conditional, partner, own_half).astype(jnp.float32)
    return (unconditional + guidance_weight * (conditional - unconditional)).astype(jnp.bfloat16)


def solution(mesh):
    in_specs = (
        P(("groups", "branch"), "tm", None, "lon", None),
        P(("groups", "branch"), "tm", None, "lon", None),
        P(("groups", "branch"), "tm", None, "lon", None),
        P(("groups", "lon"), None),
        P("groups", "lon"),
    )
    out_specs = P(("groups", "tm"), None, "lon", "branch")
    return jax.shard_map(local, mesh=mesh, in_specs=in_specs, out_specs=out_specs, check_vma=False)
```

```python
import functools

import jax
import jax.numpy as jnp
from jax import lax
from jax.experimental import pallas as pl
from jax.sharding import PartitionSpec as P

DH = 128
BLK = 2
REACH = 7
WIN = 15


guidance_weight = 5.0
masked_score = -1e30


def shifted(value, axis, by):
    count = lax.axis_size(axis)
    return lax.ppermute(value, axis, [(i, (i + by) % count) for i in range(count)])


def from_partner(value, axis, bit):
    return lax.ppermute(value, axis, [(i, i ^ 1 << bit) for i in range(lax.axis_size(axis))])


def group_width(model_width):
    for width in (1536, 768, 512, 384, 256):
        if model_width % width == 0:
            return width
    return DH


def spatial_kernel(q_ref, k_ref, v_ref, m_ref, o_ref, lse_ref, *, scale):
    allowed = m_ref[...] > 0
    for head in range(q_ref.shape[-1] // DH):
        lanes = slice(head * DH, (head + 1) * DH)
        scores = (
            lax.dot_general(
                q_ref[:, lanes],
                k_ref[:, lanes],
                (((1,), (1,)), ((), ())),
                preferred_element_type=jnp.float32,
            )
            * scale
        )
        limited = jnp.where(allowed, scores, masked_score)
        maxima = jnp.max(limited, axis=-1, keepdims=True)
        weights = jnp.exp(limited - maxima)
        totals = jnp.sum(weights, axis=-1, keepdims=True)
        result = jnp.dot(
            weights.astype(jnp.bfloat16), v_ref[:, lanes], preferred_element_type=jnp.float32
        )
        o_ref[:, lanes] = (result / totals).astype(o_ref.dtype)
        lse_ref[:, head : head + 1] = maxima + jnp.log(totals)


def spatial_attention(query_flat, key_value_flat, mask, scale, out_dtype=jnp.float32):
    frames, query_count, model_width = query_flat.shape
    key_count = key_value_flat.shape[2]
    head_count = model_width // DH
    width = group_width(model_width)
    groups = model_width // width
    return pl.pallas_call(
        functools.partial(spatial_kernel, scale=scale),
        grid=(frames, groups),
        in_specs=[
            pl.BlockSpec((None, query_count, width), lambda f, g: (f, 0, g)),
            pl.BlockSpec((None, None, key_count, width), lambda f, g: (0, f, 0, g)),
            pl.BlockSpec((None, None, key_count, width), lambda f, g: (1, f, 0, g)),
            pl.BlockSpec((query_count, key_count), lambda f, g: (0, 0)),
        ],
        out_specs=[
            pl.BlockSpec((None, query_count, width), lambda f, g: (f, 0, g)),
            pl.BlockSpec((None, None, query_count, width // DH), lambda f, g: (f, g, 0, 0)),
        ],
        out_shape=[
            jax.ShapeDtypeStruct((frames, query_count, model_width), out_dtype),
            jax.ShapeDtypeStruct((frames, groups, query_count, width // DH), jnp.float32),
        ],
        cost_estimate=pl.CostEstimate(
            flops=4 * frames * query_count * key_count * model_width,
            transcendentals=frames * head_count * query_count * key_count,
            bytes_accessed=2 * model_width * frames * (query_count + 2 * key_count)
            + 4 * frames * query_count * model_width,
        ),
    )(query_flat, key_value_flat, key_value_flat, mask)


def combine_kernel(*refs):
    *parts, temporal_ref, mixed_ref = refs
    outs, lses = parts[0::2], parts[1::2]
    for head in range(mixed_ref.shape[-1] // DH):
        lanes = slice(head * DH, (head + 1) * DH)
        logs = [lse[:, head : head + 1] for lse in lses]
        top = functools.reduce(jnp.maximum, logs)
        weights = [jnp.exp(log - top) for log in logs]
        total = functools.reduce(jnp.add, weights)
        value = functools.reduce(
            jnp.add,
            [w * o[:, lanes].astype(jnp.float32) for w, o in zip(weights, outs)],
        )
        mixed_ref[:, lanes] = (value / total + temporal_ref[:, lanes].astype(jnp.float32)).astype(
            mixed_ref.dtype
        )


def combine_partials(partials, temporal):
    frames, query_count, model_width = temporal.shape
    width = group_width(model_width)
    groups = model_width // width
    big = pl.BlockSpec((None, query_count, width), lambda f, g: (f, 0, g))
    small = pl.BlockSpec((None, None, query_count, width // DH), lambda f, g: (f, g, 0, 0))
    operands = []
    for out, lse in partials:
        operands += [out, lse]
    return pl.pallas_call(
        combine_kernel,
        grid=(frames, groups),
        in_specs=[big, small] * len(partials) + [big],
        out_specs=big,
        out_shape=jax.ShapeDtypeStruct((frames, query_count, model_width), jnp.bfloat16),
    )(*operands, temporal)


def temporal_attention(own_q, all_k, all_v, valid, own_ids, all_ids, scale):
    q32 = own_q.astype(jnp.float32)
    k32 = all_k.astype(jnp.float32)
    scores = jnp.sum(q32[:, None] * k32[None], axis=-1) * scale
    same = own_ids[:, None] == all_ids[None, :]
    allowed = (valid[None, :, :] > 0) | same[:, :, None]
    limited = jnp.where(allowed[..., None], scores, masked_score)
    maxima = jnp.max(limited, axis=1, keepdims=True)
    weights = jnp.exp(limited - maxima)
    totals = jnp.sum(weights, axis=1)
    rounded = lax.reduce_precision(weights, exponent_bits=8, mantissa_bits=7)
    result = jnp.sum(rounded[..., None] * all_v.astype(jnp.float32)[None], axis=1)
    result = lax.reduce_precision(result / totals[..., None], exponent_bits=8, mantissa_bits=7)
    return result.astype(jnp.bfloat16)


def line_gather(block, axis):
    count = lax.axis_size(axis)
    index = lax.axis_index(axis)
    left, right = {}, {}
    from_left = from_right = block
    for step in range(1, count):
        from_left = lax.ppermute(from_left, axis, [(s, s + 1) for s in range(step - 1, count - 1)])
        from_right = lax.ppermute(
            from_right, axis, [(s, s - 1) for s in range(1, count - step + 1)]
        )
        left[step], right[step] = from_left, from_right
    relative = [block]
    for d in range(1, count):
        relative.append(jnp.where(index + d < count, right[d], left[count - d]))
    return relative


def window_mask(query_cols, key_cols, column_map, total_cols, lat_rows):
    block_count = total_cols // BLK
    slots = (key_cols[None, :] // BLK - query_cols[:, None] // BLK + REACH) % block_count
    picks = slots[:, :, None] == jnp.arange(WIN, dtype=jnp.int32)[None, None, :]
    return jnp.any(picks & (column_map[:, None, :] > 0), axis=-1)


def expand_mask(active, lat_rows):
    query_cols, key_cols = active.shape
    return jnp.broadcast_to(
        active[None, :, None, :].astype(jnp.float32), (lat_rows, query_cols, lat_rows, key_cols)
    ).reshape(lat_rows * query_cols, lat_rows * key_cols)


def flat_keys(blocks):
    joined = jnp.concatenate(blocks, axis=3)
    two, frames, lat_rows, cols, model_width = joined.shape
    return joined.reshape(two, frames, lat_rows * cols, model_width)


def spatial_line_of_four(own_q, key_value, window_map, scale):
    frames, lat_rows, columns, model_width = own_q.shape
    count = 4
    total_cols = count * columns
    index = lax.axis_index("lon")
    is_middle = (index >= 1) & (index <= count - 2)
    column_ids = jnp.arange(columns, dtype=jnp.int32)
    own_map = jnp.repeat(window_map, BLK, axis=0)
    own_cols = index * columns + column_ids
    query_flat = own_q.reshape(frames, lat_rows * columns, model_width)

    from_left = lax.ppermute(key_value, "lon", [(0, 1), (1, 2), (2, 3)])
    from_right = lax.ppermute(key_value, "lon", [(3, 2), (2, 1), (1, 0)])
    guest_map = lax.ppermute(window_map, "lon", [(0, 1), (3, 2)])

    near_cols = ((index - 1) * columns + jnp.arange(3 * columns, dtype=jnp.int32)) % total_cols
    near_valid = jnp.stack([index >= 1, index >= 0, index <= count - 2])
    near_active = window_mask(own_cols, near_cols, own_map, total_cols, lat_rows) & jnp.repeat(
        near_valid, columns
    )[None, :]
    near_part = spatial_attention(
        query_flat,
        flat_keys([from_left, key_value, from_right]),
        expand_mask(near_active, lat_rows),
        scale,
    )

    two_away = jnp.where(
        index <= 1,
        lax.ppermute(from_right, "lon", [(2, 1), (1, 0)]),
        lax.ppermute(from_left, "lon", [(1, 2), (2, 3)]),
    )
    held_q, _ = lax.optimization_barrier((own_q, from_left))
    guest_q = lax.ppermute(held_q, "lon", [(0, 1), (3, 2)])
    near_part, two_away, guest_q = lax.optimization_barrier((near_part, two_away, guest_q))

    guest_device = jnp.where(index == 1, 0, count - 1)
    far_block = (index + 2) % count
    far_cols = far_block * columns + column_ids
    guest_active = window_mask(
        guest_device * columns + column_ids,
        far_cols,
        jnp.repeat(guest_map, BLK, axis=0),
        total_cols,
        lat_rows,
    ) & is_middle
    far_keys = flat_keys([two_away])
    guest_out, guest_lse = spatial_attention(
        guest_q.reshape(frames, lat_rows * columns, model_width),
        far_keys,
        expand_mask(guest_active, lat_rows),
        scale,
        jnp.bfloat16,
    )
    lse_shape = guest_lse.shape
    returned, returned_lse = lax.ppermute(
        (guest_out, jnp.swapaxes(guest_lse, 2, 3)),
        "lon",
        [(1, 0), (2, 3)],
    )
    returned_lse = jnp.where(is_middle, masked_score, jnp.swapaxes(returned_lse, 2, 3))
    assert returned_lse.shape == lse_shape

    far_active = window_mask(own_cols, far_cols, own_map, total_cols, lat_rows)
    far_part = spatial_attention(query_flat, far_keys, expand_mask(far_active, lat_rows), scale)
    return [near_part, far_part, (returned, returned_lse)]


def local(queries, keys, values, window_map, frame_valid):
    own_q = queries[0]
    own_k = keys[0]
    own_v = values[0]
    frames, lat_rows, columns, model_width = own_q.shape
    head_count = model_width // DH
    scale = DH ** (-0.5)
    reach_cols = REACH * BLK
    lon_count = lax.axis_size("lon")
    total_cols = lon_count * columns
    ext_count = columns + 2 * reach_cols
    key_value = jnp.stack([own_k, own_v])
    column_ids = jnp.arange(columns, dtype=jnp.int32)
    per_column_map = jnp.repeat(window_map, BLK, axis=0)
    full_ring = ext_count >= total_cols and WIN * BLK <= total_cols
    if full_ring and lon_count == 4:
        partials = spatial_line_of_four(own_q, key_value, window_map, scale)
    else:
        if full_ring:
            extended = jnp.concatenate(line_gather(key_value, "lon"), axis=3)
            key_cols = total_cols
            block_count = total_cols // BLK
            first_col = lax.axis_index("lon") * columns
            query_blocks = (first_col + column_ids) // BLK
            key_blocks = ((first_col + jnp.arange(total_cols, dtype=jnp.int32)) % total_cols) // BLK
            slots = (key_blocks[None, :] - query_blocks[:, None] + REACH) % block_count
        else:
            reach_devices = -(-reach_cols // columns)
            left_parts, right_parts = [], []
            for step_by in range(1, reach_devices + 1):
                need = min(columns, reach_cols - (step_by - 1) * columns)
                left_parts.insert(
                    0, shifted(key_value[:, :, :, columns - need :, :], "lon", step_by)
                )
                right_parts.append(shifted(key_value[:, :, :, :need, :], "lon", -step_by))
            extended = jnp.concatenate(left_parts + [key_value] + right_parts, axis=3)
            key_cols = ext_count
            ext_ids = jnp.arange(ext_count, dtype=jnp.int32)
            slots = ext_ids[None, :] // BLK - column_ids[:, None] // BLK
        picks = slots[:, :, None] == jnp.arange(WIN, dtype=jnp.int32)[None, None, :]
        active = jnp.any(picks & (per_column_map[:, None, :] > 0), axis=-1)
        query_flat = own_q.reshape(frames, lat_rows * columns, model_width)
        key_value_flat = extended.reshape(2, frames, lat_rows * key_cols, model_width)
        partials = [
            spatial_attention(query_flat, key_value_flat, expand_mask(active, lat_rows), scale)
        ]

    token_count = lat_rows * columns
    tm_count = lax.axis_size("tm")
    tm_index = lax.axis_index("tm")
    key_value_rows = key_value.reshape(2, frames, token_count, head_count, DH)
    pieces = [key_value_rows]
    for step_by in range(1, tm_count):
        pieces.append(shifted(key_value_rows, "tm", step_by))
    gathered = jnp.concatenate(pieces, axis=1)
    piece_ids = jnp.arange(tm_count * frames, dtype=jnp.int32)
    frame_ids = ((tm_index - piece_ids // frames) % tm_count) * frames + piece_ids % frames
    valid_tokens = jnp.take(jnp.tile(frame_valid, (1, lat_rows)), frame_ids, axis=0)
    temporal = temporal_attention(
        own_q.reshape(frames, token_count, head_count, DH),
        gathered[0],
        gathered[1],
        valid_tokens,
        frame_ids[:frames],
        frame_ids,
        scale,
    )
    temporal = temporal.reshape(frames, token_count, model_width)
    mixed = combine_partials(partials, temporal).reshape(frames, lat_rows, columns, model_width)
    half_width = model_width // 2
    branch_index = lax.axis_index("branch")
    own_half = lax.dynamic_slice_in_dim(mixed, branch_index * half_width, half_width, 3)
    other_half = lax.dynamic_slice_in_dim(mixed, (1 - branch_index) * half_width, half_width, 3)
    partner = from_partner(other_half, "branch", 0)
    is_conditional = branch_index == 0
    conditional = jnp.where(is_conditional, own_half, partner).astype(jnp.float32)
    unconditional = jnp.where(is_conditional, partner, own_half).astype(jnp.float32)
    return (unconditional + guidance_weight * (conditional - unconditional)).astype(jnp.bfloat16)


def solution(mesh):
    in_specs = (
        P(("groups", "branch"), "tm", None, "lon", None),
        P(("groups", "branch"), "tm", None, "lon", None),
        P(("groups", "branch"), "tm", None, "lon", None),
        P(("groups", "lon"), None),
        P("groups", "lon"),
    )
    out_specs = P(("groups", "tm"), None, "lon", "branch")
    return jax.shard_map(local, mesh=mesh, in_specs=in_specs, out_specs=out_specs, check_vma=False)
```

```python
import functools

import jax
import jax.numpy as jnp
from jax import lax
from jax.experimental import pallas as pl
from jax.sharding import PartitionSpec as P

DH = 128
BLK = 2
REACH = 7
WIN = 15


guidance_weight = 5.0
masked_score = -1e30


def shifted(value, axis, by):
    count = lax.axis_size(axis)
    return lax.ppermute(value, axis, [(i, (i + by) % count) for i in range(count)])


def from_partner(value, axis, bit):
    return lax.ppermute(value, axis, [(i, i ^ 1 << bit) for i in range(lax.axis_size(axis))])


def group_width(model_width):
    for width in (768, 512, 384, 256):
        if model_width % width == 0:
            return width
    return DH


def spatial_kernel(q_ref, k_ref, v_ref, m_ref, o_ref, lse_ref, *, scale):
    allowed = m_ref[...] > 0
    for head in range(q_ref.shape[-1] // DH):
        lanes = slice(head * DH, (head + 1) * DH)
        scores = (
            lax.dot_general(
                q_ref[:, lanes],
                k_ref[:, lanes],
                (((1,), (1,)), ((), ())),
                preferred_element_type=jnp.float32,
            )
            * scale
        )
        limited = jnp.where(allowed, scores, masked_score)
        maxima = jnp.max(limited, axis=-1, keepdims=True)
        weights = jnp.exp(limited - maxima)
        totals = jnp.sum(weights, axis=-1, keepdims=True)
        result = jnp.dot(
            weights.astype(jnp.bfloat16), v_ref[:, lanes], preferred_element_type=jnp.float32
        )
        o_ref[:, lanes] = (result / totals).astype(o_ref.dtype)
        lse_ref[:, head : head + 1] = maxima + jnp.log(totals)


def spatial_attention(query_flat, key_value_flat, mask, scale, out_dtype=jnp.float32):
    frames, query_count, model_width = query_flat.shape
    key_count = key_value_flat.shape[2]
    head_count = model_width // DH
    width = group_width(model_width)
    groups = model_width // width
    return pl.pallas_call(
        functools.partial(spatial_kernel, scale=scale),
        grid=(frames, groups),
        in_specs=[
            pl.BlockSpec((None, query_count, width), lambda f, g: (f, 0, g)),
            pl.BlockSpec((None, None, key_count, width), lambda f, g: (0, f, 0, g)),
            pl.BlockSpec((None, None, key_count, width), lambda f, g: (1, f, 0, g)),
            pl.BlockSpec((query_count, key_count), lambda f, g: (0, 0)),
        ],
        out_specs=[
            pl.BlockSpec((None, query_count, width), lambda f, g: (f, 0, g)),
            pl.BlockSpec((None, None, query_count, width // DH), lambda f, g: (f, g, 0, 0)),
        ],
        out_shape=[
            jax.ShapeDtypeStruct((frames, query_count, model_width), out_dtype),
            jax.ShapeDtypeStruct((frames, groups, query_count, width // DH), jnp.float32),
        ],
        cost_estimate=pl.CostEstimate(
            flops=4 * frames * query_count * key_count * model_width,
            transcendentals=frames * head_count * query_count * key_count,
            bytes_accessed=2 * model_width * frames * (query_count + 2 * key_count)
            + 4 * frames * query_count * model_width,
        ),
    )(query_flat, key_value_flat, key_value_flat, mask)


def combine_kernel(*refs):
    *parts, temporal_ref, mixed_ref = refs
    outs, lses = parts[0::2], parts[1::2]
    for head in range(mixed_ref.shape[-1] // DH):
        lanes = slice(head * DH, (head + 1) * DH)
        logs = [lse[:, head : head + 1] for lse in lses]
        top = functools.reduce(jnp.maximum, logs)
        weights = [jnp.exp(log - top) for log in logs]
        total = functools.reduce(jnp.add, weights)
        value = functools.reduce(
            jnp.add,
            [w * o[:, lanes].astype(jnp.float32) for w, o in zip(weights, outs)],
        )
        mixed_ref[:, lanes] = (value / total + temporal_ref[:, lanes].astype(jnp.float32)).astype(
            mixed_ref.dtype
        )


def combine_partials(partials, temporal):
    frames, query_count, model_width = temporal.shape
    width = group_width(model_width)
    groups = model_width // width
    big = pl.BlockSpec((None, query_count, width), lambda f, g: (f, 0, g))
    small = pl.BlockSpec((None, None, query_count, width // DH), lambda f, g: (f, g, 0, 0))
    operands = []
    for out, lse in partials:
        operands += [out, lse]
    return pl.pallas_call(
        combine_kernel,
        grid=(frames, groups),
        in_specs=[big, small] * len(partials) + [big],
        out_specs=big,
        out_shape=jax.ShapeDtypeStruct((frames, query_count, model_width), jnp.bfloat16),
    )(*operands, temporal)


def temporal_attention(own_q, all_k, all_v, valid, own_ids, all_ids, scale):
    q32 = own_q.astype(jnp.float32)
    k32 = all_k.astype(jnp.float32)
    scores = jnp.sum(q32[:, None] * k32[None], axis=-1) * scale
    same = own_ids[:, None] == all_ids[None, :]
    allowed = (valid[None, :, :] > 0) | same[:, :, None]
    limited = jnp.where(allowed[..., None], scores, masked_score)
    maxima = jnp.max(limited, axis=1, keepdims=True)
    weights = jnp.exp(limited - maxima)
    totals = jnp.sum(weights, axis=1)
    rounded = lax.reduce_precision(weights, exponent_bits=8, mantissa_bits=7)
    result = jnp.sum(rounded[..., None] * all_v.astype(jnp.float32)[None], axis=1)
    result = lax.reduce_precision(result / totals[..., None], exponent_bits=8, mantissa_bits=7)
    return result.astype(jnp.bfloat16)


def line_gather(block, axis):
    count = lax.axis_size(axis)
    index = lax.axis_index(axis)
    left, right = {}, {}
    from_left = from_right = block
    for step in range(1, count):
        from_left = lax.ppermute(from_left, axis, [(s, s + 1) for s in range(step - 1, count - 1)])
        from_right = lax.ppermute(
            from_right, axis, [(s, s - 1) for s in range(1, count - step + 1)]
        )
        left[step], right[step] = from_left, from_right
    relative = [block]
    for d in range(1, count):
        relative.append(jnp.where(index + d < count, right[d], left[count - d]))
    return relative


def window_mask(query_cols, key_cols, column_map, total_cols, lat_rows):
    block_count = total_cols // BLK
    slots = (key_cols[None, :] // BLK - query_cols[:, None] // BLK + REACH) % block_count
    picks = slots[:, :, None] == jnp.arange(WIN, dtype=jnp.int32)[None, None, :]
    return jnp.any(picks & (column_map[:, None, :] > 0), axis=-1)


def expand_mask(active, lat_rows):
    query_cols, key_cols = active.shape
    return jnp.broadcast_to(
        active[None, :, None, :].astype(jnp.bfloat16), (lat_rows, query_cols, lat_rows, key_cols)
    ).reshape(lat_rows * query_cols, lat_rows * key_cols)


def flat_keys(blocks):
    joined = jnp.concatenate(blocks, axis=3)
    two, frames, lat_rows, cols, model_width = joined.shape
    return joined.reshape(two, frames, lat_rows * cols, model_width)


def spatial_line_of_four(own_q, key_value, window_map, scale):
    frames, lat_rows, columns, model_width = own_q.shape
    count = 4
    total_cols = count * columns
    index = lax.axis_index("lon")
    is_middle = (index >= 1) & (index <= count - 2)
    column_ids = jnp.arange(columns, dtype=jnp.int32)
    own_map = jnp.repeat(window_map, BLK, axis=0)
    own_cols = index * columns + column_ids
    query_flat = own_q.reshape(frames, lat_rows * columns, model_width)

    from_left = lax.ppermute(key_value, "lon", [(0, 1), (1, 2), (2, 3)])
    from_right = lax.ppermute(key_value, "lon", [(3, 2), (2, 1), (1, 0)])
    guest_map = lax.ppermute(window_map, "lon", [(0, 1), (3, 2)])

    near_cols = ((index - 1) * columns + jnp.arange(3 * columns, dtype=jnp.int32)) % total_cols
    near_valid = jnp.stack([index >= 1, index >= 0, index <= count - 2])
    near_active = window_mask(own_cols, near_cols, own_map, total_cols, lat_rows) & jnp.repeat(
        near_valid, columns
    )[None, :]
    near_part = spatial_attention(
        query_flat,
        flat_keys([from_left, key_value, from_right]),
        expand_mask(near_active, lat_rows),
        scale,
    )

    two_away = jnp.where(
        index <= 1,
        lax.ppermute(from_right, "lon", [(2, 1), (1, 0)]),
        lax.ppermute(from_left, "lon", [(1, 2), (2, 3)]),
    )
    held_q, _ = lax.optimization_barrier((own_q, from_left))
    guest_q = lax.ppermute(held_q, "lon", [(0, 1), (3, 2)])
    near_part, two_away, guest_q = lax.optimization_barrier((near_part, two_away, guest_q))

    guest_device = jnp.where(index == 1, 0, count - 1)
    far_block = (index + 2) % count
    far_cols = far_block * columns + column_ids
    guest_active = window_mask(
        guest_device * columns + column_ids,
        far_cols,
        jnp.repeat(guest_map, BLK, axis=0),
        total_cols,
        lat_rows,
    ) & is_middle
    far_keys = flat_keys([two_away])
    guest_out, guest_lse = spatial_attention(
        guest_q.reshape(frames, lat_rows * columns, model_width),
        far_keys,
        expand_mask(guest_active, lat_rows),
        scale,
        jnp.bfloat16,
    )
    lse_shape = guest_lse.shape
    returned, returned_lse = lax.ppermute(
        (guest_out, jnp.swapaxes(guest_lse, 2, 3)),
        "lon",
        [(1, 0), (2, 3)],
    )
    returned_lse = jnp.where(is_middle, masked_score, jnp.swapaxes(returned_lse, 2, 3))
    assert returned_lse.shape == lse_shape

    far_active = window_mask(own_cols, far_cols, own_map, total_cols, lat_rows)
    far_part = spatial_attention(query_flat, far_keys, expand_mask(far_active, lat_rows), scale)
    return [near_part, far_part, (returned, returned_lse)]


def local(queries, keys, values, window_map, frame_valid):
    own_q = queries[0]
    own_k = keys[0]
    own_v = values[0]
    frames, lat_rows, columns, model_width = own_q.shape
    head_count = model_width // DH
    scale = DH ** (-0.5)
    reach_cols = REACH * BLK
    lon_count = lax.axis_size("lon")
    total_cols = lon_count * columns
    ext_count = columns + 2 * reach_cols
    key_value = jnp.stack([own_k, own_v])
    column_ids = jnp.arange(columns, dtype=jnp.int32)
    per_column_map = jnp.repeat(window_map, BLK, axis=0)
    full_ring = ext_count >= total_cols and WIN * BLK <= total_cols
    if full_ring and lon_count == 4:
        partials = spatial_line_of_four(own_q, key_value, window_map, scale)
    else:
        if full_ring:
            extended = jnp.concatenate(line_gather(key_value, "lon"), axis=3)
            key_cols = total_cols
            block_count = total_cols // BLK
            first_col = lax.axis_index("lon") * columns
            query_blocks = (first_col + column_ids) // BLK
            key_blocks = ((first_col + jnp.arange(total_cols, dtype=jnp.int32)) % total_cols) // BLK
            slots = (key_blocks[None, :] - query_blocks[:, None] + REACH) % block_count
        else:
            reach_devices = -(-reach_cols // columns)
            left_parts, right_parts = [], []
            for step_by in range(1, reach_devices + 1):
                need = min(columns, reach_cols - (step_by - 1) * columns)
                left_parts.insert(
                    0, shifted(key_value[:, :, :, columns - need :, :], "lon", step_by)
                )
                right_parts.append(shifted(key_value[:, :, :, :need, :], "lon", -step_by))
            extended = jnp.concatenate(left_parts + [key_value] + right_parts, axis=3)
            key_cols = ext_count
            ext_ids = jnp.arange(ext_count, dtype=jnp.int32)
            slots = ext_ids[None, :] // BLK - column_ids[:, None] // BLK
        picks = slots[:, :, None] == jnp.arange(WIN, dtype=jnp.int32)[None, None, :]
        active = jnp.any(picks & (per_column_map[:, None, :] > 0), axis=-1)
        query_flat = own_q.reshape(frames, lat_rows * columns, model_width)
        key_value_flat = extended.reshape(2, frames, lat_rows * key_cols, model_width)
        partials = [
            spatial_attention(query_flat, key_value_flat, expand_mask(active, lat_rows), scale)
        ]

    token_count = lat_rows * columns
    tm_count = lax.axis_size("tm")
    tm_index = lax.axis_index("tm")
    key_value_rows = key_value.reshape(2, frames, token_count, head_count, DH)
    pieces = [key_value_rows]
    for step_by in range(1, tm_count):
        pieces.append(shifted(key_value_rows, "tm", step_by))
    gathered = jnp.concatenate(pieces, axis=1)
    piece_ids = jnp.arange(tm_count * frames, dtype=jnp.int32)
    frame_ids = ((tm_index - piece_ids // frames) % tm_count) * frames + piece_ids % frames
    valid_tokens = jnp.take(jnp.tile(frame_valid, (1, lat_rows)), frame_ids, axis=0)
    temporal = temporal_attention(
        own_q.reshape(frames, token_count, head_count, DH),
        gathered[0],
        gathered[1],
        valid_tokens,
        frame_ids[:frames],
        frame_ids,
        scale,
    )
    temporal = temporal.reshape(frames, token_count, model_width)
    mixed = combine_partials(partials, temporal).reshape(frames, lat_rows, columns, model_width)
    half_width = model_width // 2
    branch_index = lax.axis_index("branch")
    own_half = lax.dynamic_slice_in_dim(mixed, branch_index * half_width, half_width, 3)
    other_half = lax.dynamic_slice_in_dim(mixed, (1 - branch_index) * half_width, half_width, 3)
    partner = from_partner(other_half, "branch", 0)
    is_conditional = branch_index == 0
    conditional = jnp.where(is_conditional, own_half, partner).astype(jnp.float32)
    unconditional = jnp.where(is_conditional, partner, own_half).astype(jnp.float32)
    return (unconditional + guidance_weight * (conditional - unconditional)).astype(jnp.bfloat16)


def solution(mesh):
    in_specs = (
        P(("groups", "branch"), "tm", None, "lon", None),
        P(("groups", "branch"), "tm", None, "lon", None),
        P(("groups", "branch"), "tm", None, "lon", None),
        P(("groups", "lon"), None),
        P("groups", "lon"),
    )
    out_specs = P(("groups", "tm"), None, "lon", "branch")
    return jax.shard_map(local, mesh=mesh, in_specs=in_specs, out_specs=out_specs, check_vma=False)
```

```python
import functools

import jax
import jax.numpy as jnp
from jax import lax
from jax.experimental import pallas as pl
from jax.sharding import PartitionSpec as P

DH = 128
BLK = 2
REACH = 7
WIN = 15


guidance_weight = 5.0
masked_score = -1e30


def shifted(value, axis, by):
    count = lax.axis_size(axis)
    return lax.ppermute(value, axis, [(i, (i + by) % count) for i in range(count)])


def from_partner(value, axis, bit):
    return lax.ppermute(value, axis, [(i, i ^ 1 << bit) for i in range(lax.axis_size(axis))])


def group_width(model_width):
    for width in (768, 512, 384, 256):
        if model_width % width == 0:
            return width
    return DH


def spatial_kernel(q_ref, k_ref, v_ref, m_ref, o_ref, lse_ref, *, scale):
    allowed = m_ref[...] > 0
    for head in range(q_ref.shape[-1] // DH):
        lanes = slice(head * DH, (head + 1) * DH)
        scores = (
            lax.dot_general(
                q_ref[:, lanes],
                k_ref[:, lanes],
                (((1,), (1,)), ((), ())),
                preferred_element_type=jnp.float32,
            )
            * scale
        )
        limited = jnp.where(allowed, scores, masked_score)
        maxima = jnp.max(limited, axis=-1, keepdims=True)
        weights = jnp.exp(limited - maxima)
        totals = jnp.sum(weights, axis=-1, keepdims=True)
        result = jnp.dot(
            weights.astype(jnp.bfloat16), v_ref[:, lanes], preferred_element_type=jnp.float32
        )
        o_ref[:, lanes] = (result / totals).astype(o_ref.dtype)
        lse_ref[:, head : head + 1] = maxima + jnp.log(totals)


def spatial_attention(query_flat, key_value_flat, mask, scale, out_dtype=jnp.float32):
    frames, query_count, model_width = query_flat.shape
    key_count = key_value_flat.shape[2]
    head_count = model_width // DH
    width = group_width(model_width)
    groups = model_width // width
    return pl.pallas_call(
        functools.partial(spatial_kernel, scale=scale),
        grid=(frames, groups),
        in_specs=[
            pl.BlockSpec((None, query_count, width), lambda f, g: (f, 0, g)),
            pl.BlockSpec((None, None, key_count, width), lambda f, g: (0, f, 0, g)),
            pl.BlockSpec((None, None, key_count, width), lambda f, g: (1, f, 0, g)),
            pl.BlockSpec((query_count, key_count), lambda f, g: (0, 0)),
        ],
        out_specs=[
            pl.BlockSpec((None, query_count, width), lambda f, g: (f, 0, g)),
            pl.BlockSpec((None, None, query_count, width // DH), lambda f, g: (f, g, 0, 0)),
        ],
        out_shape=[
            jax.ShapeDtypeStruct((frames, query_count, model_width), out_dtype),
            jax.ShapeDtypeStruct((frames, groups, query_count, width // DH), jnp.float32),
        ],
        cost_estimate=pl.CostEstimate(
            flops=4 * frames * query_count * key_count * model_width,
            transcendentals=frames * head_count * query_count * key_count,
            bytes_accessed=2 * model_width * frames * (query_count + 2 * key_count)
            + 4 * frames * query_count * model_width,
        ),
    )(query_flat, key_value_flat, key_value_flat, mask)


def combine_kernel(*refs):
    *parts, temporal_ref, mixed_ref = refs
    outs, lses = parts[0::2], parts[1::2]
    for head in range(mixed_ref.shape[-1] // DH):
        lanes = slice(head * DH, (head + 1) * DH)
        logs = [lse[:, head : head + 1] for lse in lses]
        top = functools.reduce(jnp.maximum, logs)
        weights = [jnp.exp(log - top) for log in logs]
        total = functools.reduce(jnp.add, weights)
        value = functools.reduce(
            jnp.add,
            [w * o[:, lanes].astype(jnp.float32) for w, o in zip(weights, outs)],
        )
        mixed_ref[:, lanes] = (value / total + temporal_ref[:, lanes].astype(jnp.float32)).astype(
            mixed_ref.dtype
        )


def merge_kernel(*refs):
    *parts, out_ref, lse_ref = refs
    outs, lses = parts[0::2], parts[1::2]
    for head in range(out_ref.shape[-1] // DH):
        lanes = slice(head * DH, (head + 1) * DH)
        logs = [lse[:, head : head + 1] for lse in lses]
        top = functools.reduce(jnp.maximum, logs)
        weights = [jnp.exp(log - top) for log in logs]
        total = functools.reduce(jnp.add, weights)
        value = functools.reduce(jnp.add, [w * o[:, lanes] for w, o in zip(weights, outs)])
        out_ref[:, lanes] = value / total
        lse_ref[:, head : head + 1] = top + jnp.log(total)


def merge_partials(partials):
    out, lse = partials[0]
    frames, query_count, model_width = out.shape
    width = group_width(model_width)
    groups = model_width // width
    big = pl.BlockSpec((None, query_count, width), lambda f, g: (f, 0, g))
    small = pl.BlockSpec((None, None, query_count, width // DH), lambda f, g: (f, g, 0, 0))
    operands = []
    for out, lse in partials:
        operands += [out, lse]
    return pl.pallas_call(
        merge_kernel,
        grid=(frames, groups),
        in_specs=[big, small] * len(partials),
        out_specs=[big, small],
        out_shape=[
            jax.ShapeDtypeStruct(out.shape, jnp.float32),
            jax.ShapeDtypeStruct(lse.shape, jnp.float32),
        ],
    )(*operands)


def combine_partials(partials, temporal):
    frames, query_count, model_width = temporal.shape
    width = group_width(model_width)
    groups = model_width // width
    big = pl.BlockSpec((None, query_count, width), lambda f, g: (f, 0, g))
    small = pl.BlockSpec((None, None, query_count, width // DH), lambda f, g: (f, g, 0, 0))
    operands = []
    for out, lse in partials:
        operands += [out, lse]
    return pl.pallas_call(
        combine_kernel,
        grid=(frames, groups),
        in_specs=[big, small] * len(partials) + [big],
        out_specs=big,
        out_shape=jax.ShapeDtypeStruct((frames, query_count, model_width), jnp.bfloat16),
    )(*operands, temporal)


def temporal_attention(own_q, all_k, all_v, valid, own_ids, all_ids, scale):
    q32 = own_q.astype(jnp.float32)
    k32 = all_k.astype(jnp.float32)
    scores = jnp.sum(q32[:, None] * k32[None], axis=-1) * scale
    same = own_ids[:, None] == all_ids[None, :]
    allowed = (valid[None, :, :] > 0) | same[:, :, None]
    limited = jnp.where(allowed[..., None], scores, masked_score)
    maxima = jnp.max(limited, axis=1, keepdims=True)
    weights = jnp.exp(limited - maxima)
    totals = jnp.sum(weights, axis=1)
    rounded = lax.reduce_precision(weights, exponent_bits=8, mantissa_bits=7)
    result = jnp.sum(rounded[..., None] * all_v.astype(jnp.float32)[None], axis=1)
    result = lax.reduce_precision(result / totals[..., None], exponent_bits=8, mantissa_bits=7)
    return result.astype(jnp.bfloat16)


def line_gather(block, axis):
    count = lax.axis_size(axis)
    index = lax.axis_index(axis)
    left, right = {}, {}
    from_left = from_right = block
    for step in range(1, count):
        from_left = lax.ppermute(from_left, axis, [(s, s + 1) for s in range(step - 1, count - 1)])
        from_right = lax.ppermute(
            from_right, axis, [(s, s - 1) for s in range(1, count - step + 1)]
        )
        left[step], right[step] = from_left, from_right
    relative = [block]
    for d in range(1, count):
        relative.append(jnp.where(index + d < count, right[d], left[count - d]))
    return relative


def window_mask(query_cols, key_cols, column_map, total_cols, lat_rows):
    block_count = total_cols // BLK
    slots = (key_cols[None, :] // BLK - query_cols[:, None] // BLK + REACH) % block_count
    picks = slots[:, :, None] == jnp.arange(WIN, dtype=jnp.int32)[None, None, :]
    return jnp.any(picks & (column_map[:, None, :] > 0), axis=-1)


def expand_mask(active, lat_rows):
    query_cols, key_cols = active.shape
    return jnp.broadcast_to(
        active[None, :, None, :].astype(jnp.float32), (lat_rows, query_cols, lat_rows, key_cols)
    ).reshape(lat_rows * query_cols, lat_rows * key_cols)


def flat_keys(blocks):
    joined = jnp.concatenate(blocks, axis=3)
    two, frames, lat_rows, cols, model_width = joined.shape
    return joined.reshape(two, frames, lat_rows * cols, model_width)


def spatial_line_of_four(own_q, key_value, window_map, scale):
    frames, lat_rows, columns, model_width = own_q.shape
    count = 4
    total_cols = count * columns
    index = lax.axis_index("lon")
    is_middle = (index >= 1) & (index <= count - 2)
    column_ids = jnp.arange(columns, dtype=jnp.int32)
    own_map = jnp.repeat(window_map, BLK, axis=0)
    own_cols = index * columns + column_ids
    query_flat = own_q.reshape(frames, lat_rows * columns, model_width)

    from_left = lax.ppermute(key_value, "lon", [(0, 1), (1, 2), (2, 3)])
    from_right = lax.ppermute(key_value, "lon", [(3, 2), (2, 1), (1, 0)])
    guest_map = lax.ppermute(window_map, "lon", [(0, 1), (3, 2)])

    near_cols = ((index - 1) * columns + jnp.arange(3 * columns, dtype=jnp.int32)) % total_cols
    near_valid = jnp.stack([index >= 1, index >= 0, index <= count - 2])
    near_active = window_mask(own_cols, near_cols, own_map, total_cols, lat_rows) & jnp.repeat(
        near_valid, columns
    )[None, :]
    near_part = spatial_attention(
        query_flat,
        flat_keys([from_left, key_value, from_right]),
        expand_mask(near_active, lat_rows),
        scale,
    )

    two_away = jnp.where(
        index <= 1,
        lax.ppermute(from_right, "lon", [(2, 1), (1, 0)]),
        lax.ppermute(from_left, "lon", [(1, 2), (2, 3)]),
    )
    held_q, _ = lax.optimization_barrier((own_q, from_left))
    guest_q = lax.ppermute(held_q, "lon", [(0, 1), (3, 2)])
    near_part, two_away, guest_q = lax.optimization_barrier((near_part, two_away, guest_q))

    guest_device = jnp.where(index == 1, 0, count - 1)
    far_block = (index + 2) % count
    far_cols = far_block * columns + column_ids
    guest_active = window_mask(
        guest_device * columns + column_ids,
        far_cols,
        jnp.repeat(guest_map, BLK, axis=0),
        total_cols,
        lat_rows,
    ) & is_middle
    far_keys = flat_keys([two_away])
    guest_out, guest_lse = spatial_attention(
        guest_q.reshape(frames, lat_rows * columns, model_width),
        far_keys,
        expand_mask(guest_active, lat_rows),
        scale,
        jnp.bfloat16,
    )
    lse_shape = guest_lse.shape
    returned, returned_lse = lax.ppermute(
        (guest_out, jnp.swapaxes(guest_lse, 2, 3)),
        "lon",
        [(1, 0), (2, 3)],
    )
    returned_lse = jnp.where(is_middle, masked_score, jnp.swapaxes(returned_lse, 2, 3))
    assert returned_lse.shape == lse_shape

    far_active = window_mask(own_cols, far_cols, own_map, total_cols, lat_rows)
    far_part = spatial_attention(query_flat, far_keys, expand_mask(far_active, lat_rows), scale)
    return [merge_partials([near_part, far_part]), (returned, returned_lse)]


def local(queries, keys, values, window_map, frame_valid):
    own_q = queries[0]
    own_k = keys[0]
    own_v = values[0]
    frames, lat_rows, columns, model_width = own_q.shape
    head_count = model_width // DH
    scale = DH ** (-0.5)
    reach_cols = REACH * BLK
    lon_count = lax.axis_size("lon")
    total_cols = lon_count * columns
    ext_count = columns + 2 * reach_cols
    key_value = jnp.stack([own_k, own_v])
    column_ids = jnp.arange(columns, dtype=jnp.int32)
    per_column_map = jnp.repeat(window_map, BLK, axis=0)
    full_ring = ext_count >= total_cols and WIN * BLK <= total_cols
    if full_ring and lon_count == 4:
        partials = spatial_line_of_four(own_q, key_value, window_map, scale)
    else:
        if full_ring:
            extended = jnp.concatenate(line_gather(key_value, "lon"), axis=3)
            key_cols = total_cols
            block_count = total_cols // BLK
            first_col = lax.axis_index("lon") * columns
            query_blocks = (first_col + column_ids) // BLK
            key_blocks = ((first_col + jnp.arange(total_cols, dtype=jnp.int32)) % total_cols) // BLK
            slots = (key_blocks[None, :] - query_blocks[:, None] + REACH) % block_count
        else:
            reach_devices = -(-reach_cols // columns)
            left_parts, right_parts = [], []
            for step_by in range(1, reach_devices + 1):
                need = min(columns, reach_cols - (step_by - 1) * columns)
                left_parts.insert(
                    0, shifted(key_value[:, :, :, columns - need :, :], "lon", step_by)
                )
                right_parts.append(shifted(key_value[:, :, :, :need, :], "lon", -step_by))
            extended = jnp.concatenate(left_parts + [key_value] + right_parts, axis=3)
            key_cols = ext_count
            ext_ids = jnp.arange(ext_count, dtype=jnp.int32)
            slots = ext_ids[None, :] // BLK - column_ids[:, None] // BLK
        picks = slots[:, :, None] == jnp.arange(WIN, dtype=jnp.int32)[None, None, :]
        active = jnp.any(picks & (per_column_map[:, None, :] > 0), axis=-1)
        query_flat = own_q.reshape(frames, lat_rows * columns, model_width)
        key_value_flat = extended.reshape(2, frames, lat_rows * key_cols, model_width)
        partials = [
            spatial_attention(query_flat, key_value_flat, expand_mask(active, lat_rows), scale)
        ]

    token_count = lat_rows * columns
    tm_count = lax.axis_size("tm")
    tm_index = lax.axis_index("tm")
    key_value_rows = key_value.reshape(2, frames, token_count, head_count, DH)
    pieces = [key_value_rows]
    for step_by in range(1, tm_count):
        pieces.append(shifted(key_value_rows, "tm", step_by))
    gathered = jnp.concatenate(pieces, axis=1)
    piece_ids = jnp.arange(tm_count * frames, dtype=jnp.int32)
    frame_ids = ((tm_index - piece_ids // frames) % tm_count) * frames + piece_ids % frames
    valid_tokens = jnp.take(jnp.tile(frame_valid, (1, lat_rows)), frame_ids, axis=0)
    temporal = temporal_attention(
        own_q.reshape(frames, token_count, head_count, DH),
        gathered[0],
        gathered[1],
        valid_tokens,
        frame_ids[:frames],
        frame_ids,
        scale,
    )
    temporal = temporal.reshape(frames, token_count, model_width)
    mixed = combine_partials(partials, temporal).reshape(frames, lat_rows, columns, model_width)
    half_width = model_width // 2
    branch_index = lax.axis_index("branch")
    own_half = lax.dynamic_slice_in_dim(mixed, branch_index * half_width, half_width, 3)
    other_half = lax.dynamic_slice_in_dim(mixed, (1 - branch_index) * half_width, half_width, 3)
    partner = from_partner(other_half, "branch", 0)
    is_conditional = branch_index == 0
    conditional = jnp.where(is_conditional, own_half, partner).astype(jnp.float32)
    unconditional = jnp.where(is_conditional, partner, own_half).astype(jnp.float32)
    return (unconditional + guidance_weight * (conditional - unconditional)).astype(jnp.bfloat16)


def solution(mesh):
    in_specs = (
        P(("groups", "branch"), "tm", None, "lon", None),
        P(("groups", "branch"), "tm", None, "lon", None),
        P(("groups", "branch"), "tm", None, "lon", None),
        P(("groups", "lon"), None),
        P("groups", "lon"),
    )
    out_specs = P(("groups", "tm"), None, "lon", "branch")
    return jax.shard_map(local, mesh=mesh, in_specs=in_specs, out_specs=out_specs, check_vma=False)
```
